32 devices in a mesh: section: 2 (over x), seq: 8 (over z, y), head: 2 (over core).
Axes of the slice: x: 2, y: 2, z: 4, core: 2. Of those that a mesh axis runs over, the one named last changes fastest.
Arguments:
- bwd_input: bfloat16 [2, 1024, 3584], P('section', 'seq', 'head'), may hold values from -6 to 6
- bwd_docs: int32 [2, 1024], P('section', 'seq'), may hold values from 0 to 3, as said below
- bwd_grad: bfloat16 [2, 1024, 3584], P('section', 'seq', 'head'), may hold values from -6 to 6
- proj_weight: bfloat16 [2, 256, 3584], P('section', 'seq', 'head'), may hold values from -0.09375 to 0.09375
- step_weight: float32 [2, 3584], P('section', 'head'), may hold values from -0.75 to 0.75
- step_bias: float32 [2, 56], P('section', 'head'), may hold values from -5 to -2
- rate_log: float32 [2, 56], P('section', 'head'), may hold values from -4 to 0.5
- skip_gain: float32 [2, 56], P('section', 'head'), may hold values from 0.5 to 1.5
Outputs:
- prev_grad: bfloat16 [2, 1024, 3584], P('section', 'seq', 'head')
- grad_proj: float32 [2, 256, 3584], P('section', 'seq', 'head')
- grad_step_weight: float32 [2, 3584], P('section', 'head')
- grad_step_bias: float32 [2, 56], P('section', 'head')
- grad_rate_log: float32 [2, 56], P('section', 'head')
- grad_skip: float32 [2, 56], P('section', 'head')
The draws below stay inside these ranges and needn't reach their ends.
Inputs may be any that keep to these rules, and one draw needn't show every extreme that they name: `bwd_docs`: document ids of each row never fall, start at 0, every id occurs, and one document of each row holds 512 tokens.
All inputs are finite; a program needn't handle non-finite values.
Results may differ from the reference program's by a relative error of at most 0.023.
Values may be sent and summed in bfloat16 or wider, within the bound.
No kernel may reach another device: no remote copies, remote signals or barrier semaphores. Data moves between devices by JAX's collectives and lax.ppermute only.
A program may use at most 64 MiB of HBM per device.

```python
import jax
import jax.numpy as jnp
from jax import lax

HEADS = 56
HEAD_DIM = 64
STATE = 64
TOK_DEV = 128
LEN = 1024
CHANNELS = 3584
SECTIONS = 2
N_SEQ = 8
N_HEAD = 2


def document_ids(key):
    first_key, third_key = jax.random.split(key)
    first_len = jax.random.randint(first_key, (SECTIONS, 1), 1, TOK_DEV // 2 + 1)
    rest_len = LEN - LEN // 2 - first_len
    third_len = jax.random.randint(third_key, (SECTIONS, 1), 1, rest_len)
    second_start = first_len + LEN // 2
    third_start = second_start + third_len
    position = lax.broadcasted_iota(jnp.int32, (SECTIONS, LEN), 1)
    ids = (position >= first_len).astype(jnp.int32) + (position >= second_start).astype(jnp.int32) + (position >= third_start).astype(jnp.int32)
    return ids.astype(jnp.int32)


def draw_bwd_docs(key, part):
    return document_ids(jax.random.fold_in(key, 23))


def levels(rng, dims, cuts, least, largest):
    def one(axis_at, shards_of):
        steps = jax.random.uniform(jax.random.fold_in(jax.random.fold_in(rng, 6), axis_at), (shards_of,), jnp.float32, least / len(cuts), largest / len(cuts))
        return jnp.repeat(jnp.exp(steps), dims[axis_at] // shards_of).reshape((-1,) + (1,) * (len(dims) - axis_at - 1))

    loudness = one(*cuts[0])
    for cut in cuts[1:]:
        loudness = loudness * one(*cut)
    return loudness


def noise(key, extent, spread, reach, cuts=(), held_as=jnp.bfloat16):
    factor_of = levels(key, extent, cuts, -0.22, 0.18) if cuts else 1.0
    drawn = jax.random.normal(key, extent, jnp.float32) * spread * factor_of
    return jnp.minimum(jnp.maximum(drawn, -reach), reach).astype(held_as)


def setup_inputs(seed: int = 0) -> dict:
    key_list = jax.random.split(jax.random.key(seed), 9)
    bwd_input = noise(key_list[0], (SECTIONS, LEN, CHANNELS), 1.0, 6.0, ((0, 2), (1, 8), (2, 2)))
    bwd_docs = draw_bwd_docs(jax.random.fold_in(key_list[8], 71), 0)
    bwd_grad = noise(key_list[2], (SECTIONS, LEN, CHANNELS), 1.0, 6.0, ((0, 2), (1, 8), (2, 2)))
    proj_weight = noise(key_list[3], (SECTIONS, 4 * STATE, CHANNELS), CHANNELS ** -0.5, 0.09375, ((0, 2), (1, 8), (2, 2)))
    step_weight = noise(key_list[4], (SECTIONS, CHANNELS), HEAD_DIM ** -0.5, 0.75, ((0, 2), (1, 2)), jnp.float32)
    step_bias = jnp.clip(-5.0 + 3.0 * jax.random.uniform(key_list[5], (SECTIONS, HEADS), jnp.float32) ** levels(key_list[5], (SECTIONS, HEADS), ((0, 2), (1, 2)), -0.2, 0.2), -5.0, -2.0)
    rate_log = jnp.clip(-4.0 + 4.5 * jax.random.uniform(key_list[6], (SECTIONS, HEADS), jnp.float32) ** levels(key_list[6], (SECTIONS, HEADS), ((0, 2), (1, 2)), -0.2, 0.2), -4.0, 0.5)
    skip_gain = jnp.clip(0.5 + 1.0 * jax.random.uniform(key_list[7], (SECTIONS, HEADS), jnp.float32) ** levels(key_list[7], (SECTIONS, HEADS), ((0, 2), (1, 2)), -0.2, 0.2), 0.5, 1.5)
    return {"bwd_input": bwd_input, "bwd_docs": bwd_docs, "bwd_grad": bwd_grad, "proj_weight": proj_weight, "step_weight": step_weight, "step_bias": step_bias, "rate_log": rate_log, "skip_gain": skip_gain}


EXACT = lax.Precision.HIGHEST

def contract(spec, left, right):
    return jnp.einsum(spec, left.astype(jnp.float32), right.astype(jnp.float32), precision=EXACT)

def local_setup(values, step_weight, step_bias, rate_log):
    tokens = values.shape[0]
    raw_step = jnp.einsum('thp,hp->th', values.astype(jnp.float32), step_weight, precision=EXACT) + step_bias[None, :]
    step_size = jax.nn.softplus(raw_step)
    decay_log = -jnp.exp(rate_log)[None, :] * step_size
    row_ids = lax.broadcasted_iota(jnp.int32, (tokens, tokens), 0)
    col_ids = lax.broadcasted_iota(jnp.int32, (tokens, tokens), 1)
    triangle = (row_ids >= col_ids).astype(jnp.float32)
    cumulative = jnp.dot(triangle, decay_log, precision=EXACT)
    return (step_size, cumulative, row_ids, col_ids)

def span_summary(values, mixer, step_weight, step_bias, rate_log, docs, doc_before):
    step_size, cumulative, row_ids, col_ids = local_setup(values, step_weight, step_bias, rate_log)
    final_log = cumulative[-1]
    tail_mask = (docs == docs[-1]).astype(jnp.float32)[:, None]
    tail_weight = jnp.exp(jnp.where(tail_mask > 0, final_log[None, :] - cumulative, 0.0)) * tail_mask * step_size
    unbroken = (docs[-1] == doc_before).astype(jnp.float32)
    carry_decay = jnp.exp(final_log) * unbroken
    half_width = mixer.shape[1] // 2
    writers = mixer[:, :half_width]
    weighted = (tail_weight[:, :, None] * writers.astype(jnp.float32)[:, None, :]).astype(jnp.bfloat16)
    span_state = contract('thn,thp->hnp', weighted, values)
    return (carry_decay, span_state)

def span_output(values, mixer, step_weight, step_bias, rate_log, skip_gain, docs, doc_before, incoming):
    step_size, cumulative, row_ids, col_ids = local_setup(values, step_weight, step_bias, rate_log)
    half_width = mixer.shape[1] // 2
    writers = mixer[:, :half_width]
    readers = mixer[:, half_width:]
    affinity = jnp.dot(readers, writers.T, preferred_element_type=jnp.float32)
    same_doc = ((docs[:, None] == docs[None, :]) & (row_ids >= col_ids)).astype(jnp.float32)
    heads_first = cumulative.T
    log_gap = heads_first[:, :, None] - heads_first[:, None, :]
    mixing = jnp.exp(jnp.where(same_doc[None] > 0, log_gap, 0.0)) * same_doc[None] * affinity[None] * step_size.T[:, None, :]
    mixing = mixing.astype(jnp.bfloat16)
    local_part = contract('hts,shp->thp', mixing, values)
    unbroken = (docs == doc_before).astype(jnp.float32)
    carry_scale = jnp.exp(cumulative) * unbroken[:, None]
    carried = jnp.einsum('tn,hnp->thp', readers.astype(jnp.float32), incoming, precision=EXACT)
    combined = values.astype(jnp.float32) * (1.0 + skip_gain)[None, :, None] + local_part + carry_scale[:, :, None] * carried
    return combined.astype(jnp.bfloat16)

def carry_states(decays, states):

    def advance(carry, item):
        return (item[0][:, None, None] * carry + item[1], carry)
    _, incoming = lax.scan(advance, jnp.zeros(states.shape[1:], jnp.float32), (decays, states))
    return incoming

def carry_adjoints(decays, adjoints):

    def retreat(carry, item):
        return (item[1] + item[0][:, None, None] * carry, carry)
    _, outgoing = lax.scan(retreat, jnp.zeros(adjoints.shape[1:], jnp.float32), (decays, adjoints), reverse=True)
    return outgoing

def section_run(bwd_x, bwd_seg, bwd_ct, proj_w, step_weight, step_bias, rate_log, skip_gain):
    spans = N_SEQ
    tokens = TOK_DEV
    per_group = HEADS // N_HEAD
    half_width = 2 * STATE
    weight_heads = step_weight.reshape(HEADS, HEAD_DIM)
    projected = jnp.dot(bwd_x, proj_w.T, preferred_element_type=jnp.float32).astype(jnp.bfloat16)
    projected = projected.reshape(spans, tokens, 4 * STATE)
    doc_spans = bwd_seg.reshape(spans, tokens)
    doc_before = jnp.concatenate([jnp.zeros((1,), jnp.int32), doc_spans[:-1, -1].astype(jnp.int32)])
    values = bwd_x.reshape(spans, tokens, HEADS, HEAD_DIM)
    cotangents = bwd_ct.reshape(spans, tokens, HEADS, HEAD_DIM)
    grad_values = []
    grad_mixers = []
    grad_weights = []
    grad_biases = []
    grad_rates = []
    grad_skips = []
    for group in range(N_HEAD):
        heads = slice(group * per_group, (group + 1) * per_group)
        columns = slice(group * half_width, (group + 1) * half_width)
        group_weight = weight_heads[heads]
        group_bias = step_bias[heads]
        group_rate = rate_log[heads]
        group_skip = skip_gain[heads]

        def summarize(item):
            return span_summary(item[0], item[1], group_weight, group_bias, group_rate, item[2], item[3])
        items_bwd = (values[:, :, heads], projected[:, :, columns], doc_spans, doc_before)
        decays_bwd, states_bwd = lax.map(summarize, items_bwd)
        incoming_bwd = carry_states(decays_bwd, states_bwd)

        def pull_output(item):

            def output_piece(values_in, mixer_in, weight_in, bias_in, rate_in, skip_in, state_in):
                return span_output(values_in, mixer_in, weight_in, bias_in, rate_in, skip_in, item[2], item[3], state_in)
            unused, puller = jax.vjp(output_piece, item[0], item[1], group_weight, group_bias, group_rate, group_skip, item[4])
            return puller(item[5])
        out_grads = lax.map(pull_output, items_bwd + (incoming_bwd, cotangents[:, :, heads]))
        adjoints = carry_adjoints(decays_bwd, out_grads[6])
        decay_grads = lax.optimization_barrier(jnp.sum(adjoints * incoming_bwd, axis=(2, 3)))

        def pull_summary(item):

            def summary_piece(values_in, mixer_in, weight_in, bias_in, rate_in):
                return span_summary(values_in, mixer_in, weight_in, bias_in, rate_in, item[2], item[3])
            unused, puller = jax.vjp(summary_piece, item[0], item[1], group_weight, group_bias, group_rate)
            return puller((item[4], item[5]))
        sum_grads = lax.map(pull_summary, items_bwd + (decay_grads, adjoints))
        grad_values.append(out_grads[0].astype(jnp.float32) + sum_grads[0].astype(jnp.float32))
        grad_mixers.append((out_grads[1].astype(jnp.float32) + sum_grads[1].astype(jnp.float32)).astype(jnp.bfloat16))
        grad_weights.append(lax.optimization_barrier(jnp.sum(out_grads[2], axis=0)) + lax.optimization_barrier(jnp.sum(sum_grads[2], axis=0)))
        grad_biases.append(lax.optimization_barrier(jnp.sum(out_grads[3], axis=0)) + lax.optimization_barrier(jnp.sum(sum_grads[3], axis=0)))
        grad_rates.append(lax.optimization_barrier(jnp.sum(out_grads[4], axis=0)) + lax.optimization_barrier(jnp.sum(sum_grads[4], axis=0)))
        grad_skips.append(lax.optimization_barrier(jnp.sum(out_grads[5], axis=0)))
    mixer_grad = jnp.concatenate(grad_mixers, axis=2).reshape(LEN, 4 * STATE)
    back_proj = jnp.dot(mixer_grad, proj_w, preferred_element_type=jnp.float32)
    value_grad = (jnp.concatenate(grad_values, axis=2).reshape(LEN, CHANNELS) + back_proj).astype(jnp.bfloat16)
    proj_grad = lax.dot_general(mixer_grad, bwd_x, (((0,), (0,)), ((), ())), preferred_element_type=jnp.float32)
    return (value_grad, proj_grad, jnp.concatenate(grad_weights, axis=0).reshape(CHANNELS), jnp.concatenate(grad_biases), jnp.concatenate(grad_rates), jnp.concatenate(grad_skips))

def reference(bwd_input, bwd_docs, bwd_grad, proj_weight, step_weight, step_bias, rate_log, skip_gain):
    results = lax.map(lambda item: section_run(*item), (bwd_input, bwd_docs, bwd_grad, proj_weight, step_weight, step_bias, rate_log, skip_gain))
    blank = jnp.zeros((1, LEN, CHANNELS), jnp.bfloat16)
    prev_grad = jnp.concatenate([results[0][1:], blank], axis=0)
    return (prev_grad, results[1], results[2], results[3], results[4], results[5])
```

```python
import jax
import jax.numpy as jnp
from jax import lax
from jax.sharding import PartitionSpec as P

EXACT = lax.Precision.HIGHEST


def shifted(block, axis, distance):
    devices = range(lax.axis_size(axis))
    route = [(i - distance, i) for i in devices if i - distance in devices]
    return lax.ppermute(block, axis, route)


def contract(spec, left, right):
    return jnp.einsum(spec, left, right, preferred_element_type=jnp.float32)


def local_setup(values, step_weight, step_bias, rate_log):
    tokens = values.shape[0]
    raw_step = (
        jnp.einsum("thp,hp->th", values.astype(jnp.float32), step_weight, precision=EXACT)
        + step_bias[None, :]
    )
    step_size = jax.nn.softplus(raw_step)
    decay_log = -jnp.exp(rate_log)[None, :] * step_size
    row_ids = lax.broadcasted_iota(jnp.int32, (tokens, tokens), 0)
    col_ids = lax.broadcasted_iota(jnp.int32, (tokens, tokens), 1)
    triangle = (row_ids >= col_ids).astype(jnp.float32)
    cumulative = jnp.dot(triangle, decay_log, precision=EXACT)
    return (step_size, cumulative, row_ids, col_ids)


def span_summary(values, mixer, step_weight, step_bias, rate_log, docs, doc_before):
    step_size, cumulative, row_ids, col_ids = local_setup(values, step_weight, step_bias, rate_log)
    final_log = cumulative[-1]
    tail_mask = (docs == docs[-1]).astype(jnp.float32)[:, None]
    tail_weight = (
        jnp.exp(jnp.where(tail_mask > 0, final_log[None, :] - cumulative, 0.0))
        * tail_mask
        * step_size
    )
    unbroken = (docs[-1] == doc_before).astype(jnp.float32)
    carry_decay = jnp.exp(final_log) * unbroken
    half_width = mixer.shape[1] // 2
    writers = mixer[:, :half_width]
    weighted = (tail_weight[:, :, None] * writers.astype(jnp.float32)[:, None, :]).astype(
        jnp.bfloat16
    )
    span_state = contract("thn,thp->hnp", weighted, values)
    return (carry_decay, span_state)


def span_output(
    values, mixer, step_weight, step_bias, rate_log, skip_gain, docs, doc_before, incoming
):
    step_size, cumulative, row_ids, col_ids = local_setup(values, step_weight, step_bias, rate_log)
    half_width = mixer.shape[1] // 2
    writers = mixer[:, :half_width]
    readers = mixer[:, half_width:]
    affinity = jnp.dot(readers, writers.T, preferred_element_type=jnp.float32)
    same_doc = ((docs[:, None] == docs[None, :]) & (row_ids >= col_ids)).astype(jnp.float32)
    heads_first = cumulative.T
    log_gap = heads_first[:, :, None] - heads_first[:, None, :]
    mixing = (
        jnp.exp(jnp.where(same_doc[None] > 0, log_gap, 0.0))
        * same_doc[None]
        * affinity[None]
        * step_size.T[:, None, :]
    )
    mixing = mixing.astype(jnp.bfloat16)
    local_part = contract("hts,shp->thp", mixing, values)
    unbroken = (docs == doc_before).astype(jnp.float32)
    carry_scale = jnp.exp(cumulative) * unbroken[:, None]
    carried = jnp.einsum("tn,hnp->thp", readers.astype(jnp.float32), incoming, precision=EXACT)
    combined = (
        values.astype(jnp.float32) * (1.0 + skip_gain)[None, :, None]
        + local_part
        + carry_scale[:, :, None] * carried
    )
    return combined.astype(jnp.bfloat16)


def scan_rounds(decay, state, axis, forward):
    size, mine = (lax.axis_size(axis), lax.axis_index(axis))
    far_decay, far_state = (decay, state)
    near_decay = jnp.ones_like(decay)
    near_state = jnp.zeros_like(state)
    distance = 1
    while distance < size:
        got_decay, got_state = shifted(
            (far_decay, far_state.astype(jnp.bfloat16)), axis, distance if forward else -distance
        )
        got_state = got_state.astype(jnp.float32)
        near_state = near_state + near_decay[:, None] * got_state
        near_decay = near_decay * got_decay
        if distance * 2 < size:
            far_state = far_state + far_decay[:, None] * got_state
            far_decay = far_decay * got_decay
        distance *= 2
    return near_state


def shards(bwd_input, bwd_docs, bwd_grad, proj_weight, step_weight, step_bias, rate_log, skip_gain):
    tokens = bwd_input.shape[1]
    channels_here = bwd_input.shape[2]
    heads_here = step_bias.shape[1]
    head_width = channels_here // heads_here
    bwd_flat = bwd_input[0]
    bwd_values = bwd_flat.reshape(tokens, heads_here, head_width)
    weight_heads = step_weight[0].reshape(heads_here, head_width)
    bias_heads = step_bias[0]
    rate_heads = rate_log[0]
    skip_heads = skip_gain[0]
    docs_bwd = bwd_docs[0]
    doc_before = shifted(docs_bwd[-1:], "seq", 1)[0]
    full_weight = lax.all_gather(proj_weight[0], "seq", axis=0, tiled=True)
    partial_value = jnp.dot(bwd_flat, full_weight.T, preferred_element_type=jnp.float32)
    mixer_bwd = lax.psum_scatter(
        partial_value.astype(jnp.bfloat16), "head", scatter_dimension=1, tiled=True
    )
    cotangent = bwd_grad[0].reshape(tokens, heads_here, head_width)

    def summary_bwd(values_in, mixer_in, weight_in, bias_in, rate_in):
        return span_summary(values_in, mixer_in, weight_in, bias_in, rate_in, docs_bwd, doc_before)

    summary_out, summary_pull = jax.vjp(
        summary_bwd, bwd_values, mixer_bwd, weight_heads, bias_heads, rate_heads
    )
    decay_bwd, state_bwd = summary_out
    state_shape = state_bwd.shape
    state_flat = state_bwd.reshape(heads_here, -1)

    def output_bwd(values_in, mixer_in, weight_in, bias_in, rate_in, skip_in, state_in):
        return span_output(
            values_in,
            mixer_in,
            weight_in,
            bias_in,
            rate_in,
            skip_in,
            docs_bwd,
            doc_before,
            state_in,
        )

    def carried_only(state_in):
        return output_bwd(
            bwd_values, mixer_bwd, weight_heads, bias_heads, rate_heads, skip_heads, state_in
        )

    state_grad = jax.vjp(carried_only, jnp.zeros(state_shape, jnp.float32))[1](cotangent)[0]
    state_grad = state_grad.reshape(heads_here, -1)
    incoming_flat = scan_rounds(decay_bwd, state_flat, "seq", True)
    adjoint_flat = scan_rounds(decay_bwd, state_grad, "seq", False)
    incoming_bwd = incoming_flat.reshape(state_shape)

    unused, output_pull = jax.vjp(
        output_bwd,
        bwd_values,
        mixer_bwd,
        weight_heads,
        bias_heads,
        rate_heads,
        skip_heads,
        incoming_bwd,
    )
    out_grads = output_pull(cotangent)
    decay_grad = jnp.sum(adjoint_flat * incoming_flat, axis=1)
    sum_grads = summary_pull((decay_grad, adjoint_flat.reshape(state_shape)))
    mixer_grad = (out_grads[1].astype(jnp.float32) + sum_grads[1].astype(jnp.float32)).astype(
        jnp.bfloat16
    )
    mixer_full = lax.all_gather(mixer_grad, "head", axis=1, tiled=True)
    back_proj = jnp.dot(mixer_full, full_weight, preferred_element_type=jnp.float32)
    value_grad = (out_grads[0].astype(jnp.float32) + sum_grads[0].astype(jnp.float32)).reshape(
        tokens, channels_here
    ) + back_proj
    value_grad = value_grad.astype(jnp.bfloat16)
    prev_part = shifted(value_grad.reshape(1, tokens, channels_here), "section", -1)
    grad_rows = lax.psum_scatter(
        lax.dot_general(
            mixer_full, bwd_flat, (((0,), (0,)), ((), ())), preferred_element_type=jnp.float32
        ).astype(jnp.bfloat16),
        "seq",
        scatter_dimension=0,
        tiled=True,
    ).astype(jnp.float32)
    totals = lax.psum(
        (
            (out_grads[2] + sum_grads[2]).reshape(channels_here),
            out_grads[3] + sum_grads[3],
            out_grads[4] + sum_grads[4],
            out_grads[5],
        ),
        "seq",
    )
    return (
        prev_part,
        grad_rows[None],
        totals[0][None],
        totals[1][None],
        totals[2][None],
        totals[3][None],
    )


def solution(mesh):
    in_specs = (
        P("section", "seq", "head"),
        P("section", "seq"),
        P("section", "seq", "head"),
        P("section", "seq", "head"),
        P("section", "head"),
        P("section", "head"),
        P("section", "head"),
        P("section", "head"),
    )
    out_specs = (
        P("section", "seq", "head"),
        P("section", "seq", "head"),
        P("section", "head"),
        P("section", "head"),
        P("section", "head"),
        P("section", "head"),
    )
    return jax.shard_map(shards, mesh=mesh, in_specs=in_specs, out_specs=out_specs, check_vma=False)
```

```python
import jax
import jax.numpy as jnp
from jax import lax
from jax.sharding import PartitionSpec as P

EXACT = lax.Precision.HIGHEST


def shifted(block, axis, distance):
    devices = range(lax.axis_size(axis))
    route = [(i - distance, i) for i in devices if i - distance in devices]
    return lax.ppermute(block, axis, route)


def rotated(block, axis, distance):
    size = lax.axis_size(axis)
    route = [(i, (i + distance) % size) for i in range(size)]
    return lax.ppermute(block, axis, route)


def roll_blocks(value, shift, parts, dim):
    doubled = jnp.concatenate([value, value], axis=dim)
    width = value.shape[dim] // parts
    start = ((parts - shift) % parts) * width
    return lax.dynamic_slice_in_dim(doubled, start, value.shape[dim], axis=dim)


def swap_heads(block):
    return lax.ppermute(block, "head", [(0, 1), (1, 0)])


def seq_total(value):
    size = lax.axis_size("seq")
    if size & (size - 1):
        return lax.psum(value, "seq")
    distance = 1
    while distance < size:
        value = value + lax.ppermute(value, "seq", [(i, i ^ distance) for i in range(size)])
        distance *= 2
    return value


def contract(spec, left, right):
    return jnp.einsum(spec, left, right, preferred_element_type=jnp.float32)


def local_setup(values, step_weight, step_bias, rate_log):
    tokens = values.shape[0]
    raw_step = (
        jnp.einsum("thp,hp->th", values.astype(jnp.float32), step_weight, precision=EXACT)
        + step_bias[None, :]
    )
    step_size = jax.nn.softplus(raw_step)
    decay_log = -jnp.exp(rate_log)[None, :] * step_size
    row_ids = lax.broadcasted_iota(jnp.int32, (tokens, tokens), 0)
    col_ids = lax.broadcasted_iota(jnp.int32, (tokens, tokens), 1)
    triangle = (row_ids >= col_ids).astype(jnp.float32)
    cumulative = jnp.dot(triangle, decay_log, precision=EXACT)
    return (step_size, cumulative, row_ids, col_ids)


def span_summary(values, mixer, step_weight, step_bias, rate_log, docs, doc_before):
    step_size, cumulative, row_ids, col_ids = local_setup(values, step_weight, step_bias, rate_log)
    final_log = cumulative[-1]
    tail_mask = (docs == docs[-1]).astype(jnp.float32)[:, None]
    tail_weight = (
        jnp.exp(jnp.where(tail_mask > 0, final_log[None, :] - cumulative, 0.0))
        * tail_mask
        * step_size
    )
    unbroken = (docs[-1] == doc_before).astype(jnp.float32)
    carry_decay = jnp.exp(final_log) * unbroken
    half_width = mixer.shape[1] // 2
    writers = mixer[:, :half_width]
    weighted = (tail_weight[:, :, None] * writers.astype(jnp.float32)[:, None, :]).astype(
        jnp.bfloat16
    )
    span_state = contract("thn,thp->hnp", weighted, values)
    return (carry_decay, span_state)


def span_output(
    values, mixer, step_weight, step_bias, rate_log, skip_gain, docs, doc_before, incoming
):
    step_size, cumulative, row_ids, col_ids = local_setup(values, step_weight, step_bias, rate_log)
    half_width = mixer.shape[1] // 2
    writers = mixer[:, :half_width]
    readers = mixer[:, half_width:]
    affinity = jnp.dot(readers, writers.T, preferred_element_type=jnp.float32)
    same_doc = ((docs[:, None] == docs[None, :]) & (row_ids >= col_ids)).astype(jnp.float32)
    heads_first = cumulative.T
    log_gap = heads_first[:, :, None] - heads_first[:, None, :]
    mixing = (
        jnp.exp(jnp.where(same_doc[None] > 0, log_gap, 0.0))
        * same_doc[None]
        * affinity[None]
        * step_size.T[:, None, :]
    )
    mixing = mixing.astype(jnp.bfloat16)
    local_part = contract("hts,shp->thp", mixing, values)
    unbroken = (docs == doc_before).astype(jnp.float32)
    carry_scale = jnp.exp(cumulative) * unbroken[:, None]
    carried = jnp.einsum("tn,hnp->thp", readers.astype(jnp.float32), incoming, precision=EXACT)
    combined = (
        values.astype(jnp.float32) * (1.0 + skip_gain)[None, :, None]
        + local_part
        + carry_scale[:, :, None] * carried
    )
    return combined.astype(jnp.bfloat16)


def scan_rounds(decay, state, axis, forward):
    size, mine = (lax.axis_size(axis), lax.axis_index(axis))
    far_decay, far_state = (decay, state)
    near_decay = jnp.ones_like(decay)
    near_state = jnp.zeros_like(state)
    distance = 1
    while distance < size:
        got_decay, got_state = shifted(
            (far_decay, far_state.astype(jnp.bfloat16)), axis, distance if forward else -distance
        )
        got_state = got_state.astype(jnp.float32)
        near_state = near_state + near_decay[:, None] * got_state
        near_decay = near_decay * got_decay
        if distance * 2 < size:
            far_state = far_state + far_decay[:, None] * got_state
            far_decay = far_decay * got_decay
        distance *= 2
    return near_state


def shards(bwd_input, bwd_docs, bwd_grad, proj_weight, step_weight, step_bias, rate_log, skip_gain):
    tokens = bwd_input.shape[1]
    channels_here = bwd_input.shape[2]
    heads_here = step_bias.shape[1]
    head_width = channels_here // heads_here
    bwd_flat = bwd_input[0]
    bwd_values = bwd_flat.reshape(tokens, heads_here, head_width)
    weight_heads = step_weight[0].reshape(heads_here, head_width)
    bias_heads = step_bias[0]
    rate_heads = rate_log[0]
    skip_heads = skip_gain[0]
    docs_bwd = bwd_docs[0]
    doc_before = shifted(docs_bwd[-1:], "seq", 1)[0]
    size, mine = (lax.axis_size("seq"), lax.axis_index("seq"))
    group = lax.axis_index("head")
    own_rows = proj_weight[0]
    slot_weight = jnp.concatenate(
        [own_rows] + [rotated(own_rows, "seq", k) for k in range(1, size)], axis=0
    )
    slot_value = jnp.dot(bwd_flat, slot_weight.T, preferred_element_type=jnp.float32)
    slot_value = slot_value.reshape(tokens, size, -1)[:, ::-1].reshape(tokens, -1)
    partial_value = roll_blocks(slot_value, mine + 1, size, 1)
    group_width = partial_value.shape[1] // 2
    mine_part = lax.dynamic_slice_in_dim(partial_value, group * group_width, group_width, axis=1)
    other_part = lax.dynamic_slice_in_dim(
        partial_value, (1 - group) * group_width, group_width, axis=1
    )
    mixer_bwd = (
        mine_part + swap_heads(other_part.astype(jnp.bfloat16)).astype(jnp.float32)
    ).astype(jnp.bfloat16)
    cotangent = bwd_grad[0].reshape(tokens, heads_here, head_width)

    def summary_bwd(values_in, mixer_in, weight_in, bias_in, rate_in):
        return span_summary(values_in, mixer_in, weight_in, bias_in, rate_in, docs_bwd, doc_before)

    summary_out, summary_pull = jax.vjp(
        summary_bwd, bwd_values, mixer_bwd, weight_heads, bias_heads, rate_heads
    )
    decay_bwd, state_bwd = summary_out
    state_shape = state_bwd.shape
    state_flat = state_bwd.reshape(heads_here, -1)

    def output_bwd(values_in, mixer_in, weight_in, bias_in, rate_in, skip_in, state_in):
        return span_output(
            values_in,
            mixer_in,
            weight_in,
            bias_in,
            rate_in,
            skip_in,
            docs_bwd,
            doc_before,
            state_in,
        )

    def carried_only(state_in):
        return output_bwd(
            bwd_values, mixer_bwd, weight_heads, bias_heads, rate_heads, skip_heads, state_in
        )

    state_grad = jax.vjp(carried_only, jnp.zeros(state_shape, jnp.float32))[1](cotangent)[0]
    state_grad = state_grad.reshape(heads_here, -1)
    incoming_flat = scan_rounds(decay_bwd, state_flat, "seq", True)
    adjoint_flat = scan_rounds(decay_bwd, state_grad, "seq", False)
    incoming_bwd = incoming_flat.reshape(state_shape)

    unused, output_pull = jax.vjp(
        output_bwd,
        bwd_values,
        mixer_bwd,
        weight_heads,
        bias_heads,
        rate_heads,
        skip_heads,
        incoming_bwd,
    )
    out_grads = output_pull(cotangent)
    decay_grad = jnp.sum(adjoint_flat * incoming_flat, axis=1)
    sum_grads = summary_pull((decay_grad, adjoint_flat.reshape(state_shape)))
    mixer_grad = (out_grads[1].astype(jnp.float32) + sum_grads[1].astype(jnp.float32)).astype(
        jnp.bfloat16
    )
    other_grad = swap_heads(mixer_grad)
    mixer_full = jnp.where(
        group == 0,
        jnp.concatenate([mixer_grad, other_grad], axis=1),
        jnp.concatenate([other_grad, mixer_grad], axis=1),
    )
    mixer_slots = roll_blocks(mixer_full, size - 1 - mine, size, 1)
    mixer_slots = mixer_slots.reshape(tokens, size, -1)[:, ::-1].reshape(tokens, -1)
    back_proj = jnp.dot(mixer_slots, slot_weight, preferred_element_type=jnp.float32)
    value_grad = (out_grads[0].astype(jnp.float32) + sum_grads[0].astype(jnp.float32)).reshape(
        tokens, channels_here
    ) + back_proj
    value_grad = value_grad.astype(jnp.bfloat16)
    prev_part = shifted(value_grad.reshape(1, tokens, channels_here), "section", -1)
    dest_grad = roll_blocks(mixer_full, size - mine, size, 1)
    row_parts = lax.dot_general(
        dest_grad, bwd_flat, (((0,), (0,)), ((), ())), preferred_element_type=jnp.float32
    ).reshape(size, -1, channels_here)
    grad_rows = row_parts[0]
    for k in range(1, size):
        grad_rows = grad_rows + rotated(row_parts[k].astype(jnp.bfloat16), "seq", k).astype(
            jnp.float32
        )
    small = jnp.concatenate(
        [
            (out_grads[2] + sum_grads[2]).reshape(channels_here),
            out_grads[3] + sum_grads[3],
            out_grads[4] + sum_grads[4],
            out_grads[5],
        ]
    )
    small = seq_total(small)
    totals = (
        small[:channels_here],
        small[channels_here : channels_here + heads_here],
        small[channels_here + heads_here : channels_here + 2 * heads_here],
        small[channels_here + 2 * heads_here :],
    )
    return (
        prev_part,
        grad_rows[None],
        totals[0][None],
        totals[1][None],
        totals[2][None],
        totals[3][None],
    )


def solution(mesh):
    in_specs = (
        P("section", "seq", "head"),
        P("section", "seq"),
        P("section", "seq", "head"),
        P("section", "seq", "head"),
        P("section", "head"),
        P("section", "head"),
        P("section", "head"),
        P("section", "head"),
    )
    out_specs = (
        P("section", "seq", "head"),
        P("section", "seq", "head"),
        P("section", "head"),
        P("section", "head"),
        P("section", "head"),
        P("section", "head"),
    )
    return jax.shard_map(shards, mesh=mesh, in_specs=in_specs, out_specs=out_specs, check_vma=False)
```

```python
import jax
import jax.numpy as jnp
from jax import lax
from jax.sharding import PartitionSpec as P

EXACT = lax.Precision.HIGHEST


def shifted(block, axis, distance):
    devices = range(lax.axis_size(axis))
    route = [(i - distance, i) for i in devices if i - distance in devices]
    return lax.ppermute(block, axis, route)


def rotated(block, axis, distance):
    size = lax.axis_size(axis)
    route = [(i, (i + distance) % size) for i in range(size)]
    return lax.ppermute(block, axis, route)


def roll_blocks(value, shift, parts, dim):
    doubled = jnp.concatenate([value, value], axis=dim)
    width = value.shape[dim] // parts
    start = ((parts - shift) % parts) * width
    return lax.dynamic_slice_in_dim(doubled, start, value.shape[dim], axis=dim)


def swap_heads(block):
    return lax.ppermute(block, "head", [(0, 1), (1, 0)])


def seq_total(value):
    size = lax.axis_size("seq")
    if size & (size - 1):
        return lax.psum(value, "seq")
    distance = 1
    while distance < size:
        value = value + lax.ppermute(value, "seq", [(i, i ^ distance) for i in range(size)])
        distance *= 2
    return value


def contract(spec, left, right):
    return jnp.einsum(spec, left, right, preferred_element_type=jnp.float32)


def local_setup(values, step_weight, step_bias, rate_log):
    tokens = values.shape[0]
    raw_step = (
        jnp.einsum("thp,hp->th", values.astype(jnp.float32), step_weight, precision=EXACT)
        + step_bias[None, :]
    )
    step_size = jax.nn.softplus(raw_step)
    decay_log = -jnp.exp(rate_log)[None, :] * step_size
    row_ids = lax.broadcasted_iota(jnp.int32, (tokens, tokens), 0)
    col_ids = lax.broadcasted_iota(jnp.int32, (tokens, tokens), 1)
    triangle = (row_ids >= col_ids).astype(jnp.float32)
    cumulative = jnp.dot(triangle, decay_log, precision=EXACT)
    return (step_size, cumulative, row_ids, col_ids)


def span_summary(values, mixer, step_weight, step_bias, rate_log, docs, doc_before):
    step_size, cumulative, row_ids, col_ids = local_setup(values, step_weight, step_bias, rate_log)
    final_log = cumulative[-1]
    tail_mask = (docs == docs[-1]).astype(jnp.float32)[:, None]
    tail_weight = (
        jnp.exp(jnp.where(tail_mask > 0, final_log[None, :] - cumulative, 0.0))
        * tail_mask
        * step_size
    )
    unbroken = (docs[-1] == doc_before).astype(jnp.float32)
    carry_decay = jnp.exp(final_log) * unbroken
    half_width = mixer.shape[1] // 2
    writers = mixer[:, :half_width]
    weighted = (tail_weight[:, :, None] * writers.astype(jnp.float32)[:, None, :]).astype(
        jnp.bfloat16
    )
    span_state = contract("thn,thp->hnp", weighted, values)
    return (carry_decay, span_state)


def span_output(
    values, mixer, step_weight, step_bias, rate_log, skip_gain, docs, doc_before, incoming
):
    step_size, cumulative, row_ids, col_ids = local_setup(values, step_weight, step_bias, rate_log)
    half_width = mixer.shape[1] // 2
    writers = mixer[:, :half_width]
    readers = mixer[:, half_width:]
    affinity = jnp.dot(readers, writers.T, preferred_element_type=jnp.float32)
    same_doc = ((docs[:, None] == docs[None, :]) & (row_ids >= col_ids)).astype(jnp.float32)
    heads_first = cumulative.T
    log_gap = heads_first[:, :, None] - heads_first[:, None, :]
    mixing = (
        jnp.exp(jnp.where(same_doc[None] > 0, log_gap, 0.0))
        * same_doc[None]
        * affinity[None]
        * step_size.T[:, None, :]
    )
    mixing = mixing.astype(jnp.bfloat16)
    local_part = contract("hts,shp->thp", mixing, values)
    unbroken = (docs == doc_before).astype(jnp.float32)
    carry_scale = jnp.exp(cumulative) * unbroken[:, None]
    carried = jnp.einsum("tn,hnp->thp", readers.astype(jnp.float32), incoming, precision=EXACT)
    combined = (
        values.astype(jnp.float32) * (1.0 + skip_gain)[None, :, None]
        + local_part
        + carry_scale[:, :, None] * carried
    )
    return combined.astype(jnp.bfloat16)


def scan_rounds(decay, state, axis, forward):
    size, mine = (lax.axis_size(axis), lax.axis_index(axis))
    far_decay, far_state = (decay, state)
    near_decay = jnp.ones_like(decay)
    near_state = jnp.zeros_like(state)
    distance = 1
    while distance < size:
        got_decay, got_state = shifted(
            (far_decay, far_state.astype(jnp.bfloat16)), axis, distance if forward else -distance
        )
        got_state = got_state.astype(jnp.float32)
        near_state = near_state + near_decay[:, None] * got_state
        near_decay = near_decay * got_decay
        if distance * 2 < size:
            far_state = far_state + far_decay[:, None] * got_state
            far_decay = far_decay * got_decay
        distance *= 2
    return near_state


def both_scans(decay, state, state_grad, axis):
    size, mine = (lax.axis_size(axis), lax.axis_index(axis))
    if size & (size - 1):
        return (
            scan_rounds(decay, state, axis, True),
            scan_rounds(decay, state_grad, axis, False),
        )
    width = state.shape[1]
    total_decay = decay
    total_fwd, total_bwd = (state, state_grad)
    before = jnp.zeros_like(state)
    before_decay = jnp.ones_like(decay)
    after = jnp.zeros_like(state_grad)
    after_decay = jnp.ones_like(decay)
    distance = 1
    while distance < size:
        high = lax.convert_element_type(total_decay.astype(jnp.bfloat16), jnp.float32)
        low = total_decay - high
        pad = jnp.zeros((decay.shape[0], 126), jnp.float32)
        payload = jnp.concatenate(
            [total_fwd, total_bwd, high[:, None], low[:, None], pad], axis=1
        ).astype(jnp.bfloat16)
        got = lax.ppermute(payload, axis, [(i, i ^ distance) for i in range(size)])
        got = got.astype(jnp.float32)
        got_fwd = got[:, :width]
        got_bwd = got[:, width : 2 * width]
        got_decay = got[:, 2 * width] + got[:, 2 * width + 1]
        upper = (mine // distance) % 2 == 1
        before = jnp.where(upper, before + before_decay[:, None] * got_fwd, before)
        before_decay = jnp.where(upper, before_decay * got_decay, before_decay)
        after = jnp.where(upper, after, after + after_decay[:, None] * got_bwd)
        after_decay = jnp.where(upper, after_decay, after_decay * got_decay)
        if distance * 2 < size:
            total_fwd = jnp.where(
                upper,
                total_fwd + total_decay[:, None] * got_fwd,
                got_fwd + got_decay[:, None] * total_fwd,
            )
            total_bwd = jnp.where(
                upper,
                got_bwd + got_decay[:, None] * total_bwd,
                total_bwd + total_decay[:, None] * got_bwd,
            )
            total_decay = total_decay * got_decay
        distance *= 2
    return (before, after)


def shards(bwd_input, bwd_docs, bwd_grad, proj_weight, step_weight, step_bias, rate_log, skip_gain):
    tokens = bwd_input.shape[1]
    channels_here = bwd_input.shape[2]
    heads_here = step_bias.shape[1]
    head_width = channels_here // heads_here
    bwd_flat = bwd_input[0]
    bwd_values = bwd_flat.reshape(tokens, heads_here, head_width)
    weight_heads = step_weight[0].reshape(heads_here, head_width)
    bias_heads = step_bias[0]
    rate_heads = rate_log[0]
    skip_heads = skip_gain[0]
    docs_bwd = bwd_docs[0]
    doc_before = shifted(docs_bwd[-1:], "seq", 1)[0]
    size, mine = (lax.axis_size("seq"), lax.axis_index("seq"))
    group = lax.axis_index("head")
    own_rows = proj_weight[0]
    slot_weight = jnp.concatenate(
        [own_rows] + [rotated(own_rows, "seq", k) for k in range(1, size)], axis=0
    )
    slot_value = jnp.dot(bwd_flat, slot_weight.T, preferred_element_type=jnp.float32)
    slot_value = slot_value.reshape(tokens, size, -1)[:, ::-1].reshape(tokens, -1)
    partial_value = roll_blocks(slot_value, mine + 1, size, 1)
    group_width = partial_value.shape[1] // 2
    mine_part = lax.dynamic_slice_in_dim(partial_value, group * group_width, group_width, axis=1)
    other_part = lax.dynamic_slice_in_dim(
        partial_value, (1 - group) * group_width, group_width, axis=1
    )
    mixer_bwd = (
        mine_part + swap_heads(other_part.astype(jnp.bfloat16)).astype(jnp.float32)
    ).astype(jnp.bfloat16)
    cotangent = bwd_grad[0].reshape(tokens, heads_here, head_width)

    def summary_bwd(values_in, mixer_in, weight_in, bias_in, rate_in):
        return span_summary(values_in, mixer_in, weight_in, bias_in, rate_in, docs_bwd, doc_before)

    summary_out, summary_pull = jax.vjp(
        summary_bwd, bwd_values, mixer_bwd, weight_heads, bias_heads, rate_heads
    )
    decay_bwd, state_bwd = summary_out
    state_shape = state_bwd.shape
    state_flat = state_bwd.reshape(heads_here, -1)

    def output_bwd(values_in, mixer_in, weight_in, bias_in, rate_in, skip_in, state_in):
        return span_output(
            values_in,
            mixer_in,
            weight_in,
            bias_in,
            rate_in,
            skip_in,
            docs_bwd,
            doc_before,
            state_in,
        )

    def carried_only(state_in):
        return output_bwd(
            bwd_values, mixer_bwd, weight_heads, bias_heads, rate_heads, skip_heads, state_in
        )

    state_grad = jax.vjp(carried_only, jnp.zeros(state_shape, jnp.float32))[1](cotangent)[0]
    state_grad = state_grad.reshape(heads_here, -1)
    incoming_flat, adjoint_flat = both_scans(decay_bwd, state_flat, state_grad, "seq")
    incoming_bwd = incoming_flat.reshape(state_shape)

    unused, output_pull = jax.vjp(
        output_bwd,
        bwd_values,
        mixer_bwd,
        weight_heads,
        bias_heads,
        rate_heads,
        skip_heads,
        incoming_bwd,
    )
    out_grads = output_pull(cotangent)
    decay_grad = jnp.sum(adjoint_flat * incoming_flat, axis=1)
    sum_grads = summary_pull((decay_grad, adjoint_flat.reshape(state_shape)))
    mixer_grad = (out_grads[1].astype(jnp.float32) + sum_grads[1].astype(jnp.float32)).astype(
        jnp.bfloat16
    )
    other_grad = swap_heads(mixer_grad)
    mixer_full = jnp.where(
        group == 0,
        jnp.concatenate([mixer_grad, other_grad], axis=1),
        jnp.concatenate([other_grad, mixer_grad], axis=1),
    )
    mixer_slots = roll_blocks(mixer_full, size - 1 - mine, size, 1)
    mixer_slots = mixer_slots.reshape(tokens, size, -1)[:, ::-1].reshape(tokens, -1)
    back_proj = jnp.dot(mixer_slots, slot_weight, preferred_element_type=jnp.float32)
    value_grad = (out_grads[0].astype(jnp.float32) + sum_grads[0].astype(jnp.float32)).reshape(
        tokens, channels_here
    ) + back_proj
    value_grad = value_grad.astype(jnp.bfloat16)
    prev_part = shifted(value_grad.reshape(1, tokens, channels_here), "section", -1)
    dest_grad = roll_blocks(mixer_full, size - mine, size, 1)
    row_parts = lax.dot_general(
        dest_grad, bwd_flat, (((0,), (0,)), ((), ())), preferred_element_type=jnp.float32
    ).reshape(size, -1, channels_here)
    grad_rows = row_parts[0]
    for k in range(1, size):
        grad_rows = grad_rows + rotated(row_parts[k].astype(jnp.bfloat16), "seq", k).astype(
            jnp.float32
        )
    small = jnp.concatenate(
        [
            (out_grads[2] + sum_grads[2]).reshape(channels_here),
            out_grads[3] + sum_grads[3],
            out_grads[4] + sum_grads[4],
            out_grads[5],
        ]
    )
    small = seq_total(small)
    totals = (
        small[:channels_here],
        small[channels_here : channels_here + heads_here],
        small[channels_here + heads_here : channels_here + 2 * heads_here],
        small[channels_here + 2 * heads_here :],
    )
    return (
        prev_part,
        grad_rows[None],
        totals[0][None],
        totals[1][None],
        totals[2][None],
        totals[3][None],
    )


def solution(mesh):
    in_specs = (
        P("section", "seq", "head"),
        P("section", "seq"),
        P("section", "seq", "head"),
        P("section", "seq", "head"),
        P("section", "head"),
        P("section", "head"),
        P("section", "head"),
        P("section", "head"),
    )
    out_specs = (
        P("section", "seq", "head"),
        P("section", "seq", "head"),
        P("section", "head"),
        P("section", "head"),
        P("section", "head"),
        P("section", "head"),
    )
    return jax.shard_map(shards, mesh=mesh, in_specs=in_specs, out_specs=out_specs, check_vma=False)
```

```python
import jax
import jax.numpy as jnp
from jax import lax
from jax.sharding import PartitionSpec as P

EXACT = lax.Precision.HIGHEST


def shifted(block, axis, distance):
    devices = range(lax.axis_size(axis))
    route = [(i - distance, i) for i in devices if i - distance in devices]
    return lax.ppermute(block, axis, route)


def rotated(block, axis, distance):
    size = lax.axis_size(axis)
    route = [(i, (i + distance) % size) for i in range(size)]
    return lax.ppermute(block, axis, route)


def roll_blocks(value, shift, parts, dim):
    doubled = jnp.concatenate([value, value], axis=dim)
    width = value.shape[dim] // parts
    start = ((parts - shift) % parts) * width
    return lax.dynamic_slice_in_dim(doubled, start, value.shape[dim], axis=dim)


def swap_heads(block):
    return lax.ppermute(block, "head", [(0, 1), (1, 0)])


def seq_total(value):
    size = lax.axis_size("seq")
    if size & (size - 1):
        return lax.psum(value, "seq")
    distance = 1
    while distance < size:
        value = value + lax.ppermute(value, "seq", [(i, i ^ distance) for i in range(size)])
        distance *= 2
    return value


def contract(spec, left, right):
    return jnp.einsum(spec, left, right, preferred_element_type=jnp.float32)


def local_setup(values, step_weight, step_bias, rate_log):
    tokens = values.shape[0]
    raw_step = (
        jnp.einsum("thp,hp->th", values.astype(jnp.float32), step_weight, precision=EXACT)
        + step_bias[None, :]
    )
    step_size = jax.nn.softplus(raw_step)
    decay_log = -jnp.exp(rate_log)[None, :] * step_size
    row_ids = lax.broadcasted_iota(jnp.int32, (tokens, tokens), 0)
    col_ids = lax.broadcasted_iota(jnp.int32, (tokens, tokens), 1)
    triangle = (row_ids >= col_ids).astype(jnp.float32)
    cumulative = jnp.dot(triangle, decay_log, precision=EXACT)
    return (step_size, cumulative, row_ids, col_ids)


def span_summary(values, mixer, step_weight, step_bias, rate_log, docs, doc_before):
    step_size, cumulative, row_ids, col_ids = local_setup(values, step_weight, step_bias, rate_log)
    final_log = cumulative[-1]
    tail_mask = (docs == docs[-1]).astype(jnp.float32)[:, None]
    tail_weight = (
        jnp.exp(jnp.where(tail_mask > 0, final_log[None, :] - cumulative, 0.0))
        * tail_mask
        * step_size
    )
    unbroken = (docs[-1] == doc_before).astype(jnp.float32)
    carry_decay = jnp.exp(final_log) * unbroken
    half_width = mixer.shape[1] // 2
    writers = mixer[:, :half_width]
    weighted = (tail_weight[:, :, None] * writers.astype(jnp.float32)[:, None, :]).astype(
        jnp.bfloat16
    )
    span_state = contract("thn,thp->hnp", weighted, values)
    return (carry_decay, span_state)


def span_local(values, mixer, step_weight, step_bias, rate_log, skip_gain, docs):
    step_size, cumulative, row_ids, col_ids = local_setup(values, step_weight, step_bias, rate_log)
    half_width = mixer.shape[1] // 2
    writers = mixer[:, :half_width]
    readers = mixer[:, half_width:]
    affinity = jnp.dot(readers, writers.T, preferred_element_type=jnp.float32)
    same_doc = ((docs[:, None] == docs[None, :]) & (row_ids >= col_ids)).astype(jnp.float32)
    heads_first = cumulative.T
    log_gap = heads_first[:, :, None] - heads_first[:, None, :]
    mixing = (
        jnp.exp(jnp.where(same_doc[None] > 0, log_gap, 0.0))
        * same_doc[None]
        * affinity[None]
        * step_size.T[:, None, :]
    )
    mixing = mixing.astype(jnp.bfloat16)
    local_part = contract("hts,shp->thp", mixing, values)
    return values.astype(jnp.float32) * (1.0 + skip_gain)[None, :, None] + local_part


def span_carry(values, mixer, step_weight, step_bias, rate_log, docs, doc_before, incoming):
    step_size, cumulative, row_ids, col_ids = local_setup(values, step_weight, step_bias, rate_log)
    half_width = mixer.shape[1] // 2
    readers = mixer[:, half_width:]
    unbroken = (docs == doc_before).astype(jnp.float32)
    carry_scale = jnp.exp(cumulative) * unbroken[:, None]
    carried = jnp.einsum("tn,hnp->thp", readers.astype(jnp.float32), incoming, precision=EXACT)
    return carry_scale[:, :, None] * carried


def scan_rounds(decay, state, axis, forward):
    size, mine = (lax.axis_size(axis), lax.axis_index(axis))
    far_decay, far_state = (decay, state)
    near_decay = jnp.ones_like(decay)
    near_state = jnp.zeros_like(state)
    distance = 1
    while distance < size:
        got_decay, got_state = shifted(
            (far_decay, far_state.astype(jnp.bfloat16)), axis, distance if forward else -distance
        )
        got_state = got_state.astype(jnp.float32)
        near_state = near_state + near_decay[:, None] * got_state
        near_decay = near_decay * got_decay
        if distance * 2 < size:
            far_state = far_state + far_decay[:, None] * got_state
            far_decay = far_decay * got_decay
        distance *= 2
    return near_state


def both_scans(decay, state, state_grad, axis):
    size, mine = (lax.axis_size(axis), lax.axis_index(axis))
    if size & (size - 1):
        return (
            scan_rounds(decay, state, axis, True),
            scan_rounds(decay, state_grad, axis, False),
        )
    width = state.shape[1]
    total_decay = decay
    total_fwd, total_bwd = (state, state_grad)
    before = jnp.zeros_like(state)
    before_decay = jnp.ones_like(decay)
    after = jnp.zeros_like(state_grad)
    after_decay = jnp.ones_like(decay)
    distance = 1
    while distance < size:
        high = lax.convert_element_type(total_decay.astype(jnp.bfloat16), jnp.float32)
        low = total_decay - high
        pad = jnp.zeros((decay.shape[0], 126), jnp.float32)
        payload = jnp.concatenate(
            [total_fwd, total_bwd, high[:, None], low[:, None], pad], axis=1
        ).astype(jnp.bfloat16)
        upper = (mine // distance) % 2 == 1
        if distance * 2 < size:
            got = lax.ppermute(payload, axis, [(i, i ^ distance) for i in range(size)])
            got = got.astype(jnp.float32)
            got_fwd = got[:, :width]
            got_bwd = got[:, width : 2 * width]
        else:
            last = jnp.where(upper, total_bwd, total_fwd).astype(jnp.bfloat16)
            last = jnp.concatenate([last, payload[:, 2 * width :]], axis=1)
            got = lax.ppermute(last, axis, [(i, i ^ distance) for i in range(size)])
            got = got.astype(jnp.float32)
            got_fwd = got[:, :width]
            got_bwd = got_fwd
            got = jnp.concatenate([got[:, :width], got], axis=1)
        got_decay = got[:, 2 * width] + got[:, 2 * width + 1]
        before = jnp.where(upper, before + before_decay[:, None] * got_fwd, before)
        before_decay = jnp.where(upper, before_decay * got_decay, before_decay)
        after = jnp.where(upper, after, after + after_decay[:, None] * got_bwd)
        after_decay = jnp.where(upper, after_decay, after_decay * got_decay)
        if distance * 2 < size:
            total_fwd = jnp.where(
                upper,
                total_fwd + total_decay[:, None] * got_fwd,
                got_fwd + got_decay[:, None] * total_fwd,
            )
            total_bwd = jnp.where(
                upper,
                got_bwd + got_decay[:, None] * total_bwd,
                total_bwd + total_decay[:, None] * got_bwd,
            )
            total_decay = total_decay * got_decay
        distance *= 2
    return (before, after)


def shards(bwd_input, bwd_docs, bwd_grad, proj_weight, step_weight, step_bias, rate_log, skip_gain):
    tokens = bwd_input.shape[1]
    channels_here = bwd_input.shape[2]
    heads_here = step_bias.shape[1]
    head_width = channels_here // heads_here
    bwd_flat = bwd_input[0]
    bwd_values = bwd_flat.reshape(tokens, heads_here, head_width)
    weight_heads = step_weight[0].reshape(heads_here, head_width)
    bias_heads = step_bias[0]
    rate_heads = rate_log[0]
    skip_heads = skip_gain[0]
    docs_bwd = bwd_docs[0]
    doc_before = shifted(docs_bwd[-1:], "seq", 1)[0]
    size, mine = (lax.axis_size("seq"), lax.axis_index("seq"))
    group = lax.axis_index("head")
    own_rows = proj_weight[0]
    slot_weight = jnp.concatenate(
        [own_rows] + [rotated(own_rows, "seq", k) for k in range(1, size)], axis=0
    )
    slot_value = jnp.dot(bwd_flat, slot_weight.T, preferred_element_type=jnp.float32)
    slot_value = slot_value.reshape(tokens, size, -1)[:, ::-1].reshape(tokens, -1)
    partial_value = roll_blocks(slot_value, mine + 1, size, 1)
    group_width = partial_value.shape[1] // 2
    mine_part = lax.dynamic_slice_in_dim(partial_value, group * group_width, group_width, axis=1)
    other_part = lax.dynamic_slice_in_dim(
        partial_value, (1 - group) * group_width, group_width, axis=1
    )
    mixer_bwd = (
        mine_part + swap_heads(other_part.astype(jnp.bfloat16)).astype(jnp.float32)
    ).astype(jnp.bfloat16)
    cotangent = bwd_grad[0].reshape(tokens, heads_here, head_width)

    def summary_bwd(values_in, mixer_in, weight_in, bias_in, rate_in):
        return span_summary(values_in, mixer_in, weight_in, bias_in, rate_in, docs_bwd, doc_before)

    summary_out, summary_pull = jax.vjp(
        summary_bwd, bwd_values, mixer_bwd, weight_heads, bias_heads, rate_heads
    )
    decay_bwd, state_bwd = summary_out
    state_shape = state_bwd.shape
    state_flat = state_bwd.reshape(heads_here, -1)

    out_ct = cotangent.astype(jnp.float32)

    def local_bwd(values_in, mixer_in, weight_in, bias_in, rate_in, skip_in):
        return span_local(values_in, mixer_in, weight_in, bias_in, rate_in, skip_in, docs_bwd)

    local_grads = jax.vjp(
        local_bwd, bwd_values, mixer_bwd, weight_heads, bias_heads, rate_heads, skip_heads
    )[1](out_ct)

    def carry_bwd(values_in, mixer_in, weight_in, bias_in, rate_in, state_in):
        return span_carry(
            values_in, mixer_in, weight_in, bias_in, rate_in, docs_bwd, doc_before, state_in
        )

    def carried_only(state_in):
        return carry_bwd(bwd_values, mixer_bwd, weight_heads, bias_heads, rate_heads, state_in)

    state_grad = jax.vjp(carried_only, jnp.zeros(state_shape, jnp.float32))[1](out_ct)[0]
    state_grad = state_grad.reshape(heads_here, -1)
    incoming_flat, adjoint_flat = both_scans(decay_bwd, state_flat, state_grad, "seq")
    incoming_bwd = incoming_flat.reshape(state_shape)
    carry_grads = jax.vjp(
        carry_bwd, bwd_values, mixer_bwd, weight_heads, bias_heads, rate_heads, incoming_bwd
    )[1](out_ct)
    out_grads = (
        (local_grads[0].astype(jnp.float32) + carry_grads[0].astype(jnp.float32)),
        (local_grads[1].astype(jnp.float32) + carry_grads[1].astype(jnp.float32)),
        local_grads[2] + carry_grads[2],
        local_grads[3] + carry_grads[3],
        local_grads[4] + carry_grads[4],
        local_grads[5],
    )
    decay_grad = jnp.sum(adjoint_flat * incoming_flat, axis=1)
    sum_grads = summary_pull((decay_grad, adjoint_flat.reshape(state_shape)))
    mixer_grad = (out_grads[1].astype(jnp.float32) + sum_grads[1].astype(jnp.float32)).astype(
        jnp.bfloat16
    )
    other_grad = swap_heads(mixer_grad)
    mixer_full = jnp.where(
        group == 0,
        jnp.concatenate([mixer_grad, other_grad], axis=1),
        jnp.concatenate([other_grad, mixer_grad], axis=1),
    )
    mixer_slots = roll_blocks(mixer_full, size - 1 - mine, size, 1)
    mixer_slots = mixer_slots.reshape(tokens, size, -1)[:, ::-1].reshape(tokens, -1)
    back_proj = jnp.dot(mixer_slots, slot_weight, preferred_element_type=jnp.float32)
    value_grad = (out_grads[0].astype(jnp.float32) + sum_grads[0].astype(jnp.float32)).reshape(
        tokens, channels_here
    ) + back_proj
    value_grad = value_grad.astype(jnp.bfloat16)
    prev_part = shifted(value_grad.reshape(1, tokens, channels_here), "section", -1)
    dest_grad = roll_blocks(mixer_full, size - mine, size, 1)
    row_parts = lax.dot_general(
        dest_grad, bwd_flat, (((0,), (0,)), ((), ())), preferred_element_type=jnp.float32
    ).reshape(size, -1, channels_here)
    grad_rows = row_parts[0]
    for k in range(1, size):
        grad_rows = grad_rows + rotated(row_parts[k].astype(jnp.bfloat16), "seq", k).astype(
            jnp.float32
        )
    small = jnp.concatenate(
        [
            (out_grads[2] + sum_grads[2]).reshape(channels_here),
            out_grads[3] + sum_grads[3],
            out_grads[4] + sum_grads[4],
            out_grads[5],
        ]
    )
    small = seq_total(small)
    totals = (
        small[:channels_here],
        small[channels_here : channels_here + heads_here],
        small[channels_here + heads_here : channels_here + 2 * heads_here],
        small[channels_here + 2 * heads_here :],
    )
    return (
        prev_part,
        grad_rows[None],
        totals[0][None],
        totals[1][None],
        totals[2][None],
        totals[3][None],
    )


def solution(mesh):
    in_specs = (
        P("section", "seq", "head"),
        P("section", "seq"),
        P("section", "seq", "head"),
        P("section", "seq", "head"),
        P("section", "head"),
        P("section", "head"),
        P("section", "head"),
        P("section", "head"),
    )
    out_specs = (
        P("section", "seq", "head"),
        P("section", "seq", "head"),
        P("section", "head"),
        P("section", "head"),
        P("section", "head"),
        P("section", "head"),
    )
    return jax.shard_map(shards, mesh=mesh, in_specs=in_specs, out_specs=out_specs, check_vma=False)
```

```python
import jax
import jax.numpy as jnp
from jax import lax
from jax.sharding import PartitionSpec as P

EXACT = lax.Precision.HIGHEST


def shifted(block, axis, distance):
    devices = range(lax.axis_size(axis))
    route = [(i - distance, i) for i in devices if i - distance in devices]
    return lax.ppermute(block, axis, route)


def rotated(block, axis, distance):
    size = lax.axis_size(axis)
    route = [(i, (i + distance) % size) for i in range(size)]
    return lax.ppermute(block, axis, route)


def roll_blocks(value, shift, parts, dim):
    doubled = jnp.concatenate([value, value], axis=dim)
    width = value.shape[dim] // parts
    start = ((parts - shift) % parts) * width
    return lax.dynamic_slice_in_dim(doubled, start, value.shape[dim], axis=dim)


def swap_heads(block):
    return lax.ppermute(block, "head", [(0, 1), (1, 0)])


def contract(spec, left, right):
    return jnp.einsum(spec, left, right, preferred_element_type=jnp.float32)


def local_setup(values, step_weight, step_bias, rate_log):
    tokens = values.shape[0]
    raw_step = (
        jnp.einsum("thp,hp->th", values.astype(jnp.float32), step_weight, precision=EXACT)
        + step_bias[None, :]
    )
    step_size = jax.nn.softplus(raw_step)
    decay_log = -jnp.exp(rate_log)[None, :] * step_size
    row_ids = lax.broadcasted_iota(jnp.int32, (tokens, tokens), 0)
    col_ids = lax.broadcasted_iota(jnp.int32, (tokens, tokens), 1)
    triangle = (row_ids >= col_ids).astype(jnp.float32)
    cumulative = jnp.dot(triangle, decay_log, precision=EXACT)
    return (step_size, cumulative, row_ids, col_ids)


def span_summary(values, mixer, step_weight, step_bias, rate_log, docs, doc_before):
    step_size, cumulative, row_ids, col_ids = local_setup(values, step_weight, step_bias, rate_log)
    final_log = cumulative[-1]
    tail_mask = (docs == docs[-1]).astype(jnp.float32)[:, None]
    tail_weight = (
        jnp.exp(jnp.where(tail_mask > 0, final_log[None, :] - cumulative, 0.0))
        * tail_mask
        * step_size
    )
    unbroken = (docs[-1] == doc_before).astype(jnp.float32)
    carry_decay = jnp.exp(final_log) * unbroken
    half_width = mixer.shape[1] // 2
    writers = mixer[:, :half_width]
    weighted = (tail_weight[:, :, None] * writers.astype(jnp.float32)[:, None, :]).astype(
        jnp.bfloat16
    )
    span_state = contract("thn,thp->hnp", weighted, values)
    return (carry_decay, span_state)


def span_local(values, mixer, step_weight, step_bias, rate_log, skip_gain, docs):
    step_size, cumulative, row_ids, col_ids = local_setup(values, step_weight, step_bias, rate_log)
    half_width = mixer.shape[1] // 2
    writers = mixer[:, :half_width]
    readers = mixer[:, half_width:]
    affinity = jnp.dot(readers, writers.T, preferred_element_type=jnp.float32)
    same_doc = ((docs[:, None] == docs[None, :]) & (row_ids >= col_ids)).astype(jnp.float32)
    heads_first = cumulative.T
    log_gap = heads_first[:, :, None] - heads_first[:, None, :]
    mixing = (
        jnp.exp(jnp.where(same_doc[None] > 0, log_gap, 0.0))
        * same_doc[None]
        * affinity[None]
        * step_size.T[:, None, :]
    )
    mixing = mixing.astype(jnp.bfloat16)
    local_part = contract("hts,shp->thp", mixing, values)
    return values.astype(jnp.float32) * (1.0 + skip_gain)[None, :, None] + local_part


def span_carry(values, mixer, step_weight, step_bias, rate_log, docs, doc_before, incoming):
    step_size, cumulative, row_ids, col_ids = local_setup(values, step_weight, step_bias, rate_log)
    half_width = mixer.shape[1] // 2
    readers = mixer[:, half_width:]
    unbroken = (docs == doc_before).astype(jnp.float32)
    carry_scale = jnp.exp(cumulative) * unbroken[:, None]
    carried = jnp.einsum("tn,hnp->thp", readers.astype(jnp.float32), incoming, precision=EXACT)
    return carry_scale[:, :, None] * carried


def scan_rounds(decay, state, axis, forward):
    size, mine = (lax.axis_size(axis), lax.axis_index(axis))
    far_decay, far_state = (decay, state)
    near_decay = jnp.ones_like(decay)
    near_state = jnp.zeros_like(state)
    distance = 1
    while distance < size:
        got_decay, got_state = shifted(
            (far_decay, far_state.astype(jnp.bfloat16)), axis, distance if forward else -distance
        )
        got_state = got_state.astype(jnp.float32)
        near_state = near_state + near_decay[:, None] * got_state
        near_decay = near_decay * got_decay
        if distance * 2 < size:
            far_state = far_state + far_decay[:, None] * got_state
            far_decay = far_decay * got_decay
        distance *= 2
    return near_state


def both_scans(decay, state, state_grad, axis, filler_fn, filler_args):
    size, mine = (lax.axis_size(axis), lax.axis_index(axis))
    if size & (size - 1):
        return (
            scan_rounds(decay, state, axis, True),
            scan_rounds(decay, state_grad, axis, False),
            filler_fn(*filler_args),
        )
    width = state.shape[1]
    total_decay = decay
    total_fwd, total_bwd = (state, state_grad)
    before = jnp.zeros_like(state)
    before_decay = jnp.ones_like(decay)
    after = jnp.zeros_like(state_grad)
    after_decay = jnp.ones_like(decay)
    distance = 1
    while distance < size:
        high = lax.convert_element_type(total_decay.astype(jnp.bfloat16), jnp.float32)
        low = total_decay - high
        pad = jnp.zeros((decay.shape[0], 126), jnp.float32)
        payload = jnp.concatenate(
            [total_fwd, total_bwd, high[:, None], low[:, None], pad], axis=1
        ).astype(jnp.bfloat16)
        upper = (mine // distance) % 2 == 1
        if distance == 1:
            payload, filler_args = lax.optimization_barrier((payload, filler_args))
        if distance * 2 < size:
            got = lax.ppermute(payload, axis, [(i, i ^ distance) for i in range(size)])
            got = got.astype(jnp.float32)
            got_fwd = got[:, :width]
            got_bwd = got[:, width : 2 * width]
        else:
            last = jnp.where(upper, total_bwd, total_fwd).astype(jnp.bfloat16)
            last = jnp.concatenate([last, payload[:, 2 * width :]], axis=1)
            got = lax.ppermute(last, axis, [(i, i ^ distance) for i in range(size)])
            got = got.astype(jnp.float32)
            got_fwd = got[:, :width]
            got_bwd = got_fwd
            got = jnp.concatenate([got[:, :width], got], axis=1)
        if distance == 1:
            got, filler = lax.optimization_barrier((got, filler_fn(*filler_args)))
        got_decay = got[:, 2 * width] + got[:, 2 * width + 1]
        before = jnp.where(upper, before + before_decay[:, None] * got_fwd, before)
        before_decay = jnp.where(upper, before_decay * got_decay, before_decay)
        after = jnp.where(upper, after, after + after_decay[:, None] * got_bwd)
        after_decay = jnp.where(upper, after_decay, after_decay * got_decay)
        if distance * 2 < size:
            total_fwd = jnp.where(
                upper,
                total_fwd + total_decay[:, None] * got_fwd,
                got_fwd + got_decay[:, None] * total_fwd,
            )
            total_bwd = jnp.where(
                upper,
                got_bwd + got_decay[:, None] * total_bwd,
                total_bwd + total_decay[:, None] * got_bwd,
            )
            total_decay = total_decay * got_decay
        distance *= 2
    return (before, after, filler)


def shards(bwd_input, bwd_docs, bwd_grad, proj_weight, step_weight, step_bias, rate_log, skip_gain):
    tokens = bwd_input.shape[1]
    channels_here = bwd_input.shape[2]
    heads_here = step_bias.shape[1]
    head_width = channels_here // heads_here
    bwd_flat = bwd_input[0]
    bwd_values = bwd_flat.reshape(tokens, heads_here, head_width)
    weight_heads = step_weight[0].reshape(heads_here, head_width)
    bias_heads = step_bias[0]
    rate_heads = rate_log[0]
    skip_heads = skip_gain[0]
    docs_bwd = bwd_docs[0]
    doc_before = shifted(docs_bwd[-1:], "seq", 1)[0]
    size, mine = (lax.axis_size("seq"), lax.axis_index("seq"))
    group = lax.axis_index("head")
    own_rows = proj_weight[0]
    slot_weight = jnp.concatenate(
        [own_rows] + [rotated(own_rows, "seq", k) for k in range(1, size)], axis=0
    )
    slot_value = jnp.dot(bwd_flat, slot_weight.T, preferred_element_type=jnp.float32)
    slot_value = slot_value.reshape(tokens, size, -1)[:, ::-1].reshape(tokens, -1)
    partial_value = roll_blocks(slot_value, mine + 1, size, 1)
    group_width = partial_value.shape[1] // 2
    mine_part = lax.dynamic_slice_in_dim(partial_value, group * group_width, group_width, axis=1)
    other_part = lax.dynamic_slice_in_dim(
        partial_value, (1 - group) * group_width, group_width, axis=1
    )
    mixer_bwd = (
        mine_part + swap_heads(other_part.astype(jnp.bfloat16)).astype(jnp.float32)
    ).astype(jnp.bfloat16)
    cotangent = bwd_grad[0].reshape(tokens, heads_here, head_width)

    def summary_bwd(values_in, mixer_in, weight_in, bias_in, rate_in):
        return span_summary(values_in, mixer_in, weight_in, bias_in, rate_in, docs_bwd, doc_before)

    summary_out, summary_pull = jax.vjp(
        summary_bwd, bwd_values, mixer_bwd, weight_heads, bias_heads, rate_heads
    )
    decay_bwd, state_bwd = summary_out
    state_shape = state_bwd.shape
    state_flat = state_bwd.reshape(heads_here, -1)

    out_ct = cotangent.astype(jnp.float32)

    def local_bwd(values_in, mixer_in, weight_in, bias_in, rate_in, skip_in):
        return span_local(values_in, mixer_in, weight_in, bias_in, rate_in, skip_in, docs_bwd)

    def local_pull(*primals):
        return jax.vjp(local_bwd, *primals[:-1])[1](primals[-1])


    def carry_bwd(values_in, mixer_in, weight_in, bias_in, rate_in, state_in):
        return span_carry(
            values_in, mixer_in, weight_in, bias_in, rate_in, docs_bwd, doc_before, state_in
        )

    def carried_only(state_in):
        return carry_bwd(bwd_values, mixer_bwd, weight_heads, bias_heads, rate_heads, state_in)

    state_grad = jax.vjp(carried_only, jnp.zeros(state_shape, jnp.float32))[1](out_ct)[0]
    state_grad = state_grad.reshape(heads_here, -1)
    incoming_flat, adjoint_flat, local_grads = both_scans(
        decay_bwd,
        state_flat,
        state_grad,
        "seq",
        local_pull,
        (bwd_values, mixer_bwd, weight_heads, bias_heads, rate_heads, skip_heads, out_ct),
    )
    incoming_bwd = incoming_flat.reshape(state_shape)
    carry_grads = jax.vjp(
        carry_bwd, bwd_values, mixer_bwd, weight_heads, bias_heads, rate_heads, incoming_bwd
    )[1](out_ct)
    out_grads = (
        (local_grads[0].astype(jnp.float32) + carry_grads[0].astype(jnp.float32)),
        (local_grads[1].astype(jnp.float32) + carry_grads[1].astype(jnp.float32)),
        local_grads[2] + carry_grads[2],
        local_grads[3] + carry_grads[3],
        local_grads[4] + carry_grads[4],
        local_grads[5],
    )
    decay_grad = jnp.sum(adjoint_flat * incoming_flat, axis=1)
    sum_grads = summary_pull((decay_grad, adjoint_flat.reshape(state_shape)))
    mixer_grad = (out_grads[1].astype(jnp.float32) + sum_grads[1].astype(jnp.float32)).astype(
        jnp.bfloat16
    )
    other_grad = swap_heads(mixer_grad)
    mixer_full = jnp.where(
        group == 0,
        jnp.concatenate([mixer_grad, other_grad], axis=1),
        jnp.concatenate([other_grad, mixer_grad], axis=1),
    )
    mixer_slots = roll_blocks(mixer_full, size - 1 - mine, size, 1)
    mixer_slots = mixer_slots.reshape(tokens, size, -1)[:, ::-1].reshape(tokens, -1)
    back_proj = jnp.dot(mixer_slots, slot_weight, preferred_element_type=jnp.float32)
    value_grad = (out_grads[0].astype(jnp.float32) + sum_grads[0].astype(jnp.float32)).reshape(
        tokens, channels_here
    ) + back_proj
    value_grad = value_grad.astype(jnp.bfloat16)
    prev_part = shifted(value_grad.reshape(1, tokens, channels_here), "section", -1)
    dest_grad = roll_blocks(mixer_full, size - mine, size, 1)
    row_parts = lax.dot_general(
        dest_grad, bwd_flat, (((0,), (0,)), ((), ())), preferred_element_type=jnp.float32
    ).reshape(size, -1, channels_here)
    small = jnp.concatenate(
        [
            (out_grads[2] + sum_grads[2]).reshape(channels_here),
            out_grads[3] + sum_grads[3],
            out_grads[4] + sum_grads[4],
            out_grads[5],
        ]
    )
    small_rows = -(-small.shape[0] // channels_here)
    small = jnp.pad(small, (0, small_rows * channels_here - small.shape[0]))
    small = small.reshape(small_rows, channels_here)
    small_high = small.astype(jnp.bfloat16)
    small_low = (small - small_high.astype(jnp.float32)).astype(jnp.bfloat16)
    small_coded = jnp.concatenate([small_high, small_low], axis=0)
    block_rows = row_parts.shape[1]
    grad_rows = row_parts[0]
    small_slots = [small_coded]
    for k in range(1, size):
        message = jnp.concatenate([row_parts[k].astype(jnp.bfloat16), small_coded], axis=0)
        got = rotated(message, "seq", k)
        grad_rows = grad_rows + got[:block_rows].astype(jnp.float32)
        small_slots.append(got[block_rows:])
    small_slots = jnp.stack(small_slots[::-1])
    small_slots = roll_blocks(small_slots, mine + 1, size, 0).astype(jnp.float32)
    small_parts = small_slots[:, :small_rows] + small_slots[:, small_rows:]
    small_total = small_parts[0]
    for j in range(1, size):
        small_total = small_total + small_parts[j]
    small = small_total.reshape(-1)
    totals = (
        small[:channels_here],
        small[channels_here : channels_here + heads_here],
        small[channels_here + heads_here : channels_here + 2 * heads_here],
        small[channels_here + 2 * heads_here : channels_here + 3 * heads_here],
    )
    return (
        prev_part,
        grad_rows[None],
        totals[0][None],
        totals[1][None],
        totals[2][None],
        totals[3][None],
    )


def solution(mesh):
    in_specs = (
        P("section", "seq", "head"),
        P("section", "seq"),
        P("section", "seq", "head"),
        P("section", "seq", "head"),
        P("section", "head"),
        P("section", "head"),
        P("section", "head"),
        P("section", "head"),
    )
    out_specs = (
        P("section", "seq", "head"),
        P("section", "seq", "head"),
        P("section", "head"),
        P("section", "head"),
        P("section", "head"),
        P("section", "head"),
    )
    return jax.shard_map(shards, mesh=mesh, in_specs=in_specs, out_specs=out_specs, check_vma=False)
```

```python
import jax
import jax.numpy as jnp
from jax import lax
from jax.sharding import PartitionSpec as P

EXACT = lax.Precision.HIGHEST


def shifted(block, axis, distance):
    devices = range(lax.axis_size(axis))
    route = [(i - distance, i) for i in devices if i - distance in devices]
    return lax.ppermute(block, axis, route)


def rotated(block, axis, distance):
    size = lax.axis_size(axis)
    route = [(i, (i + distance) % size) for i in range(size)]
    return lax.ppermute(block, axis, route)


def roll_blocks(value, shift, parts, dim):
    doubled = jnp.concatenate([value, value], axis=dim)
    width = value.shape[dim] // parts
    start = ((parts - shift) % parts) * width
    return lax.dynamic_slice_in_dim(doubled, start, value.shape[dim], axis=dim)


def swap_heads(block):
    return lax.ppermute(block, "head", [(0, 1), (1, 0)])


def contract(spec, left, right):
    return jnp.einsum(spec, left, right, preferred_element_type=jnp.float32)


def local_setup(values, step_weight, step_bias, rate_log):
    tokens = values.shape[0]
    raw_step = (
        jnp.einsum("thp,hp->th", values.astype(jnp.float32), step_weight, precision=EXACT)
        + step_bias[None, :]
    )
    step_size = jax.nn.softplus(raw_step)
    decay_log = -jnp.exp(rate_log)[None, :] * step_size
    row_ids = lax.broadcasted_iota(jnp.int32, (tokens, tokens), 0)
    col_ids = lax.broadcasted_iota(jnp.int32, (tokens, tokens), 1)
    triangle = (row_ids >= col_ids).astype(jnp.float32)
    cumulative = jnp.dot(triangle, decay_log, precision=EXACT)
    return (step_size, cumulative, row_ids, col_ids)


def span_summary(values, mixer, step_weight, step_bias, rate_log, docs, doc_before):
    step_size, cumulative, row_ids, col_ids = local_setup(values, step_weight, step_bias, rate_log)
    final_log = cumulative[-1]
    tail_mask = (docs == docs[-1]).astype(jnp.float32)[:, None]
    tail_weight = (
        jnp.exp(jnp.where(tail_mask > 0, final_log[None, :] - cumulative, 0.0))
        * tail_mask
        * step_size
    )
    unbroken = (docs[-1] == doc_before).astype(jnp.float32)
    carry_decay = jnp.exp(final_log) * unbroken
    half_width = mixer.shape[1] // 2
    writers = mixer[:, :half_width]
    weighted = (tail_weight[:, :, None] * writers.astype(jnp.float32)[:, None, :]).astype(
        jnp.bfloat16
    )
    span_state = contract("thn,thp->hnp", weighted, values)
    return (carry_decay, span_state)


def span_local(values, mixer, step_weight, step_bias, rate_log, skip_gain, docs):
    step_size, cumulative, row_ids, col_ids = local_setup(values, step_weight, step_bias, rate_log)
    half_width = mixer.shape[1] // 2
    writers = mixer[:, :half_width]
    readers = mixer[:, half_width:]
    affinity = jnp.dot(readers, writers.T, preferred_element_type=jnp.float32)
    same_doc = ((docs[:, None] == docs[None, :]) & (row_ids >= col_ids)).astype(jnp.float32)
    heads_first = cumulative.T
    log_gap = heads_first[:, :, None] - heads_first[:, None, :]
    mixing = (
        jnp.exp(jnp.where(same_doc[None] > 0, log_gap, 0.0))
        * same_doc[None]
        * affinity[None]
        * step_size.T[:, None, :]
    )
    mixing = mixing.astype(jnp.bfloat16)
    local_part = contract("hts,shp->thp", mixing, values)
    return values.astype(jnp.float32) * (1.0 + skip_gain)[None, :, None] + local_part


def span_carry(values, mixer, step_weight, step_bias, rate_log, docs, doc_before, incoming):
    step_size, cumulative, row_ids, col_ids = local_setup(values, step_weight, step_bias, rate_log)
    half_width = mixer.shape[1] // 2
    readers = mixer[:, half_width:]
    unbroken = (docs == doc_before).astype(jnp.float32)
    carry_scale = jnp.exp(cumulative) * unbroken[:, None]
    carried = jnp.einsum("tn,hnp->thp", readers.astype(jnp.float32), incoming, precision=EXACT)
    return carry_scale[:, :, None] * carried


def scan_rounds(decay, state, axis, forward):
    size, mine = (lax.axis_size(axis), lax.axis_index(axis))
    far_decay, far_state = (decay, state)
    near_decay = jnp.ones_like(decay)
    near_state = jnp.zeros_like(state)
    distance = 1
    while distance < size:
        got_decay, got_state = shifted(
            (far_decay, far_state.astype(jnp.bfloat16)), axis, distance if forward else -distance
        )
        got_state = got_state.astype(jnp.float32)
        near_state = near_state + near_decay[:, None] * got_state
        near_decay = near_decay * got_decay
        if distance * 2 < size:
            far_state = far_state + far_decay[:, None] * got_state
            far_decay = far_decay * got_decay
        distance *= 2
    return near_state


def both_scans(decay, state, state_grad, axis, filler_fn, filler_args):
    size, mine = (lax.axis_size(axis), lax.axis_index(axis))
    if size & (size - 1):
        return (
            scan_rounds(decay, state, axis, True),
            scan_rounds(decay, state_grad, axis, False),
            filler_fn(*filler_args),
        )
    width = state.shape[1]
    total_decay = decay
    total_fwd, total_bwd = (state, state_grad)
    before = jnp.zeros_like(state)
    before_decay = jnp.ones_like(decay)
    after = jnp.zeros_like(state_grad)
    after_decay = jnp.ones_like(decay)
    distance = 1
    while distance < size:
        high = lax.convert_element_type(total_decay.astype(jnp.bfloat16), jnp.float32)
        low = total_decay - high
        pad = jnp.zeros((decay.shape[0], 126), jnp.float32)
        payload = jnp.concatenate(
            [total_fwd, total_bwd, high[:, None], low[:, None], pad], axis=1
        ).astype(jnp.bfloat16)
        upper = (mine // distance) % 2 == 1
        if distance == 1:
            payload, filler_args = lax.optimization_barrier((payload, filler_args))
        if distance * 2 < size:
            got = lax.ppermute(payload, axis, [(i, i ^ distance) for i in range(size)])
            got = got.astype(jnp.float32)
            got_fwd = got[:, :width]
            got_bwd = got[:, width : 2 * width]
        else:
            last = jnp.where(upper, total_bwd, total_fwd).astype(jnp.bfloat16)
            last = jnp.concatenate([last, payload[:, 2 * width :]], axis=1)
            got = lax.ppermute(last, axis, [(i, i ^ distance) for i in range(size)])
            got = got.astype(jnp.float32)
            got_fwd = got[:, :width]
            got_bwd = got_fwd
            got = jnp.concatenate([got[:, :width], got], axis=1)
        if distance == 1:
            got, filler = lax.optimization_barrier((got, filler_fn(*filler_args)))
        got_decay = got[:, 2 * width] + got[:, 2 * width + 1]
        before = jnp.where(upper, before + before_decay[:, None] * got_fwd, before)
        before_decay = jnp.where(upper, before_decay * got_decay, before_decay)
        after = jnp.where(upper, after, after + after_decay[:, None] * got_bwd)
        after_decay = jnp.where(upper, after_decay, after_decay * got_decay)
        if distance * 2 < size:
            total_fwd = jnp.where(
                upper,
                total_fwd + total_decay[:, None] * got_fwd,
                got_fwd + got_decay[:, None] * total_fwd,
            )
            total_bwd = jnp.where(
                upper,
                got_bwd + got_decay[:, None] * total_bwd,
                total_bwd + total_decay[:, None] * got_bwd,
            )
            total_decay = total_decay * got_decay
        distance *= 2
    return (before, after, filler)


def shards(bwd_input, bwd_docs, bwd_grad, proj_weight, step_weight, step_bias, rate_log, skip_gain):
    tokens = bwd_input.shape[1]
    channels_here = bwd_input.shape[2]
    heads_here = step_bias.shape[1]
    head_width = channels_here // heads_here
    bwd_flat = bwd_input[0]
    bwd_values = bwd_flat.reshape(tokens, heads_here, head_width)
    weight_heads = step_weight[0].reshape(heads_here, head_width)
    bias_heads = step_bias[0]
    rate_heads = rate_log[0]
    skip_heads = skip_gain[0]
    docs_bwd = bwd_docs[0]
    doc_before = shifted(docs_bwd[-1:], "seq", 1)[0]
    size, mine = (lax.axis_size("seq"), lax.axis_index("seq"))
    group = lax.axis_index("head")
    own_rows = proj_weight[0]
    pairs, pair, parity = (size // 2, mine // 2, mine % 2)
    partner_rows = lax.ppermute(own_rows, "seq", [(i, i ^ 1) for i in range(size)])
    pair_rows = jnp.where(
        parity == 0,
        jnp.concatenate([own_rows, partner_rows], axis=0),
        jnp.concatenate([partner_rows, own_rows], axis=0),
    )
    slot_weight = jnp.concatenate(
        [pair_rows] + [rotated(pair_rows, "seq", 2 * k) for k in range(1, pairs)], axis=0
    )
    slot_value = jnp.dot(bwd_flat, slot_weight.T, preferred_element_type=jnp.float32)
    slot_value = slot_value.reshape(tokens, pairs, -1)[:, ::-1].reshape(tokens, -1)
    partial_value = roll_blocks(slot_value, pair + 1, pairs, 1)
    group_width = partial_value.shape[1] // 2
    mine_part = lax.dynamic_slice_in_dim(partial_value, group * group_width, group_width, axis=1)
    other_part = lax.dynamic_slice_in_dim(
        partial_value, (1 - group) * group_width, group_width, axis=1
    )
    mixer_bwd = (
        mine_part + swap_heads(other_part.astype(jnp.bfloat16)).astype(jnp.float32)
    ).astype(jnp.bfloat16)
    cotangent = bwd_grad[0].reshape(tokens, heads_here, head_width)

    def summary_bwd(values_in, mixer_in, weight_in, bias_in, rate_in):
        return span_summary(values_in, mixer_in, weight_in, bias_in, rate_in, docs_bwd, doc_before)

    summary_out, summary_pull = jax.vjp(
        summary_bwd, bwd_values, mixer_bwd, weight_heads, bias_heads, rate_heads
    )
    decay_bwd, state_bwd = summary_out
    state_shape = state_bwd.shape
    state_flat = state_bwd.reshape(heads_here, -1)

    out_ct = cotangent.astype(jnp.float32)

    def local_bwd(values_in, mixer_in, weight_in, bias_in, rate_in, skip_in):
        return span_local(values_in, mixer_in, weight_in, bias_in, rate_in, skip_in, docs_bwd)

    def local_pull(*primals):
        return jax.vjp(local_bwd, *primals[:-1])[1](primals[-1])


    def carry_bwd(values_in, mixer_in, weight_in, bias_in, rate_in, state_in):
        return span_carry(
            values_in, mixer_in, weight_in, bias_in, rate_in, docs_bwd, doc_before, state_in
        )

    def carried_only(state_in):
        return carry_bwd(bwd_values, mixer_bwd, weight_heads, bias_heads, rate_heads, state_in)

    state_grad = jax.vjp(carried_only, jnp.zeros(state_shape, jnp.float32))[1](out_ct)[0]
    state_grad = state_grad.reshape(heads_here, -1)
    incoming_flat, adjoint_flat, local_grads = both_scans(
        decay_bwd,
        state_flat,
        state_grad,
        "seq",
        local_pull,
        (bwd_values, mixer_bwd, weight_heads, bias_heads, rate_heads, skip_heads, out_ct),
    )
    incoming_bwd = incoming_flat.reshape(state_shape)
    carry_grads = jax.vjp(
        carry_bwd, bwd_values, mixer_bwd, weight_heads, bias_heads, rate_heads, incoming_bwd
    )[1](out_ct)
    out_grads = (
        (local_grads[0].astype(jnp.float32) + carry_grads[0].astype(jnp.float32)),
        (local_grads[1].astype(jnp.float32) + carry_grads[1].astype(jnp.float32)),
        local_grads[2] + carry_grads[2],
        local_grads[3] + carry_grads[3],
        local_grads[4] + carry_grads[4],
        local_grads[5],
    )
    decay_grad = jnp.sum(adjoint_flat * incoming_flat, axis=1)
    sum_grads = summary_pull((decay_grad, adjoint_flat.reshape(state_shape)))
    mixer_grad = (out_grads[1].astype(jnp.float32) + sum_grads[1].astype(jnp.float32)).astype(
        jnp.bfloat16
    )
    other_grad = swap_heads(mixer_grad)
    mixer_full = jnp.where(
        group == 0,
        jnp.concatenate([mixer_grad, other_grad], axis=1),
        jnp.concatenate([other_grad, mixer_grad], axis=1),
    )
    mixer_slots = roll_blocks(mixer_full, pairs - 1 - pair, pairs, 1)
    mixer_slots = mixer_slots.reshape(tokens, pairs, -1)[:, ::-1].reshape(tokens, -1)
    back_proj = jnp.dot(mixer_slots, slot_weight, preferred_element_type=jnp.float32)
    value_grad = (out_grads[0].astype(jnp.float32) + sum_grads[0].astype(jnp.float32)).reshape(
        tokens, channels_here
    ) + back_proj
    value_grad = value_grad.astype(jnp.bfloat16)
    prev_part = shifted(value_grad.reshape(1, tokens, channels_here), "section", -1)
    dest_grad = roll_blocks(mixer_full, pairs - pair, pairs, 1)
    row_parts = lax.dot_general(
        dest_grad, bwd_flat, (((0,), (0,)), ((), ())), preferred_element_type=jnp.float32
    ).reshape(pairs, -1, channels_here)
    small = jnp.concatenate(
        [
            (out_grads[2] + sum_grads[2]).reshape(channels_here),
            out_grads[3] + sum_grads[3],
            out_grads[4] + sum_grads[4],
            out_grads[5],
        ]
    )
    small_rows = -(-small.shape[0] // channels_here)
    small = jnp.pad(small, (0, small_rows * channels_here - small.shape[0]))
    small = small.reshape(small_rows, channels_here)
    small_high = small.astype(jnp.bfloat16)
    small_low = (small - small_high.astype(jnp.float32)).astype(jnp.bfloat16)
    small_coded = jnp.concatenate([small_high, small_low], axis=0)
    block_rows = row_parts.shape[1]
    pair_sum = row_parts[0]
    small_slots = [small_coded]
    for k in range(1, pairs):
        message = jnp.concatenate([row_parts[k].astype(jnp.bfloat16), small_coded], axis=0)
        got = rotated(message, "seq", 2 * k)
        pair_sum = pair_sum + got[:block_rows].astype(jnp.float32)
        small_slots.append(got[block_rows:])
    small_slots = jnp.stack(small_slots[::-1])
    small_slots = roll_blocks(small_slots, pair + 1, pairs, 0).astype(jnp.float32)
    small_parts = small_slots[:, :small_rows] + small_slots[:, small_rows:]
    side_total = small_parts[0]
    for j in range(1, pairs):
        side_total = side_total + small_parts[j]
    side_high = side_total.astype(jnp.bfloat16)
    side_low = (side_total - side_high.astype(jnp.float32)).astype(jnp.bfloat16)
    half_rows = block_rows // 2
    mine_rows = lax.dynamic_slice_in_dim(pair_sum, parity * half_rows, half_rows, axis=0)
    other_rows = lax.dynamic_slice_in_dim(pair_sum, (1 - parity) * half_rows, half_rows, axis=0)
    message = jnp.concatenate([other_rows.astype(jnp.bfloat16), side_high, side_low], axis=0)
    got = lax.ppermute(message, "seq", [(i, i ^ 1) for i in range(size)])
    grad_rows = mine_rows + got[:half_rows].astype(jnp.float32)
    own_side = side_high.astype(jnp.float32) + side_low.astype(jnp.float32)
    got_side = got[half_rows:].astype(jnp.float32)
    got_side = got_side[:small_rows] + got_side[small_rows:]
    small_total = jnp.where(parity == 0, own_side + got_side, got_side + own_side)
    small = small_total.reshape(-1)
    totals = (
        small[:channels_here],
        small[channels_here : channels_here + heads_here],
        small[channels_here + heads_here : channels_here + 2 * heads_here],
        small[channels_here + 2 * heads_here : channels_here + 3 * heads_here],
    )
    return (
        prev_part,
        grad_rows[None],
        totals[0][None],
        totals[1][None],
        totals[2][None],
        totals[3][None],
    )


def solution(mesh):
    in_specs = (
        P("section", "seq", "head"),
        P("section", "seq"),
        P("section", "seq", "head"),
        P("section", "seq", "head"),
        P("section", "head"),
        P("section", "head"),
        P("section", "head"),
        P("section", "head"),
    )
    out_specs = (
        P("section", "seq", "head"),
        P("section", "seq", "head"),
        P("section", "head"),
        P("section", "head"),
        P("section", "head"),
        P("section", "head"),
    )
    return jax.shard_map(shards, mesh=mesh, in_specs=in_specs, out_specs=out_specs, check_vma=False)
```

```python
import jax
import jax.numpy as jnp
from jax import lax
from jax.sharding import PartitionSpec as P

EXACT = lax.Precision.HIGHEST


def shifted(block, axis, distance):
    devices = range(lax.axis_size(axis))
    route = [(i - distance, i) for i in devices if i - distance in devices]
    return lax.ppermute(block, axis, route)


def rotated(block, axis, distance):
    size = lax.axis_size(axis)
    route = [(i, (i + distance) % size) for i in range(size)]
    return lax.ppermute(block, axis, route)


def roll_blocks(value, shift, parts, dim):
    doubled = jnp.concatenate([value, value], axis=dim)
    width = value.shape[dim] // parts
    start = ((parts - shift) % parts) * width
    return lax.dynamic_slice_in_dim(doubled, start, value.shape[dim], axis=dim)


def swap_heads(block):
    return lax.ppermute(block, "head", [(0, 1), (1, 0)])


def contract(spec, left, right):
    return jnp.einsum(spec, left, right, preferred_element_type=jnp.float32)


def local_setup(values, step_weight, step_bias, rate_log):
    tokens = values.shape[0]
    raw_step = (
        jnp.einsum("thp,hp->th", values.astype(jnp.float32), step_weight, precision=EXACT)
        + step_bias[None, :]
    )
    step_size = jax.nn.softplus(raw_step)
    decay_log = -jnp.exp(rate_log)[None, :] * step_size
    row_ids = lax.broadcasted_iota(jnp.int32, (tokens, tokens), 0)
    col_ids = lax.broadcasted_iota(jnp.int32, (tokens, tokens), 1)
    triangle = (row_ids >= col_ids).astype(jnp.float32)
    cumulative = jnp.dot(triangle, decay_log, precision=EXACT)
    return (step_size, cumulative, row_ids, col_ids)


def span_summary(values, mixer, step_weight, step_bias, rate_log, docs, doc_before):
    step_size, cumulative, row_ids, col_ids = local_setup(values, step_weight, step_bias, rate_log)
    final_log = cumulative[-1]
    tail_mask = (docs == docs[-1]).astype(jnp.float32)[:, None]
    tail_weight = (
        jnp.exp(jnp.where(tail_mask > 0, final_log[None, :] - cumulative, 0.0))
        * tail_mask
        * step_size
    )
    unbroken = (docs[-1] == doc_before).astype(jnp.float32)
    carry_decay = jnp.exp(final_log) * unbroken
    half_width = mixer.shape[1] // 2
    writers = mixer[:, :half_width]
    weighted = (tail_weight[:, :, None] * writers.astype(jnp.float32)[:, None, :]).astype(
        jnp.bfloat16
    )
    span_state = contract("thn,thp->hnp", weighted, values)
    return (carry_decay, span_state)


def span_local(values, mixer, step_weight, step_bias, rate_log, skip_gain, docs):
    step_size, cumulative, row_ids, col_ids = local_setup(values, step_weight, step_bias, rate_log)
    half_width = mixer.shape[1] // 2
    writers = mixer[:, :half_width]
    readers = mixer[:, half_width:]
    affinity = jnp.dot(readers, writers.T, preferred_element_type=jnp.float32)
    same_doc = ((docs[:, None] == docs[None, :]) & (row_ids >= col_ids)).astype(jnp.float32)
    heads_first = cumulative.T
    log_gap = heads_first[:, :, None] - heads_first[:, None, :]
    mixing = (
        jnp.exp(jnp.where(same_doc[None] > 0, log_gap, 0.0))
        * same_doc[None]
        * affinity[None]
        * step_size.T[:, None, :]
    )
    mixing = mixing.astype(jnp.bfloat16)
    local_part = contract("hts,shp->thp", mixing, values)
    return values.astype(jnp.float32) * (1.0 + skip_gain)[None, :, None] + local_part


def span_carry(values, mixer, step_weight, step_bias, rate_log, docs, doc_before, incoming):
    step_size, cumulative, row_ids, col_ids = local_setup(values, step_weight, step_bias, rate_log)
    half_width = mixer.shape[1] // 2
    readers = mixer[:, half_width:]
    unbroken = (docs == doc_before).astype(jnp.float32)
    carry_scale = jnp.exp(cumulative) * unbroken[:, None]
    carried = jnp.einsum("tn,hnp->thp", readers.astype(jnp.float32), incoming, precision=EXACT)
    return carry_scale[:, :, None] * carried


def scan_rounds(decay, state, axis, forward):
    size, mine = (lax.axis_size(axis), lax.axis_index(axis))
    far_decay, far_state = (decay, state)
    near_decay = jnp.ones_like(decay)
    near_state = jnp.zeros_like(state)
    distance = 1
    while distance < size:
        got_decay, got_state = shifted(
            (far_decay, far_state.astype(jnp.bfloat16)), axis, distance if forward else -distance
        )
        got_state = got_state.astype(jnp.float32)
        near_state = near_state + near_decay[:, None] * got_state
        near_decay = near_decay * got_decay
        if distance * 2 < size:
            far_state = far_state + far_decay[:, None] * got_state
            far_decay = far_decay * got_decay
        distance *= 2
    return near_state


def scan_message(part, distance, size, upper):
    width = part["fwd"].shape[1]
    high = lax.convert_element_type(part["decay"].astype(jnp.bfloat16), jnp.float32)
    low = part["decay"] - high
    pad = jnp.zeros((high.shape[0], 126), jnp.float32)
    tail = jnp.concatenate([high[:, None], low[:, None], pad], axis=1)
    if distance * 2 < size:
        body = [part["fwd"], part["bwd"]]
    else:
        body = [jnp.where(upper, part["bwd"], part["fwd"])]
    return jnp.concatenate(body + [tail], axis=1).astype(jnp.bfloat16)


def scan_absorb(part, got, distance, size, upper):
    width = part["fwd"].shape[1]
    got = got.astype(jnp.float32)
    got_fwd = got[:, :width]
    if distance * 2 < size:
        got_bwd = got[:, width : 2 * width]
        at = 2 * width
    else:
        got_bwd = got_fwd
        at = width
    got_decay = got[:, at] + got[:, at + 1]
    new = dict(part)
    new["before"] = jnp.where(upper, part["before"] + part["before_decay"][:, None] * got_fwd, part["before"])
    new["before_decay"] = jnp.where(upper, part["before_decay"] * got_decay, part["before_decay"])
    new["after"] = jnp.where(upper, part["after"], part["after"] + part["after_decay"][:, None] * got_bwd)
    new["after_decay"] = jnp.where(upper, part["after_decay"], part["after_decay"] * got_decay)
    if distance * 2 < size:
        new["fwd"] = jnp.where(
            upper,
            part["fwd"] + part["decay"][:, None] * got_fwd,
            got_fwd + got_decay[:, None] * part["fwd"],
        )
        new["bwd"] = jnp.where(
            upper,
            got_bwd + got_decay[:, None] * part["bwd"],
            part["bwd"] + part["decay"][:, None] * got_bwd,
        )
        new["decay"] = part["decay"] * got_decay
    return new


def both_scans(decay, state, state_grad, axis, filler_fn, filler_args, chunks=2):
    size, mine = (lax.axis_size(axis), lax.axis_index(axis))
    if size & (size - 1):
        return (
            scan_rounds(decay, state, axis, True),
            scan_rounds(decay, state_grad, axis, False),
            filler_fn(*filler_args),
        )
    heads = decay.shape[0]
    if heads % chunks:
        chunks = 1
    step_heads = heads // chunks
    parts = []
    for c in range(chunks):
        cut = slice(c * step_heads, (c + 1) * step_heads)
        parts.append(
            {
                "decay": decay[cut],
                "fwd": state[cut],
                "bwd": state_grad[cut],
                "before": jnp.zeros_like(state[cut]),
                "before_decay": jnp.ones_like(decay[cut]),
                "after": jnp.zeros_like(state_grad[cut]),
                "after_decay": jnp.ones_like(decay[cut]),
            }
        )
    rounds = size.bit_length() - 1
    filler = None
    for step in range(rounds + chunks - 1):
        active = [c for c in range(chunks) if 0 <= step - c < rounds]
        messages = []
        for c in active:
            distance = 2 ** (step - c)
            upper = (mine // distance) % 2 == 1
            messages.append(scan_message(parts[c], distance, size, upper))
        if step == 0:
            messages, filler_args = lax.optimization_barrier((messages, filler_args))
        gots = []
        for c, message in zip(active, messages):
            distance = 2 ** (step - c)
            gots.append(lax.ppermute(message, axis, [(i, i ^ distance) for i in range(size)]))
        if step == 0:
            gots, filler = lax.optimization_barrier((gots, filler_fn(*filler_args)))
        elif len(gots) > 1:
            gots = lax.optimization_barrier(gots)
        for c, got in zip(active, gots):
            distance = 2 ** (step - c)
            upper = (mine // distance) % 2 == 1
            parts[c] = scan_absorb(parts[c], got, distance, size, upper)
    before = jnp.concatenate([p["before"] for p in parts], axis=0)
    after = jnp.concatenate([p["after"] for p in parts], axis=0)
    return (before, after, filler)


def shards(bwd_input, bwd_docs, bwd_grad, proj_weight, step_weight, step_bias, rate_log, skip_gain):
    tokens = bwd_input.shape[1]
    channels_here = bwd_input.shape[2]
    heads_here = step_bias.shape[1]
    head_width = channels_here // heads_here
    bwd_flat = bwd_input[0]
    bwd_values = bwd_flat.reshape(tokens, heads_here, head_width)
    weight_heads = step_weight[0].reshape(heads_here, head_width)
    bias_heads = step_bias[0]
    rate_heads = rate_log[0]
    skip_heads = skip_gain[0]
    docs_bwd = bwd_docs[0]
    doc_before = shifted(docs_bwd[-1:], "seq", 1)[0]
    size, mine = (lax.axis_size("seq"), lax.axis_index("seq"))
    group = lax.axis_index("head")
    own_rows = proj_weight[0]
    slot_weight = jnp.concatenate(
        [own_rows] + [rotated(own_rows, "seq", k) for k in range(1, size)], axis=0
    )
    slot_value = jnp.dot(bwd_flat, slot_weight.T, preferred_element_type=jnp.float32)
    slot_value = slot_value.reshape(tokens, size, -1)[:, ::-1].reshape(tokens, -1)
    partial_value = roll_blocks(slot_value, mine + 1, size, 1)
    group_width = partial_value.shape[1] // 2
    mine_part = lax.dynamic_slice_in_dim(partial_value, group * group_width, group_width, axis=1)
    other_part = lax.dynamic_slice_in_dim(
        partial_value, (1 - group) * group_width, group_width, axis=1
    )
    mixer_bwd = (
        mine_part + swap_heads(other_part.astype(jnp.bfloat16)).astype(jnp.float32)
    ).astype(jnp.bfloat16)
    cotangent = bwd_grad[0].reshape(tokens, heads_here, head_width)

    def summary_bwd(values_in, mixer_in, weight_in, bias_in, rate_in):
        return span_summary(values_in, mixer_in, weight_in, bias_in, rate_in, docs_bwd, doc_before)

    summary_out, summary_pull = jax.vjp(
        summary_bwd, bwd_values, mixer_bwd, weight_heads, bias_heads, rate_heads
    )
    decay_bwd, state_bwd = summary_out
    state_shape = state_bwd.shape
    state_flat = state_bwd.reshape(heads_here, -1)

    out_ct = cotangent.astype(jnp.float32)

    def local_bwd(values_in, mixer_in, weight_in, bias_in, rate_in, skip_in):
        return span_local(values_in, mixer_in, weight_in, bias_in, rate_in, skip_in, docs_bwd)

    def local_pull(*primals):
        return jax.vjp(local_bwd, *primals[:-1])[1](primals[-1])


    def carry_bwd(values_in, mixer_in, weight_in, bias_in, rate_in, state_in):
        return span_carry(
            values_in, mixer_in, weight_in, bias_in, rate_in, docs_bwd, doc_before, state_in
        )

    def carried_only(state_in):
        return carry_bwd(bwd_values, mixer_bwd, weight_heads, bias_heads, rate_heads, state_in)

    state_grad = jax.vjp(carried_only, jnp.zeros(state_shape, jnp.float32))[1](out_ct)[0]
    state_grad = state_grad.reshape(heads_here, -1)
    incoming_flat, adjoint_flat, local_grads = both_scans(
        decay_bwd,
        state_flat,
        state_grad,
        "seq",
        local_pull,
        (bwd_values, mixer_bwd, weight_heads, bias_heads, rate_heads, skip_heads, out_ct),
    )
    incoming_bwd = incoming_flat.reshape(state_shape)
    carry_grads = jax.vjp(
        carry_bwd, bwd_values, mixer_bwd, weight_heads, bias_heads, rate_heads, incoming_bwd
    )[1](out_ct)
    out_grads = (
        (local_grads[0].astype(jnp.float32) + carry_grads[0].astype(jnp.float32)),
        (local_grads[1].astype(jnp.float32) + carry_grads[1].astype(jnp.float32)),
        local_grads[2] + carry_grads[2],
        local_grads[3] + carry_grads[3],
        local_grads[4] + carry_grads[4],
        local_grads[5],
    )
    decay_grad = jnp.sum(adjoint_flat * incoming_flat, axis=1)
    sum_grads = summary_pull((decay_grad, adjoint_flat.reshape(state_shape)))
    mixer_grad = (out_grads[1].astype(jnp.float32) + sum_grads[1].astype(jnp.float32)).astype(
        jnp.bfloat16
    )
    other_grad = swap_heads(mixer_grad)
    mixer_full = jnp.where(
        group == 0,
        jnp.concatenate([mixer_grad, other_grad], axis=1),
        jnp.concatenate([other_grad, mixer_grad], axis=1),
    )
    mixer_slots = roll_blocks(mixer_full, size - 1 - mine, size, 1)
    mixer_slots = mixer_slots.reshape(tokens, size, -1)[:, ::-1].reshape(tokens, -1)
    back_proj = jnp.dot(mixer_slots, slot_weight, preferred_element_type=jnp.float32)
    value_grad = (out_grads[0].astype(jnp.float32) + sum_grads[0].astype(jnp.float32)).reshape(
        tokens, channels_here
    ) + back_proj
    value_grad = value_grad.astype(jnp.bfloat16)
    prev_part = shifted(value_grad.reshape(1, tokens, channels_here), "section", -1)
    dest_grad = roll_blocks(mixer_full, size - mine, size, 1)
    row_parts = lax.dot_general(
        dest_grad, bwd_flat, (((0,), (0,)), ((), ())), preferred_element_type=jnp.float32
    ).reshape(size, -1, channels_here)
    small = jnp.concatenate(
        [
            (out_grads[2] + sum_grads[2]).reshape(channels_here),
            out_grads[3] + sum_grads[3],
            out_grads[4] + sum_grads[4],
            out_grads[5],
        ]
    )
    small_rows = -(-small.shape[0] // channels_here)
    small = jnp.pad(small, (0, small_rows * channels_here - small.shape[0]))
    small = small.reshape(small_rows, channels_here)
    small_high = small.astype(jnp.bfloat16)
    small_low = (small - small_high.astype(jnp.float32)).astype(jnp.bfloat16)
    small_coded = jnp.concatenate([small_high, small_low], axis=0)
    block_rows = row_parts.shape[1]
    grad_rows = row_parts[0]
    small_slots = [small_coded]
    for k in range(1, size):
        message = jnp.concatenate([row_parts[k].astype(jnp.bfloat16), small_coded], axis=0)
        got = rotated(message, "seq", k)
        grad_rows = grad_rows + got[:block_rows].astype(jnp.float32)
        small_slots.append(got[block_rows:])
    small_slots = jnp.stack(small_slots[::-1])
    small_slots = roll_blocks(small_slots, mine + 1, size, 0).astype(jnp.float32)
    small_parts = small_slots[:, :small_rows] + small_slots[:, small_rows:]
    small_total = small_parts[0]
    for j in range(1, size):
        small_total = small_total + small_parts[j]
    small = small_total.reshape(-1)
    totals = (
        small[:channels_here],
        small[channels_here : channels_here + heads_here],
        small[channels_here + heads_here : channels_here + 2 * heads_here],
        small[channels_here + 2 * heads_here : channels_here + 3 * heads_here],
    )
    return (
        prev_part,
        grad_rows[None],
        totals[0][None],
        totals[1][None],
        totals[2][None],
        totals[3][None],
    )


def solution(mesh):
    in_specs = (
        P("section", "seq", "head"),
        P("section", "seq"),
        P("section", "seq", "head"),
        P("section", "seq", "head"),
        P("section", "head"),
        P("section", "head"),
        P("section", "head"),
        P("section", "head"),
    )
    out_specs = (
        P("section", "seq", "head"),
        P("section", "seq", "head"),
        P("section", "head"),
        P("section", "head"),
        P("section", "head"),
        P("section", "head"),
    )
    return jax.shard_map(shards, mesh=mesh, in_specs=in_specs, out_specs=out_specs, check_vma=False)
```

```python
import jax
import jax.numpy as jnp
from jax import lax
from jax.sharding import PartitionSpec as P

EXACT = lax.Precision.HIGHEST


def shifted(block, axis, distance):
    devices = range(lax.axis_size(axis))
    route = [(i - distance, i) for i in devices if i - distance in devices]
    return lax.ppermute(block, axis, route)


def rotated(block, axis, distance):
    size = lax.axis_size(axis)
    route = [(i, (i + distance) % size) for i in range(size)]
    return lax.ppermute(block, axis, route)


def roll_blocks(value, shift, parts, dim):
    doubled = jnp.concatenate([value, value], axis=dim)
    width = value.shape[dim] // parts
    start = ((parts - shift) % parts) * width
    return lax.dynamic_slice_in_dim(doubled, start, value.shape[dim], axis=dim)


def swap_heads(block):
    return lax.ppermute(block, "head", [(0, 1), (1, 0)])


def contract(spec, left, right):
    return jnp.einsum(spec, left, right, preferred_element_type=jnp.float32)


def local_setup(values, step_weight, step_bias, rate_log):
    tokens = values.shape[0]
    raw_step = (
        jnp.einsum("thp,hp->th", values.astype(jnp.float32), step_weight, precision=EXACT)
        + step_bias[None, :]
    )
    step_size = jax.nn.softplus(raw_step)
    decay_log = -jnp.exp(rate_log)[None, :] * step_size
    row_ids = lax.broadcasted_iota(jnp.int32, (tokens, tokens), 0)
    col_ids = lax.broadcasted_iota(jnp.int32, (tokens, tokens), 1)
    triangle = (row_ids >= col_ids).astype(jnp.float32)
    cumulative = jnp.dot(triangle, decay_log, precision=EXACT)
    return (step_size, cumulative, row_ids, col_ids)


def span_summary(values, mixer, step_weight, step_bias, rate_log, docs, doc_before):
    step_size, cumulative, row_ids, col_ids = local_setup(values, step_weight, step_bias, rate_log)
    final_log = cumulative[-1]
    tail_mask = (docs == docs[-1]).astype(jnp.float32)[:, None]
    tail_weight = (
        jnp.exp(jnp.where(tail_mask > 0, final_log[None, :] - cumulative, 0.0))
        * tail_mask
        * step_size
    )
    unbroken = (docs[-1] == doc_before).astype(jnp.float32)
    carry_decay = jnp.exp(final_log) * unbroken
    half_width = mixer.shape[1] // 2
    writers = mixer[:, :half_width]
    weighted = (tail_weight[:, :, None] * writers.astype(jnp.float32)[:, None, :]).astype(
        jnp.bfloat16
    )
    span_state = contract("thn,thp->hnp", weighted, values)
    return (carry_decay, span_state)


def span_local(values, mixer, step_weight, step_bias, rate_log, skip_gain, docs):
    step_size, cumulative, row_ids, col_ids = local_setup(values, step_weight, step_bias, rate_log)
    half_width = mixer.shape[1] // 2
    writers = mixer[:, :half_width]
    readers = mixer[:, half_width:]
    affinity = jnp.dot(readers, writers.T, preferred_element_type=jnp.float32)
    same_doc = ((docs[:, None] == docs[None, :]) & (row_ids >= col_ids)).astype(jnp.float32)
    heads_first = cumulative.T
    log_gap = heads_first[:, :, None] - heads_first[:, None, :]
    mixing = (
        jnp.exp(jnp.where(same_doc[None] > 0, log_gap, 0.0))
        * same_doc[None]
        * affinity[None]
        * step_size.T[:, None, :]
    )
    mixing = mixing.astype(jnp.bfloat16)
    local_part = contract("hts,shp->thp", mixing, values)
    return values.astype(jnp.float32) * (1.0 + skip_gain)[None, :, None] + local_part


def span_carry(values, mixer, step_weight, step_bias, rate_log, docs, doc_before, incoming):
    step_size, cumulative, row_ids, col_ids = local_setup(values, step_weight, step_bias, rate_log)
    half_width = mixer.shape[1] // 2
    readers = mixer[:, half_width:]
    unbroken = (docs == doc_before).astype(jnp.float32)
    carry_scale = jnp.exp(cumulative) * unbroken[:, None]
    carried = jnp.einsum("tn,hnp->thp", readers.astype(jnp.float32), incoming, precision=EXACT)
    return carry_scale[:, :, None] * carried


def scan_rounds(decay, state, axis, forward):
    size, mine = (lax.axis_size(axis), lax.axis_index(axis))
    far_decay, far_state = (decay, state)
    near_decay = jnp.ones_like(decay)
    near_state = jnp.zeros_like(state)
    distance = 1
    while distance < size:
        got_decay, got_state = shifted(
            (far_decay, far_state.astype(jnp.bfloat16)), axis, distance if forward else -distance
        )
        got_state = got_state.astype(jnp.float32)
        near_state = near_state + near_decay[:, None] * got_state
        near_decay = near_decay * got_decay
        if distance * 2 < size:
            far_state = far_state + far_decay[:, None] * got_state
            far_decay = far_decay * got_decay
        distance *= 2
    return near_state


def both_scans(decay, state, state_grad, axis, filler_fn, filler_args):
    size, mine = (lax.axis_size(axis), lax.axis_index(axis))
    if size & (size - 1):
        return (
            scan_rounds(decay, state, axis, True),
            scan_rounds(decay, state_grad, axis, False),
            filler_fn(*filler_args),
        )
    width = state.shape[1]
    total_decay = decay
    total_fwd, total_bwd = (state, state_grad)
    before = jnp.zeros_like(state)
    before_decay = jnp.ones_like(decay)
    after = jnp.zeros_like(state_grad)
    after_decay = jnp.ones_like(decay)
    distance = 1
    while distance < size:
        high = lax.convert_element_type(total_decay.astype(jnp.bfloat16), jnp.float32)
        low = total_decay - high
        pad = jnp.zeros((decay.shape[0], 126), jnp.float32)
        payload = jnp.concatenate(
            [total_fwd, total_bwd, high[:, None], low[:, None], pad], axis=1
        ).astype(jnp.bfloat16)
        upper = (mine // distance) % 2 == 1
        if distance == 1:
            payload, filler_args = lax.optimization_barrier((payload, filler_args))
        if distance * 2 < size:
            got = lax.ppermute(payload, axis, [(i, i ^ distance) for i in range(size)])
            got = got.astype(jnp.float32)
            got_fwd = got[:, :width]
            got_bwd = got[:, width : 2 * width]
        else:
            last = jnp.where(upper, total_bwd, total_fwd).astype(jnp.bfloat16)
            last = jnp.concatenate([last, payload[:, 2 * width :]], axis=1)
            got = lax.ppermute(last, axis, [(i, i ^ distance) for i in range(size)])
            got = got.astype(jnp.float32)
            got_fwd = got[:, :width]
            got_bwd = got_fwd
            got = jnp.concatenate([got[:, :width], got], axis=1)
        if distance == 1:
            got, filler = lax.optimization_barrier((got, filler_fn(*filler_args)))
        got_decay = got[:, 2 * width] + got[:, 2 * width + 1]
        before = jnp.where(upper, before + before_decay[:, None] * got_fwd, before)
        before_decay = jnp.where(upper, before_decay * got_decay, before_decay)
        after = jnp.where(upper, after, after + after_decay[:, None] * got_bwd)
        after_decay = jnp.where(upper, after_decay, after_decay * got_decay)
        if distance * 2 < size:
            total_fwd = jnp.where(
                upper,
                total_fwd + total_decay[:, None] * got_fwd,
                got_fwd + got_decay[:, None] * total_fwd,
            )
            total_bwd = jnp.where(
                upper,
                got_bwd + got_decay[:, None] * total_bwd,
                total_bwd + total_decay[:, None] * got_bwd,
            )
            total_decay = total_decay * got_decay
        distance *= 2
    return (before, after, filler)


def shards(bwd_input, bwd_docs, bwd_grad, proj_weight, step_weight, step_bias, rate_log, skip_gain):
    tokens = bwd_input.shape[1]
    channels_here = bwd_input.shape[2]
    heads_here = step_bias.shape[1]
    head_width = channels_here // heads_here
    bwd_flat = bwd_input[0]
    bwd_values = bwd_flat.reshape(tokens, heads_here, head_width)
    weight_heads = step_weight[0].reshape(heads_here, head_width)
    bias_heads = step_bias[0]
    rate_heads = rate_log[0]
    skip_heads = skip_gain[0]
    docs_bwd = bwd_docs[0]
    size, mine = (lax.axis_size("seq"), lax.axis_index("seq"))
    group = lax.axis_index("head")
    own_rows = proj_weight[0]
    last_doc = docs_bwd[-1]
    doc_digits = jnp.stack([last_doc // 256, last_doc % 256]).astype(jnp.bfloat16)
    doc_column = jnp.zeros((own_rows.shape[0], 128), jnp.bfloat16)
    doc_column = doc_column.at[:2, 0].set(doc_digits)
    first = rotated(jnp.concatenate([own_rows, doc_column], axis=1), "seq", 1)
    got_digits = first[:2, own_rows.shape[1]].astype(jnp.int32)
    doc_before = jnp.where(mine == 0, 0, got_digits[0] * 256 + got_digits[1])
    slot_weight = jnp.concatenate(
        [own_rows, first[:, : own_rows.shape[1]]]
        + [rotated(own_rows, "seq", k) for k in range(2, size)],
        axis=0,
    )
    slot_value = jnp.dot(bwd_flat, slot_weight.T, preferred_element_type=jnp.float32)
    slot_value = slot_value.reshape(tokens, size, -1)[:, ::-1].reshape(tokens, -1)
    partial_value = roll_blocks(slot_value, mine + 1, size, 1)
    group_width = partial_value.shape[1] // 2
    mine_part = lax.dynamic_slice_in_dim(partial_value, group * group_width, group_width, axis=1)
    other_part = lax.dynamic_slice_in_dim(
        partial_value, (1 - group) * group_width, group_width, axis=1
    )
    mixer_bwd = (
        mine_part + swap_heads(other_part.astype(jnp.bfloat16)).astype(jnp.float32)
    ).astype(jnp.bfloat16)
    cotangent = bwd_grad[0].reshape(tokens, heads_here, head_width)

    def summary_bwd(values_in, mixer_in, weight_in, bias_in, rate_in):
        return span_summary(values_in, mixer_in, weight_in, bias_in, rate_in, docs_bwd, doc_before)

    summary_out, summary_pull = jax.vjp(
        summary_bwd, bwd_values, mixer_bwd, weight_heads, bias_heads, rate_heads
    )
    decay_bwd, state_bwd = summary_out
    state_shape = state_bwd.shape
    state_flat = state_bwd.reshape(heads_here, -1)

    out_ct = cotangent.astype(jnp.float32)

    def local_bwd(values_in, mixer_in, weight_in, bias_in, rate_in, skip_in):
        return span_local(values_in, mixer_in, weight_in, bias_in, rate_in, skip_in, docs_bwd)

    def local_pull(*primals):
        return jax.vjp(local_bwd, *primals[:-1])[1](primals[-1])


    def carry_bwd(values_in, mixer_in, weight_in, bias_in, rate_in, state_in):
        return span_carry(
            values_in, mixer_in, weight_in, bias_in, rate_in, docs_bwd, doc_before, state_in
        )

    def carried_only(state_in):
        return carry_bwd(bwd_values, mixer_bwd, weight_heads, bias_heads, rate_heads, state_in)

    state_grad = jax.vjp(carried_only, jnp.zeros(state_shape, jnp.float32))[1](out_ct)[0]
    state_grad = state_grad.reshape(heads_here, -1)
    incoming_flat, adjoint_flat, local_grads = both_scans(
        decay_bwd,
        state_flat,
        state_grad,
        "seq",
        local_pull,
        (bwd_values, mixer_bwd, weight_heads, bias_heads, rate_heads, skip_heads, out_ct),
    )
    incoming_bwd = incoming_flat.reshape(state_shape)
    carry_grads = jax.vjp(
        carry_bwd, bwd_values, mixer_bwd, weight_heads, bias_heads, rate_heads, incoming_bwd
    )[1](out_ct)
    out_grads = (
        (local_grads[0].astype(jnp.float32) + carry_grads[0].astype(jnp.float32)),
        (local_grads[1].astype(jnp.float32) + carry_grads[1].astype(jnp.float32)),
        local_grads[2] + carry_grads[2],
        local_grads[3] + carry_grads[3],
        local_grads[4] + carry_grads[4],
        local_grads[5],
    )
    decay_grad = jnp.sum(adjoint_flat * incoming_flat, axis=1)
    sum_grads = summary_pull((decay_grad, adjoint_flat.reshape(state_shape)))
    mixer_grad = (out_grads[1].astype(jnp.float32) + sum_grads[1].astype(jnp.float32)).astype(
        jnp.bfloat16
    )
    other_grad = swap_heads(mixer_grad)
    mixer_full = jnp.where(
        group == 0,
        jnp.concatenate([mixer_grad, other_grad], axis=1),
        jnp.concatenate([other_grad, mixer_grad], axis=1),
    )
    mixer_slots = roll_blocks(mixer_full, size - 1 - mine, size, 1)
    mixer_slots = mixer_slots.reshape(tokens, size, -1)[:, ::-1].reshape(tokens, -1)
    back_proj = jnp.dot(mixer_slots, slot_weight, preferred_element_type=jnp.float32)
    value_grad = (out_grads[0].astype(jnp.float32) + sum_grads[0].astype(jnp.float32)).reshape(
        tokens, channels_here
    ) + back_proj
    value_grad = value_grad.astype(jnp.bfloat16)
    prev_part = shifted(value_grad.reshape(1, tokens, channels_here), "section", -1)
    dest_grad = roll_blocks(mixer_full, size - mine, size, 1)
    row_parts = lax.dot_general(
        dest_grad, bwd_flat, (((0,), (0,)), ((), ())), preferred_element_type=jnp.float32
    ).reshape(size, -1, channels_here)
    small = jnp.concatenate(
        [
            (out_grads[2] + sum_grads[2]).reshape(channels_here),
            out_grads[3] + sum_grads[3],
            out_grads[4] + sum_grads[4],
            out_grads[5],
        ]
    )
    small_rows = -(-small.shape[0] // channels_here)
    small = jnp.pad(small, (0, small_rows * channels_here - small.shape[0]))
    small = small.reshape(small_rows, channels_here)
    small_high = small.astype(jnp.bfloat16)
    small_low = (small - small_high.astype(jnp.float32)).astype(jnp.bfloat16)
    small_coded = jnp.concatenate([small_high, small_low], axis=0)
    block_rows = row_parts.shape[1]
    grad_rows = row_parts[0]
    small_slots = [small_coded]
    for k in range(1, size):
        message = jnp.concatenate([row_parts[k].astype(jnp.bfloat16), small_coded], axis=0)
        got = rotated(message, "seq", k)
        grad_rows = grad_rows + got[:block_rows].astype(jnp.float32)
        small_slots.append(got[block_rows:])
    small_slots = jnp.stack(small_slots[::-1])
    small_slots = roll_blocks(small_slots, mine + 1, size, 0).astype(jnp.float32)
    small_parts = small_slots[:, :small_rows] + small_slots[:, small_rows:]
    small_total = small_parts[0]
    for j in range(1, size):
        small_total = small_total + small_parts[j]
    small = small_total.reshape(-1)
    totals = (
        small[:channels_here],
        small[channels_here : channels_here + heads_here],
        small[channels_here + heads_here : channels_here + 2 * heads_here],
        small[channels_here + 2 * heads_here : channels_here + 3 * heads_here],
    )
    return (
        prev_part,
        grad_rows[None],
        totals[0][None],
        totals[1][None],
        totals[2][None],
        totals[3][None],
    )


def solution(mesh):
    in_specs = (
        P("section", "seq", "head"),
        P("section", "seq"),
        P("section", "seq", "head"),
        P("section", "seq", "head"),
        P("section", "head"),
        P("section", "head"),
        P("section", "head"),
        P("section", "head"),
    )
    out_specs = (
        P("section", "seq", "head"),
        P("section", "seq", "head"),
        P("section", "head"),
        P("section", "head"),
        P("section", "head"),
        P("section", "head"),
    )
    return jax.shard_map(shards, mesh=mesh, in_specs=in_specs, out_specs=out_specs, check_vma=False)
```

```python
import jax
import jax.numpy as jnp
from jax import lax
from jax.sharding import PartitionSpec as P

EXACT = lax.Precision.HIGHEST


def shifted(block, axis, distance):
    devices = range(lax.axis_size(axis))
    route = [(i - distance, i) for i in devices if i - distance in devices]
    return lax.ppermute(block, axis, route)


def rotated(block, axis, distance):
    size = lax.axis_size(axis)
    route = [(i, (i + distance) % size) for i in range(size)]
    return lax.ppermute(block, axis, route)


def roll_blocks(value, shift, parts, dim):
    doubled = jnp.concatenate([value, value], axis=dim)
    width = value.shape[dim] // parts
    start = ((parts - shift) % parts) * width
    return lax.dynamic_slice_in_dim(doubled, start, value.shape[dim], axis=dim)


def swap_heads(block):
    return lax.ppermute(block, "head", [(0, 1), (1, 0)])


def contract(spec, left, right):
    return jnp.einsum(spec, left, right, preferred_element_type=jnp.float32)


def local_setup(values, step_weight, step_bias, rate_log):
    tokens = values.shape[0]
    raw_step = (
        jnp.einsum("thp,hp->th", values.astype(jnp.float32), step_weight, precision=EXACT)
        + step_bias[None, :]
    )
    step_size = jax.nn.softplus(raw_step)
    decay_log = -jnp.exp(rate_log)[None, :] * step_size
    row_ids = lax.broadcasted_iota(jnp.int32, (tokens, tokens), 0)
    col_ids = lax.broadcasted_iota(jnp.int32, (tokens, tokens), 1)
    triangle = (row_ids >= col_ids).astype(jnp.float32)
    cumulative = jnp.dot(triangle, decay_log, precision=EXACT)
    return (step_size, cumulative, row_ids, col_ids)


def span_summary(values, mixer, step_weight, step_bias, rate_log, docs, doc_before):
    step_size, cumulative, row_ids, col_ids = local_setup(values, step_weight, step_bias, rate_log)
    final_log = cumulative[-1]
    tail_mask = (docs == docs[-1]).astype(jnp.float32)[:, None]
    tail_weight = (
        jnp.exp(jnp.where(tail_mask > 0, final_log[None, :] - cumulative, 0.0))
        * tail_mask
        * step_size
    )
    unbroken = (docs[-1] == doc_before).astype(jnp.float32)
    carry_decay = jnp.exp(final_log) * unbroken
    half_width = mixer.shape[1] // 2
    writers = mixer[:, :half_width]
    weighted = (tail_weight[:, :, None] * writers.astype(jnp.float32)[:, None, :]).astype(
        jnp.bfloat16
    )
    span_state = contract("thn,thp->hnp", weighted, values)
    return (carry_decay, span_state)


def span_local(values, mixer, step_weight, step_bias, rate_log, skip_gain, docs):
    step_size, cumulative, row_ids, col_ids = local_setup(values, step_weight, step_bias, rate_log)
    half_width = mixer.shape[1] // 2
    writers = mixer[:, :half_width]
    readers = mixer[:, half_width:]
    affinity = jnp.dot(readers, writers.T, preferred_element_type=jnp.float32)
    same_doc = ((docs[:, None] == docs[None, :]) & (row_ids >= col_ids)).astype(jnp.float32)
    heads_first = cumulative.T
    log_gap = heads_first[:, :, None] - heads_first[:, None, :]
    mixing = (
        jnp.exp(jnp.where(same_doc[None] > 0, log_gap, 0.0))
        * same_doc[None]
        * affinity[None]
        * step_size.T[:, None, :]
    )
    mixing = mixing.astype(jnp.bfloat16)
    local_part = contract("hts,shp->thp", mixing, values)
    return values.astype(jnp.float32) * (1.0 + skip_gain)[None, :, None] + local_part


def span_carry(values, mixer, step_weight, step_bias, rate_log, docs, doc_before, incoming):
    step_size, cumulative, row_ids, col_ids = local_setup(values, step_weight, step_bias, rate_log)
    half_width = mixer.shape[1] // 2
    readers = mixer[:, half_width:]
    unbroken = (docs == doc_before).astype(jnp.float32)
    carry_scale = jnp.exp(cumulative) * unbroken[:, None]
    carried = jnp.einsum("tn,hnp->thp", readers.astype(jnp.float32), incoming, precision=EXACT)
    return carry_scale[:, :, None] * carried


def scan_rounds(decay, state, axis, forward):
    size, mine = (lax.axis_size(axis), lax.axis_index(axis))
    far_decay, far_state = (decay, state)
    near_decay = jnp.ones_like(decay)
    near_state = jnp.zeros_like(state)
    distance = 1
    while distance < size:
        got_decay, got_state = shifted(
            (far_decay, far_state.astype(jnp.bfloat16)), axis, distance if forward else -distance
        )
        got_state = got_state.astype(jnp.float32)
        near_state = near_state + near_decay[:, None] * got_state
        near_decay = near_decay * got_decay
        if distance * 2 < size:
            far_state = far_state + far_decay[:, None] * got_state
            far_decay = far_decay * got_decay
        distance *= 2
    return near_state


def both_scans(decay, state, state_grad, axis, filler_fn, filler_args):
    size, mine = (lax.axis_size(axis), lax.axis_index(axis))
    if size & (size - 1):
        return (
            scan_rounds(decay, state, axis, True),
            scan_rounds(decay, state_grad, axis, False),
            filler_fn(*filler_args),
        )
    width = state.shape[1]
    total_decay = decay
    total_fwd, total_bwd = (state, state_grad)
    before = jnp.zeros_like(state)
    before_decay = jnp.ones_like(decay)
    after = jnp.zeros_like(state_grad)
    after_decay = jnp.ones_like(decay)
    distance = 1
    while distance < size:
        high = lax.convert_element_type(total_decay.astype(jnp.bfloat16), jnp.float32)
        low = total_decay - high
        pad = jnp.zeros((decay.shape[0], 126), jnp.float32)
        payload = jnp.concatenate(
            [total_fwd, total_bwd, high[:, None], low[:, None], pad], axis=1
        ).astype(jnp.bfloat16)
        upper = (mine // distance) % 2 == 1
        if distance == 1:
            payload, filler_args = lax.optimization_barrier((payload, filler_args))
        if distance * 2 < size:
            got = lax.ppermute(payload, axis, [(i, i ^ distance) for i in range(size)])
            got = got.astype(jnp.float32)
            got_fwd = got[:, :width]
            got_bwd = got[:, width : 2 * width]
        else:
            last = jnp.where(upper, total_bwd, total_fwd).astype(jnp.bfloat16)
            last = jnp.concatenate([last, payload[:, 2 * width :]], axis=1)
            got = lax.ppermute(last, axis, [(i, i ^ distance) for i in range(size)])
            got = got.astype(jnp.float32)
            got_fwd = got[:, :width]
            got_bwd = got_fwd
            got = jnp.concatenate([got[:, :width], got], axis=1)
        if distance == 1:
            got, filler = lax.optimization_barrier((got, filler_fn(*filler_args)))
        got_decay = got[:, 2 * width] + got[:, 2 * width + 1]
        before = jnp.where(upper, before + before_decay[:, None] * got_fwd, before)
        before_decay = jnp.where(upper, before_decay * got_decay, before_decay)
        after = jnp.where(upper, after, after + after_decay[:, None] * got_bwd)
        after_decay = jnp.where(upper, after_decay, after_decay * got_decay)
        if distance * 2 < size:
            total_fwd = jnp.where(
                upper,
                total_fwd + total_decay[:, None] * got_fwd,
                got_fwd + got_decay[:, None] * total_fwd,
            )
            total_bwd = jnp.where(
                upper,
                got_bwd + got_decay[:, None] * total_bwd,
                total_bwd + total_decay[:, None] * got_bwd,
            )
            total_decay = total_decay * got_decay
        distance *= 2
    return (before, after, filler)


def shards(bwd_input, bwd_docs, bwd_grad, proj_weight, step_weight, step_bias, rate_log, skip_gain):
    tokens = bwd_input.shape[1]
    channels_here = bwd_input.shape[2]
    heads_here = step_bias.shape[1]
    head_width = channels_here // heads_here
    bwd_flat = bwd_input[0]
    bwd_values = bwd_flat.reshape(tokens, heads_here, head_width)
    weight_heads = step_weight[0].reshape(heads_here, head_width)
    bias_heads = step_bias[0]
    rate_heads = rate_log[0]
    skip_heads = skip_gain[0]
    docs_bwd = bwd_docs[0]
    doc_before = shifted(docs_bwd[-1:], "seq", 1)[0]
    size, mine = (lax.axis_size("seq"), lax.axis_index("seq"))
    group = lax.axis_index("head")
    own_rows = proj_weight[0]
    slot_weight = jnp.concatenate(
        [own_rows] + [rotated(own_rows, "seq", k) for k in range(1, size)], axis=0
    )
    slot_value = jnp.dot(bwd_flat, slot_weight.T, preferred_element_type=jnp.float32)
    slot_value = slot_value.reshape(tokens, size, -1)[:, ::-1].reshape(tokens, -1)
    partial_value = roll_blocks(slot_value, mine + 1, size, 1)
    group_width = partial_value.shape[1] // 2
    mine_part = lax.dynamic_slice_in_dim(partial_value, group * group_width, group_width, axis=1)
    other_part = lax.dynamic_slice_in_dim(
        partial_value, (1 - group) * group_width, group_width, axis=1
    )
    mixer_bwd = (
        mine_part + swap_heads(other_part.astype(jnp.bfloat16)).astype(jnp.float32)
    ).astype(jnp.bfloat16)
    cotangent = bwd_grad[0].reshape(tokens, heads_here, head_width)

    def summary_bwd(values_in, mixer_in, weight_in, bias_in, rate_in):
        return span_summary(values_in, mixer_in, weight_in, bias_in, rate_in, docs_bwd, doc_before)

    summary_out, summary_pull = jax.vjp(
        summary_bwd, bwd_values, mixer_bwd, weight_heads, bias_heads, rate_heads
    )
    decay_bwd, state_bwd = summary_out
    state_shape = state_bwd.shape
    state_flat = state_bwd.reshape(heads_here, -1)

    out_ct = cotangent.astype(jnp.float32)

    def local_bwd(values_in, mixer_in, weight_in, bias_in, rate_in, skip_in):
        return span_local(values_in, mixer_in, weight_in, bias_in, rate_in, skip_in, docs_bwd)

    def local_pull(*primals):
        return jax.vjp(local_bwd, *primals[:-1])[1](primals[-1])


    def carry_bwd(values_in, mixer_in, weight_in, bias_in, rate_in, state_in):
        return span_carry(
            values_in, mixer_in, weight_in, bias_in, rate_in, docs_bwd, doc_before, state_in
        )

    def carried_only(state_in):
        return carry_bwd(bwd_values, mixer_bwd, weight_heads, bias_heads, rate_heads, state_in)

    state_grad = jax.vjp(carried_only, jnp.zeros(state_shape, jnp.float32))[1](out_ct)[0]
    state_grad = state_grad.reshape(heads_here, -1)
    incoming_flat, adjoint_flat, local_grads = both_scans(
        decay_bwd,
        state_flat,
        state_grad,
        "seq",
        local_pull,
        (bwd_values, mixer_bwd, weight_heads, bias_heads, rate_heads, skip_heads, out_ct),
    )
    incoming_bwd = incoming_flat.reshape(state_shape)
    carry_grads = jax.vjp(
        carry_bwd, bwd_values, mixer_bwd, weight_heads, bias_heads, rate_heads, incoming_bwd
    )[1](out_ct)
    out_grads = (
        (local_grads[0].astype(jnp.float32) + carry_grads[0].astype(jnp.float32)),
        (local_grads[1].astype(jnp.float32) + carry_grads[1].astype(jnp.float32)),
        local_grads[2] + carry_grads[2],
        local_grads[3] + carry_grads[3],
        local_grads[4] + carry_grads[4],
        local_grads[5],
    )
    decay_grad = jnp.sum(adjoint_flat * incoming_flat, axis=1)
    sum_grads = summary_pull((decay_grad, adjoint_flat.reshape(state_shape)))
    mixer_grad = (out_grads[1].astype(jnp.float32) + sum_grads[1].astype(jnp.float32)).astype(
        jnp.bfloat16
    )
    other_grad = swap_heads(mixer_grad)
    mixer_full = jnp.where(
        group == 0,
        jnp.concatenate([mixer_grad, other_grad], axis=1),
        jnp.concatenate([other_grad, mixer_grad], axis=1),
    )
    mixer_slots = roll_blocks(mixer_full, size - 1 - mine, size, 1)
    mixer_slots = mixer_slots.reshape(tokens, size, -1)[:, ::-1].reshape(tokens, -1)
    back_proj = jnp.dot(mixer_slots, slot_weight, preferred_element_type=jnp.float32)
    value_grad = (out_grads[0].astype(jnp.float32) + sum_grads[0].astype(jnp.float32)).reshape(
        tokens, channels_here
    ) + back_proj
    value_grad = value_grad.astype(jnp.bfloat16)
    prev_part = shifted(value_grad.reshape(1, tokens, channels_here), "section", -1)
    row_parts = lax.dot_general(
        mixer_full, bwd_flat, (((0,), (0,)), ((), ())), preferred_element_type=jnp.float32
    ).reshape(size, -1, channels_here)
    small = jnp.concatenate(
        [
            (out_grads[2] + sum_grads[2]).reshape(channels_here),
            out_grads[3] + sum_grads[3],
            out_grads[4] + sum_grads[4],
            out_grads[5],
        ]
    )
    small_rows = -(-small.shape[0] // channels_here)
    small = jnp.pad(small, (0, small_rows * channels_here - small.shape[0]))
    small = small.reshape(small_rows, channels_here)
    small_high = small.astype(jnp.bfloat16)
    small_low = (small - small_high.astype(jnp.float32)).astype(jnp.bfloat16)
    small_coded = jnp.concatenate([small_high, small_low], axis=0)
    block_rows = row_parts.shape[1]
    messages = jnp.concatenate(
        [
            row_parts.astype(jnp.bfloat16),
            jnp.broadcast_to(small_coded[None], (size,) + small_coded.shape),
        ],
        axis=1,
    )
    got = lax.all_to_all(messages, "seq", 0, 0, tiled=False).astype(jnp.float32)
    grad_rows = got[0, :block_rows]
    for j in range(1, size):
        grad_rows = grad_rows + got[j, :block_rows]
    small_parts = got[:, block_rows : block_rows + small_rows] + got[:, block_rows + small_rows :]
    small_total = small_parts[0]
    for j in range(1, size):
        small_total = small_total + small_parts[j]
    small = small_total.reshape(-1)
    totals = (
        small[:channels_here],
        small[channels_here : channels_here + heads_here],
        small[channels_here + heads_here : channels_here + 2 * heads_here],
        small[channels_here + 2 * heads_here : channels_here + 3 * heads_here],
    )
    return (
        prev_part,
        grad_rows[None],
        totals[0][None],
        totals[1][None],
        totals[2][None],
        totals[3][None],
    )


def solution(mesh):
    in_specs = (
        P("section", "seq", "head"),
        P("section", "seq"),
        P("section", "seq", "head"),
        P("section", "seq", "head"),
        P("section", "head"),
        P("section", "head"),
        P("section", "head"),
        P("section", "head"),
    )
    out_specs = (
        P("section", "seq", "head"),
        P("section", "seq", "head"),
        P("section", "head"),
        P("section", "head"),
        P("section", "head"),
        P("section", "head"),
    )
    return jax.shard_map(shards, mesh=mesh, in_specs=in_specs, out_specs=out_specs, check_vma=False)
```

```python
import jax
import jax.numpy as jnp
from jax import lax
from jax.sharding import PartitionSpec as P

EXACT = lax.Precision.HIGHEST


def shifted(block, axis, distance):
    devices = range(lax.axis_size(axis))
    route = [(i - distance, i) for i in devices if i - distance in devices]
    return lax.ppermute(block, axis, route)


def rotated(block, axis, distance):
    size = lax.axis_size(axis)
    route = [(i, (i + distance) % size) for i in range(size)]
    return lax.ppermute(block, axis, route)


def roll_blocks(value, shift, parts, dim):
    doubled = jnp.concatenate([value, value], axis=dim)
    width = value.shape[dim] // parts
    start = ((parts - shift) % parts) * width
    return lax.dynamic_slice_in_dim(doubled, start, value.shape[dim], axis=dim)


def swap_heads(block):
    return lax.ppermute(block, "head", [(0, 1), (1, 0)])


def contract(spec, left, right):
    return jnp.einsum(spec, left, right, preferred_element_type=jnp.float32)


def local_setup(values, step_weight, step_bias, rate_log):
    tokens = values.shape[0]
    raw_step = (
        jnp.einsum("thp,hp->th", values.astype(jnp.float32), step_weight, precision=EXACT)
        + step_bias[None, :]
    )
    step_size = jax.nn.softplus(raw_step)
    decay_log = -jnp.exp(rate_log)[None, :] * step_size
    row_ids = lax.broadcasted_iota(jnp.int32, (tokens, tokens), 0)
    col_ids = lax.broadcasted_iota(jnp.int32, (tokens, tokens), 1)
    triangle = (row_ids >= col_ids).astype(jnp.float32)
    cumulative = jnp.dot(triangle, decay_log, precision=EXACT)
    return (step_size, cumulative, row_ids, col_ids)


def span_summary(values, mixer, step_weight, step_bias, rate_log, docs, doc_before):
    step_size, cumulative, row_ids, col_ids = local_setup(values, step_weight, step_bias, rate_log)
    final_log = cumulative[-1]
    tail_mask = (docs == docs[-1]).astype(jnp.float32)[:, None]
    tail_weight = (
        jnp.exp(jnp.where(tail_mask > 0, final_log[None, :] - cumulative, 0.0))
        * tail_mask
        * step_size
    )
    unbroken = (docs[-1] == doc_before).astype(jnp.float32)
    carry_decay = jnp.exp(final_log) * unbroken
    half_width = mixer.shape[1] // 2
    writers = mixer[:, :half_width]
    weighted = (tail_weight[:, :, None] * writers.astype(jnp.float32)[:, None, :]).astype(
        jnp.bfloat16
    )
    span_state = contract("thn,thp->hnp", weighted, values)
    return (carry_decay, span_state)


def span_local(values, mixer, step_weight, step_bias, rate_log, skip_gain, docs):
    step_size, cumulative, row_ids, col_ids = local_setup(values, step_weight, step_bias, rate_log)
    half_width = mixer.shape[1] // 2
    writers = mixer[:, :half_width]
    readers = mixer[:, half_width:]
    affinity = jnp.dot(readers, writers.T, preferred_element_type=jnp.float32)
    same_doc = ((docs[:, None] == docs[None, :]) & (row_ids >= col_ids)).astype(jnp.float32)
    heads_first = cumulative.T
    log_gap = heads_first[:, :, None] - heads_first[:, None, :]
    mixing = (
        jnp.exp(jnp.where(same_doc[None] > 0, log_gap, 0.0))
        * same_doc[None]
        * affinity[None]
        * step_size.T[:, None, :]
    )
    mixing = mixing.astype(jnp.bfloat16)
    local_part = contract("hts,shp->thp", mixing, values)
    return values.astype(jnp.float32) * (1.0 + skip_gain)[None, :, None] + local_part


def span_carry(values, mixer, step_weight, step_bias, rate_log, docs, doc_before, incoming):
    step_size, cumulative, row_ids, col_ids = local_setup(values, step_weight, step_bias, rate_log)
    half_width = mixer.shape[1] // 2
    readers = mixer[:, half_width:]
    unbroken = (docs == doc_before).astype(jnp.float32)
    carry_scale = jnp.exp(cumulative) * unbroken[:, None]
    carried = jnp.einsum("tn,hnp->thp", readers.astype(jnp.float32), incoming, precision=EXACT)
    return carry_scale[:, :, None] * carried


def scan_rounds(decay, state, axis, forward):
    size, mine = (lax.axis_size(axis), lax.axis_index(axis))
    far_decay, far_state = (decay, state)
    near_decay = jnp.ones_like(decay)
    near_state = jnp.zeros_like(state)
    distance = 1
    while distance < size:
        got_decay, got_state = shifted(
            (far_decay, far_state.astype(jnp.bfloat16)), axis, distance if forward else -distance
        )
        got_state = got_state.astype(jnp.float32)
        near_state = near_state + near_decay[:, None] * got_state
        near_decay = near_decay * got_decay
        if distance * 2 < size:
            far_state = far_state + far_decay[:, None] * got_state
            far_decay = far_decay * got_decay
        distance *= 2
    return near_state


def both_scans(decay, state, state_grad, axis):
    size, mine = (lax.axis_size(axis), lax.axis_index(axis))
    if size & (size - 1):
        return (
            scan_rounds(decay, state, axis, True),
            scan_rounds(decay, state_grad, axis, False),
        )
    width = state.shape[1]
    total_decay = decay
    total_fwd, total_bwd = (state, state_grad)
    before = jnp.zeros_like(state)
    before_decay = jnp.ones_like(decay)
    after = jnp.zeros_like(state_grad)
    after_decay = jnp.ones_like(decay)
    distance = 1
    while distance < size:
        high = lax.convert_element_type(total_decay.astype(jnp.bfloat16), jnp.float32)
        low = total_decay - high
        pad = jnp.zeros((decay.shape[0], 126), jnp.float32)
        payload = jnp.concatenate(
            [total_fwd, total_bwd, high[:, None], low[:, None], pad], axis=1
        ).astype(jnp.bfloat16)
        upper = (mine // distance) % 2 == 1
        if distance * 2 < size:
            got = lax.ppermute(payload, axis, [(i, i ^ distance) for i in range(size)])
            got = got.astype(jnp.float32)
            got_fwd = got[:, :width]
            got_bwd = got[:, width : 2 * width]
        else:
            last = jnp.where(upper, total_bwd, total_fwd).astype(jnp.bfloat16)
            last = jnp.concatenate([last, payload[:, 2 * width :]], axis=1)
            got = lax.ppermute(last, axis, [(i, i ^ distance) for i in range(size)])
            got = got.astype(jnp.float32)
            got_fwd = got[:, :width]
            got_bwd = got_fwd
            got = jnp.concatenate([got[:, :width], got], axis=1)
        got_decay = got[:, 2 * width] + got[:, 2 * width + 1]
        before = jnp.where(upper, before + before_decay[:, None] * got_fwd, before)
        before_decay = jnp.where(upper, before_decay * got_decay, before_decay)
        after = jnp.where(upper, after, after + after_decay[:, None] * got_bwd)
        after_decay = jnp.where(upper, after_decay, after_decay * got_decay)
        if distance * 2 < size:
            total_fwd = jnp.where(
                upper,
                total_fwd + total_decay[:, None] * got_fwd,
                got_fwd + got_decay[:, None] * total_fwd,
            )
            total_bwd = jnp.where(
                upper,
                got_bwd + got_decay[:, None] * total_bwd,
                total_bwd + total_decay[:, None] * got_bwd,
            )
            total_decay = total_decay * got_decay
        distance *= 2
    return (before, after)


def shards(bwd_input, bwd_docs, bwd_grad, proj_weight, step_weight, step_bias, rate_log, skip_gain):
    tokens = bwd_input.shape[1]
    channels_here = bwd_input.shape[2]
    heads_here = step_bias.shape[1]
    head_width = channels_here // heads_here
    bwd_flat = bwd_input[0]
    bwd_values = bwd_flat.reshape(tokens, heads_here, head_width)
    weight_heads = step_weight[0].reshape(heads_here, head_width)
    bias_heads = step_bias[0]
    rate_heads = rate_log[0]
    skip_heads = skip_gain[0]
    docs_bwd = bwd_docs[0]
    doc_before = shifted(docs_bwd[-1:], "seq", 1)[0]
    size, mine = (lax.axis_size("seq"), lax.axis_index("seq"))
    group = lax.axis_index("head")
    own_rows = proj_weight[0]
    slot_weight = jnp.concatenate(
        [own_rows] + [rotated(own_rows, "seq", k) for k in range(1, size)], axis=0
    )
    slot_value = jnp.dot(bwd_flat, slot_weight.T, preferred_element_type=jnp.float32)
    slot_value = slot_value.reshape(tokens, size, -1)[:, ::-1].reshape(tokens, -1)
    partial_value = roll_blocks(slot_value, mine + 1, size, 1)
    group_width = partial_value.shape[1] // 2
    mine_part = lax.dynamic_slice_in_dim(partial_value, group * group_width, group_width, axis=1)
    other_part = lax.dynamic_slice_in_dim(
        partial_value, (1 - group) * group_width, group_width, axis=1
    )
    mixer_bwd = (
        mine_part + swap_heads(other_part.astype(jnp.bfloat16)).astype(jnp.float32)
    ).astype(jnp.bfloat16)
    cotangent = bwd_grad[0].reshape(tokens, heads_here, head_width)

    def summary_bwd(values_in, mixer_in, weight_in, bias_in, rate_in):
        return span_summary(values_in, mixer_in, weight_in, bias_in, rate_in, docs_bwd, doc_before)

    summary_out, summary_pull = jax.vjp(
        summary_bwd, bwd_values, mixer_bwd, weight_heads, bias_heads, rate_heads
    )
    decay_bwd, state_bwd = summary_out
    state_shape = state_bwd.shape
    state_flat = state_bwd.reshape(heads_here, -1)

    out_ct = cotangent.astype(jnp.float32)

    def local_bwd(values_in, mixer_in, weight_in, bias_in, rate_in, skip_in):
        return span_local(values_in, mixer_in, weight_in, bias_in, rate_in, skip_in, docs_bwd)

    local_grads = jax.vjp(
        local_bwd, bwd_values, mixer_bwd, weight_heads, bias_heads, rate_heads, skip_heads
    )[1](out_ct)

    def carry_bwd(values_in, mixer_in, weight_in, bias_in, rate_in, state_in):
        return span_carry(
            values_in, mixer_in, weight_in, bias_in, rate_in, docs_bwd, doc_before, state_in
        )

    def carried_only(state_in):
        return carry_bwd(bwd_values, mixer_bwd, weight_heads, bias_heads, rate_heads, state_in)

    state_grad = jax.vjp(carried_only, jnp.zeros(state_shape, jnp.float32))[1](out_ct)[0]
    state_grad = state_grad.reshape(heads_here, -1)
    incoming_flat, adjoint_flat = both_scans(decay_bwd, state_flat, state_grad, "seq")
    incoming_bwd = incoming_flat.reshape(state_shape)
    carry_grads = jax.vjp(
        carry_bwd, bwd_values, mixer_bwd, weight_heads, bias_heads, rate_heads, incoming_bwd
    )[1](out_ct)
    out_grads = (
        (local_grads[0].astype(jnp.float32) + carry_grads[0].astype(jnp.float32)),
        (local_grads[1].astype(jnp.float32) + carry_grads[1].astype(jnp.float32)),
        local_grads[2] + carry_grads[2],
        local_grads[3] + carry_grads[3],
        local_grads[4] + carry_grads[4],
        local_grads[5],
    )
    decay_grad = jnp.sum(adjoint_flat * incoming_flat, axis=1)
    sum_grads = summary_pull((decay_grad, adjoint_flat.reshape(state_shape)))
    mixer_grad = (out_grads[1].astype(jnp.float32) + sum_grads[1].astype(jnp.float32)).astype(
        jnp.bfloat16
    )
    other_grad = swap_heads(mixer_grad)
    mixer_full = jnp.where(
        group == 0,
        jnp.concatenate([mixer_grad, other_grad], axis=1),
        jnp.concatenate([other_grad, mixer_grad], axis=1),
    )
    mixer_slots = roll_blocks(mixer_full, size - 1 - mine, size, 1)
    mixer_slots = mixer_slots.reshape(tokens, size, -1)[:, ::-1].reshape(tokens, -1)
    back_proj = jnp.dot(mixer_slots, slot_weight, preferred_element_type=jnp.float32)
    value_grad = (out_grads[0].astype(jnp.float32) + sum_grads[0].astype(jnp.float32)).reshape(
        tokens, channels_here
    ) + back_proj
    value_grad = value_grad.astype(jnp.bfloat16)
    prev_part = shifted(value_grad.reshape(1, tokens, channels_here), "section", -1)
    dest_grad = roll_blocks(mixer_full, size - mine, size, 1)
    row_parts = lax.dot_general(
        dest_grad, bwd_flat, (((0,), (0,)), ((), ())), preferred_element_type=jnp.float32
    ).reshape(size, -1, channels_here)
    small = jnp.concatenate(
        [
            (out_grads[2] + sum_grads[2]).reshape(channels_here),
            out_grads[3] + sum_grads[3],
            out_grads[4] + sum_grads[4],
            out_grads[5],
        ]
    )
    small_rows = -(-small.shape[0] // channels_here)
    small = jnp.pad(small, (0, small_rows * channels_here - small.shape[0]))
    small = small.reshape(small_rows, channels_here)
    small_high = small.astype(jnp.bfloat16)
    small_low = (small - small_high.astype(jnp.float32)).astype(jnp.bfloat16)
    small_coded = jnp.concatenate([small_high, small_low], axis=0)
    block_rows = row_parts.shape[1]
    grad_rows = row_parts[0]
    small_slots = [small_coded]
    for k in range(1, size):
        message = jnp.concatenate([row_parts[k].astype(jnp.bfloat16), small_coded], axis=0)
        got = rotated(message, "seq", k)
        grad_rows = grad_rows + got[:block_rows].astype(jnp.float32)
        small_slots.append(got[block_rows:])
    small_slots = jnp.stack(small_slots[::-1])
    small_slots = roll_blocks(small_slots, mine + 1, size, 0).astype(jnp.float32)
    small_parts = small_slots[:, :small_rows] + small_slots[:, small_rows:]
    small_total = small_parts[0]
    for j in range(1, size):
        small_total = small_total + small_parts[j]
    small = small_total.reshape(-1)
    totals = (
        small[:channels_here],
        small[channels_here : channels_here + heads_here],
        small[channels_here + heads_here : channels_here + 2 * heads_here],
        small[channels_here + 2 * heads_here : channels_here + 3 * heads_here],
    )
    return (
        prev_part,
        grad_rows[None],
        totals[0][None],
        totals[1][None],
        totals[2][None],
        totals[3][None],
    )


def solution(mesh):
    in_specs = (
        P("section", "seq", "head"),
        P("section", "seq"),
        P("section", "seq", "head"),
        P("section", "seq", "head"),
        P("section", "head"),
        P("section", "head"),
        P("section", "head"),
        P("section", "head"),
    )
    out_specs = (
        P("section", "seq", "head"),
        P("section", "seq", "head"),
        P("section", "head"),
        P("section", "head"),
        P("section", "head"),
        P("section", "head"),
    )
    return jax.shard_map(shards, mesh=mesh, in_specs=in_specs, out_specs=out_specs, check_vma=False)
```

```python
import jax
import jax.numpy as jnp
from jax import lax
from jax.sharding import PartitionSpec as P

EXACT = lax.Precision.HIGHEST


def shifted(block, axis, distance):
    devices = range(lax.axis_size(axis))
    route = [(i - distance, i) for i in devices if i - distance in devices]
    return lax.ppermute(block, axis, route)


def rotated(block, axis, distance):
    size = lax.axis_size(axis)
    route = [(i, (i + distance) % size) for i in range(size)]
    return lax.ppermute(block, axis, route)


def roll_blocks(value, shift, parts, dim):
    doubled = jnp.concatenate([value, value], axis=dim)
    width = value.shape[dim] // parts
    start = ((parts - shift) % parts) * width
    return lax.dynamic_slice_in_dim(doubled, start, value.shape[dim], axis=dim)


def swap_heads(block):
    return lax.ppermute(block, "head", [(0, 1), (1, 0)])


def contract(spec, left, right):
    return jnp.einsum(spec, left, right, preferred_element_type=jnp.float32)


def local_setup(values, step_weight, step_bias, rate_log):
    tokens = values.shape[0]
    raw_step = (
        jnp.einsum("thp,hp->th", values.astype(jnp.float32), step_weight, precision=EXACT)
        + step_bias[None, :]
    )
    step_size = jax.nn.softplus(raw_step)
    decay_log = -jnp.exp(rate_log)[None, :] * step_size
    row_ids = lax.broadcasted_iota(jnp.int32, (tokens, tokens), 0)
    col_ids = lax.broadcasted_iota(jnp.int32, (tokens, tokens), 1)
    triangle = (row_ids >= col_ids).astype(jnp.float32)
    cumulative = jnp.dot(triangle, decay_log, precision=EXACT)
    return (step_size, cumulative, row_ids, col_ids)


def span_summary(values, mixer, step_weight, step_bias, rate_log, docs, doc_before):
    step_size, cumulative, row_ids, col_ids = local_setup(values, step_weight, step_bias, rate_log)
    final_log = cumulative[-1]
    tail_mask = (docs == docs[-1]).astype(jnp.float32)[:, None]
    tail_weight = (
        jnp.exp(jnp.where(tail_mask > 0, final_log[None, :] - cumulative, 0.0))
        * tail_mask
        * step_size
    )
    unbroken = (docs[-1] == doc_before).astype(jnp.float32)
    carry_decay = jnp.exp(final_log) * unbroken
    half_width = mixer.shape[1] // 2
    writers = mixer[:, :half_width]
    weighted = (tail_weight[:, :, None] * writers.astype(jnp.float32)[:, None, :]).astype(
        jnp.bfloat16
    )
    span_state = contract("thn,thp->hnp", weighted, values)
    return (carry_decay, span_state)


def span_local(values, mixer, step_weight, step_bias, rate_log, skip_gain, docs):
    step_size, cumulative, row_ids, col_ids = local_setup(values, step_weight, step_bias, rate_log)
    half_width = mixer.shape[1] // 2
    writers = mixer[:, :half_width]
    readers = mixer[:, half_width:]
    affinity = jnp.dot(readers, writers.T, preferred_element_type=jnp.float32)
    same_doc = ((docs[:, None] == docs[None, :]) & (row_ids >= col_ids)).astype(jnp.float32)
    heads_first = cumulative.T
    log_gap = heads_first[:, :, None] - heads_first[:, None, :]
    mixing = (
        jnp.exp(jnp.where(same_doc[None] > 0, log_gap, 0.0))
        * same_doc[None]
        * affinity[None]
        * step_size.T[:, None, :]
    )
    mixing = mixing.astype(jnp.bfloat16)
    local_part = contract("hts,shp->thp", mixing, values)
    return values.astype(jnp.float32) * (1.0 + skip_gain)[None, :, None] + local_part


def span_carry(values, mixer, step_weight, step_bias, rate_log, docs, doc_before, incoming):
    step_size, cumulative, row_ids, col_ids = local_setup(values, step_weight, step_bias, rate_log)
    half_width = mixer.shape[1] // 2
    readers = mixer[:, half_width:]
    unbroken = (docs == doc_before).astype(jnp.float32)
    carry_scale = jnp.exp(cumulative) * unbroken[:, None]
    carried = jnp.einsum("tn,hnp->thp", readers.astype(jnp.float32), incoming, precision=EXACT)
    return carry_scale[:, :, None] * carried


def scan_rounds(decay, state, axis, forward):
    size, mine = (lax.axis_size(axis), lax.axis_index(axis))
    far_decay, far_state = (decay, state)
    near_decay = jnp.ones_like(decay)
    near_state = jnp.zeros_like(state)
    distance = 1
    while distance < size:
        got_decay, got_state = shifted(
            (far_decay, far_state.astype(jnp.bfloat16)), axis, distance if forward else -distance
        )
        got_state = got_state.astype(jnp.float32)
        near_state = near_state + near_decay[:, None] * got_state
        near_decay = near_decay * got_decay
        if distance * 2 < size:
            far_state = far_state + far_decay[:, None] * got_state
            far_decay = far_decay * got_decay
        distance *= 2
    return near_state


def both_scans(decay, state, state_grad, axis, filler_fn, filler_args):
    size, mine = (lax.axis_size(axis), lax.axis_index(axis))
    if size & (size - 1):
        return (
            scan_rounds(decay, state, axis, True),
            scan_rounds(decay, state_grad, axis, False),
            filler_fn(*filler_args),
        )
    width = state.shape[1]
    total_decay = decay
    total_fwd, total_bwd = (state, state_grad)
    before = jnp.zeros_like(state)
    before_decay = jnp.ones_like(decay)
    after = jnp.zeros_like(state_grad)
    after_decay = jnp.ones_like(decay)
    distance = 1
    while distance < size:
        high = lax.convert_element_type(total_decay.astype(jnp.bfloat16), jnp.float32)
        low = total_decay - high
        pad = jnp.zeros((decay.shape[0], 126), jnp.float32)
        payload = jnp.concatenate(
            [total_fwd, total_bwd, high[:, None], low[:, None], pad], axis=1
        ).astype(jnp.bfloat16)
        upper = (mine // distance) % 2 == 1
        if distance == 1:
            payload, filler_args = lax.optimization_barrier((payload, filler_args))
        if distance * 2 < size:
            got = lax.ppermute(payload, axis, [(i, i ^ distance) for i in range(size)])
            got = got.astype(jnp.float32)
            got_fwd = got[:, :width]
            got_bwd = got[:, width : 2 * width]
        else:
            last = jnp.where(upper, total_bwd, total_fwd).astype(jnp.bfloat16)
            last = jnp.concatenate([last, payload[:, 2 * width :]], axis=1)
            got = lax.ppermute(last, axis, [(i, i ^ distance) for i in range(size)])
            got = got.astype(jnp.float32)
            got_fwd = got[:, :width]
            got_bwd = got_fwd
            got = jnp.concatenate([got[:, :width], got], axis=1)
        if distance == 1:
            got, filler = lax.optimization_barrier((got, filler_fn(*filler_args)))
        got_decay = got[:, 2 * width] + got[:, 2 * width + 1]
        before = jnp.where(upper, before + before_decay[:, None] * got_fwd, before)
        before_decay = jnp.where(upper, before_decay * got_decay, before_decay)
        after = jnp.where(upper, after, after + after_decay[:, None] * got_bwd)
        after_decay = jnp.where(upper, after_decay, after_decay * got_decay)
        if distance * 2 < size:
            total_fwd = jnp.where(
                upper,
                total_fwd + total_decay[:, None] * got_fwd,
                got_fwd + got_decay[:, None] * total_fwd,
            )
            total_bwd = jnp.where(
                upper,
                got_bwd + got_decay[:, None] * total_bwd,
                total_bwd + total_decay[:, None] * got_bwd,
            )
            total_decay = total_decay * got_decay
        distance *= 2
    return (before, after, filler)


def shards(bwd_input, bwd_docs, bwd_grad, proj_weight, step_weight, step_bias, rate_log, skip_gain):
    tokens = bwd_input.shape[1]
    channels_here = bwd_input.shape[2]
    heads_here = step_bias.shape[1]
    head_width = channels_here // heads_here
    bwd_flat = bwd_input[0]
    bwd_values = bwd_flat.reshape(tokens, heads_here, head_width)
    weight_heads = step_weight[0].reshape(heads_here, head_width)
    bias_heads = step_bias[0]
    rate_heads = rate_log[0]
    skip_heads = skip_gain[0]
    docs_bwd = bwd_docs[0]
    doc_before = shifted(docs_bwd[-1:], "seq", 1)[0]
    size, mine = (lax.axis_size("seq"), lax.axis_index("seq"))
    group = lax.axis_index("head")
    own_rows = proj_weight[0]
    slot_weight = jnp.concatenate(
        [own_rows] + [rotated(own_rows, "seq", k) for k in range(1, size)], axis=0
    )
    slot_value = jnp.dot(bwd_flat, slot_weight.T, preferred_element_type=jnp.float32)
    slot_value = slot_value.reshape(tokens, size, -1)[:, ::-1].reshape(tokens, -1)
    partial_value = roll_blocks(slot_value, mine + 1, size, 1)
    group_width = partial_value.shape[1] // 2
    mine_part = lax.dynamic_slice_in_dim(partial_value, group * group_width, group_width, axis=1)
    other_part = lax.dynamic_slice_in_dim(
        partial_value, (1 - group) * group_width, group_width, axis=1
    )
    mixer_bwd = (
        mine_part + swap_heads(other_part.astype(jnp.bfloat16)).astype(jnp.float32)
    ).astype(jnp.bfloat16)
    cotangent = bwd_grad[0].reshape(tokens, heads_here, head_width)

    def summary_bwd(values_in, mixer_in, weight_in, bias_in, rate_in):
        return span_summary(values_in, mixer_in, weight_in, bias_in, rate_in, docs_bwd, doc_before)

    summary_out, summary_pull = jax.vjp(
        summary_bwd, bwd_values, mixer_bwd, weight_heads, bias_heads, rate_heads
    )
    decay_bwd, state_bwd = summary_out
    state_shape = state_bwd.shape
    state_flat = state_bwd.reshape(heads_here, -1)

    out_ct = cotangent.astype(jnp.float32)

    def local_bwd(values_in, mixer_in, weight_in, bias_in, rate_in, skip_in):
        return span_local(values_in, mixer_in, weight_in, bias_in, rate_in, skip_in, docs_bwd)

    def local_pull(*primals):
        return jax.vjp(local_bwd, *primals[:-1])[1](primals[-1])


    def carry_bwd(values_in, mixer_in, weight_in, bias_in, rate_in, state_in):
        return span_carry(
            values_in, mixer_in, weight_in, bias_in, rate_in, docs_bwd, doc_before, state_in
        )

    def carried_only(state_in):
        return carry_bwd(bwd_values, mixer_bwd, weight_heads, bias_heads, rate_heads, state_in)

    state_grad = jax.vjp(carried_only, jnp.zeros(state_shape, jnp.float32))[1](out_ct)[0]
    state_grad = state_grad.reshape(heads_here, -1)
    incoming_flat, adjoint_flat, local_grads = both_scans(
        decay_bwd,
        state_flat,
        state_grad,
        "seq",
        local_pull,
        (bwd_values, mixer_bwd, weight_heads, bias_heads, rate_heads, skip_heads, out_ct),
    )
    incoming_bwd = incoming_flat.reshape(state_shape)
    carry_grads = jax.vjp(
        carry_bwd, bwd_values, mixer_bwd, weight_heads, bias_heads, rate_heads, incoming_bwd
    )[1](out_ct)
    out_grads = (
        (local_grads[0].astype(jnp.float32) + carry_grads[0].astype(jnp.float32)),
        (local_grads[1].astype(jnp.float32) + carry_grads[1].astype(jnp.float32)),
        local_grads[2] + carry_grads[2],
        local_grads[3] + carry_grads[3],
        local_grads[4] + carry_grads[4],
        local_grads[5],
    )
    decay_grad = jnp.sum(adjoint_flat * incoming_flat, axis=1)
    sum_grads = summary_pull((decay_grad, adjoint_flat.reshape(state_shape)))
    mixer_grad = (out_grads[1].astype(jnp.float32) + sum_grads[1].astype(jnp.float32)).astype(
        jnp.bfloat16
    )
    other_grad = swap_heads(mixer_grad)
    mixer_full = jnp.where(
        group == 0,
        jnp.concatenate([mixer_grad, other_grad], axis=1),
        jnp.concatenate([other_grad, mixer_grad], axis=1),
    )
    mixer_slots = roll_blocks(mixer_full, size - 1 - mine, size, 1)
    mixer_slots = mixer_slots.reshape(tokens, size, -1)[:, ::-1].reshape(tokens, -1)
    back_proj = jnp.dot(mixer_slots, slot_weight, preferred_element_type=jnp.float32)
    value_grad = (out_grads[0].astype(jnp.float32) + sum_grads[0].astype(jnp.float32)).reshape(
        tokens, channels_here
    ) + back_proj
    value_grad = value_grad.astype(jnp.bfloat16)
    prev_part = shifted(value_grad.reshape(1, tokens, channels_here), "section", -1)
    dest_grad = roll_blocks(mixer_full, size - mine, size, 1)
    row_parts = lax.dot_general(
        dest_grad, bwd_flat, (((0,), (0,)), ((), ())), preferred_element_type=jnp.float32
    ).reshape(size, -1, channels_here)
    small = jnp.concatenate(
        [
            (out_grads[2] + sum_grads[2]).reshape(channels_here),
            out_grads[3] + sum_grads[3],
            out_grads[4] + sum_grads[4],
            out_grads[5],
        ]
    )
    count = small.shape[0]
    block_rows = row_parts.shape[1]
    small_high = small.astype(jnp.bfloat16)
    small_low = (small - small_high.astype(jnp.float32)).astype(jnp.bfloat16)
    small_cols = -(-(2 * count) // (block_rows * 128)) * 128
    small_coded = jnp.concatenate([small_high, small_low])
    small_coded = jnp.pad(small_coded, (0, block_rows * small_cols - 2 * count))
    small_coded = small_coded.reshape(block_rows, small_cols)
    grad_rows = row_parts[0]
    small_slots = [small_coded]
    for k in range(1, size):
        message = jnp.concatenate([row_parts[k].astype(jnp.bfloat16), small_coded], axis=1)
        got = rotated(message, "seq", k)
        grad_rows = grad_rows + got[:, :channels_here].astype(jnp.float32)
        small_slots.append(got[:, channels_here:])
    small_slots = jnp.stack(small_slots[::-1])
    small_slots = roll_blocks(small_slots, mine + 1, size, 0).astype(jnp.float32)
    small_slots = small_slots.reshape(size, -1)
    small_parts = small_slots[:, :count] + small_slots[:, count : 2 * count]
    small_total = small_parts[0]
    for j in range(1, size):
        small_total = small_total + small_parts[j]
    small = small_total.reshape(-1)
    totals = (
        small[:channels_here],
        small[channels_here : channels_here + heads_here],
        small[channels_here + heads_here : channels_here + 2 * heads_here],
        small[channels_here + 2 * heads_here : channels_here + 3 * heads_here],
    )
    return (
        prev_part,
        grad_rows[None],
        totals[0][None],
        totals[1][None],
        totals[2][None],
        totals[3][None],
    )


def solution(mesh):
    in_specs = (
        P("section", "seq", "head"),
        P("section", "seq"),
        P("section", "seq", "head"),
        P("section", "seq", "head"),
        P("section", "head"),
        P("section", "head"),
        P("section", "head"),
        P("section", "head"),
    )
    out_specs = (
        P("section", "seq", "head"),
        P("section", "seq", "head"),
        P("section", "head"),
        P("section", "head"),
        P("section", "head"),
        P("section", "head"),
    )
    return jax.shard_map(shards, mesh=mesh, in_specs=in_specs, out_specs=out_specs, check_vma=False)
```

```python
import jax
import jax.numpy as jnp
from jax import lax
from jax.sharding import PartitionSpec as P

EXACT = lax.Precision.HIGHEST


def shifted(block, axis, distance):
    devices = range(lax.axis_size(axis))
    route = [(i - distance, i) for i in devices if i - distance in devices]
    return lax.ppermute(block, axis, route)


def rotated(block, axis, distance):
    size = lax.axis_size(axis)
    route = [(i, (i + distance) % size) for i in range(size)]
    return lax.ppermute(block, axis, route)


def roll_blocks(value, shift, parts, dim):
    doubled = jnp.concatenate([value, value], axis=dim)
    width = value.shape[dim] // parts
    start = ((parts - shift) % parts) * width
    return lax.dynamic_slice_in_dim(doubled, start, value.shape[dim], axis=dim)


def swap_heads(block):
    return lax.ppermute(block, "head", [(0, 1), (1, 0)])


def contract(spec, left, right):
    return jnp.einsum(spec, left, right, preferred_element_type=jnp.float32)


def local_setup(values, step_weight, step_bias, rate_log):
    tokens = values.shape[0]
    raw_step = (
        jnp.einsum("thp,hp->th", values.astype(jnp.float32), step_weight, precision=EXACT)
        + step_bias[None, :]
    )
    step_size = jax.nn.softplus(raw_step)
    decay_log = -jnp.exp(rate_log)[None, :] * step_size
    row_ids = lax.broadcasted_iota(jnp.int32, (tokens, tokens), 0)
    col_ids = lax.broadcasted_iota(jnp.int32, (tokens, tokens), 1)
    triangle = (row_ids >= col_ids).astype(jnp.float32)
    cumulative = jnp.dot(triangle, decay_log, precision=EXACT)
    return (step_size, cumulative, row_ids, col_ids)


def span_summary(values, mixer, step_weight, step_bias, rate_log, docs, doc_before):
    step_size, cumulative, row_ids, col_ids = local_setup(values, step_weight, step_bias, rate_log)
    final_log = cumulative[-1]
    tail_mask = (docs == docs[-1]).astype(jnp.float32)[:, None]
    tail_weight = (
        jnp.exp(jnp.where(tail_mask > 0, final_log[None, :] - cumulative, 0.0))
        * tail_mask
        * step_size
    )
    unbroken = (docs[-1] == doc_before).astype(jnp.float32)
    carry_decay = jnp.exp(final_log) * unbroken
    half_width = mixer.shape[1] // 2
    writers = mixer[:, :half_width]
    weighted = (tail_weight[:, :, None] * writers.astype(jnp.float32)[:, None, :]).astype(
        jnp.bfloat16
    )
    span_state = contract("thn,thp->hnp", weighted, values)
    return (carry_decay, span_state)


def span_local(values, mixer, step_weight, step_bias, rate_log, skip_gain, docs):
    step_size, cumulative, row_ids, col_ids = local_setup(values, step_weight, step_bias, rate_log)
    half_width = mixer.shape[1] // 2
    writers = mixer[:, :half_width]
    readers = mixer[:, half_width:]
    affinity = jnp.dot(readers, writers.T, preferred_element_type=jnp.float32)
    same_doc = ((docs[:, None] == docs[None, :]) & (row_ids >= col_ids)).astype(jnp.float32)
    heads_first = cumulative.T
    log_gap = heads_first[:, :, None] - heads_first[:, None, :]
    mixing = (
        jnp.exp(jnp.where(same_doc[None] > 0, log_gap, 0.0))
        * same_doc[None]
        * affinity[None]
        * step_size.T[:, None, :]
    )
    mixing = mixing.astype(jnp.bfloat16)
    local_part = contract("hts,shp->thp", mixing, values)
    return values.astype(jnp.float32) * (1.0 + skip_gain)[None, :, None] + local_part


def span_carry(values, mixer, step_weight, step_bias, rate_log, docs, doc_before, incoming):
    step_size, cumulative, row_ids, col_ids = local_setup(values, step_weight, step_bias, rate_log)
    half_width = mixer.shape[1] // 2
    readers = mixer[:, half_width:]
    unbroken = (docs == doc_before).astype(jnp.float32)
    carry_scale = jnp.exp(cumulative) * unbroken[:, None]
    carried = jnp.einsum("tn,hnp->thp", readers.astype(jnp.float32), incoming, precision=EXACT)
    return carry_scale[:, :, None] * carried


def scan_rounds(decay, state, axis, forward):
    size, mine = (lax.axis_size(axis), lax.axis_index(axis))
    far_decay, far_state = (decay, state)
    near_decay = jnp.ones_like(decay)
    near_state = jnp.zeros_like(state)
    distance = 1
    while distance < size:
        got_decay, got_state = shifted(
            (far_decay, far_state.astype(jnp.bfloat16)), axis, distance if forward else -distance
        )
        got_state = got_state.astype(jnp.float32)
        near_state = near_state + near_decay[:, None] * got_state
        near_decay = near_decay * got_decay
        if distance * 2 < size:
            far_state = far_state + far_decay[:, None] * got_state
            far_decay = far_decay * got_decay
        distance *= 2
    return near_state


def dense_swap(block, axis, pairs):
    count = block.size
    tiles = -(-count // 2048) * 2048
    flat = jnp.pad(block.reshape(-1), (0, tiles - count)).reshape(-1, 128)
    got = lax.ppermute(flat, axis, pairs)
    return got.reshape(-1)[:count].reshape(block.shape)


def both_scans(decay, state, state_grad, axis, filler_fn, filler_args):
    size, mine = (lax.axis_size(axis), lax.axis_index(axis))
    if size & (size - 1):
        return (
            scan_rounds(decay, state, axis, True),
            scan_rounds(decay, state_grad, axis, False),
            filler_fn(*filler_args),
        )
    width = state.shape[1]
    total_decay = decay
    total_fwd, total_bwd = (state, state_grad)
    before = jnp.zeros_like(state)
    before_decay = jnp.ones_like(decay)
    after = jnp.zeros_like(state_grad)
    after_decay = jnp.ones_like(decay)
    distance = 1
    while distance < size:
        high = lax.convert_element_type(total_decay.astype(jnp.bfloat16), jnp.float32)
        low = total_decay - high
        pad = jnp.zeros((decay.shape[0], 126), jnp.float32)
        payload = jnp.concatenate(
            [total_fwd, total_bwd, high[:, None], low[:, None], pad], axis=1
        ).astype(jnp.bfloat16)
        upper = (mine // distance) % 2 == 1
        if distance == 1:
            payload, filler_args = lax.optimization_barrier((payload, filler_args))
        if distance * 2 < size:
            got = dense_swap(payload, axis, [(i, i ^ distance) for i in range(size)])
            got = got.astype(jnp.float32)
            got_fwd = got[:, :width]
            got_bwd = got[:, width : 2 * width]
        else:
            last = jnp.where(upper, total_bwd, total_fwd).astype(jnp.bfloat16)
            last = jnp.concatenate([last, payload[:, 2 * width :]], axis=1)
            got = dense_swap(last, axis, [(i, i ^ distance) for i in range(size)])
            got = got.astype(jnp.float32)
            got_fwd = got[:, :width]
            got_bwd = got_fwd
            got = jnp.concatenate([got[:, :width], got], axis=1)
        if distance == 1:
            got, filler = lax.optimization_barrier((got, filler_fn(*filler_args)))
        got_decay = got[:, 2 * width] + got[:, 2 * width + 1]
        before = jnp.where(upper, before + before_decay[:, None] * got_fwd, before)
        before_decay = jnp.where(upper, before_decay * got_decay, before_decay)
        after = jnp.where(upper, after, after + after_decay[:, None] * got_bwd)
        after_decay = jnp.where(upper, after_decay, after_decay * got_decay)
        if distance * 2 < size:
            total_fwd = jnp.where(
                upper,
                total_fwd + total_decay[:, None] * got_fwd,
                got_fwd + got_decay[:, None] * total_fwd,
            )
            total_bwd = jnp.where(
                upper,
                got_bwd + got_decay[:, None] * total_bwd,
                total_bwd + total_decay[:, None] * got_bwd,
            )
            total_decay = total_decay * got_decay
        distance *= 2
    return (before, after, filler)


def shards(bwd_input, bwd_docs, bwd_grad, proj_weight, step_weight, step_bias, rate_log, skip_gain):
    tokens = bwd_input.shape[1]
    channels_here = bwd_input.shape[2]
    heads_here = step_bias.shape[1]
    head_width = channels_here // heads_here
    bwd_flat = bwd_input[0]
    bwd_values = bwd_flat.reshape(tokens, heads_here, head_width)
    weight_heads = step_weight[0].reshape(heads_here, head_width)
    bias_heads = step_bias[0]
    rate_heads = rate_log[0]
    skip_heads = skip_gain[0]
    docs_bwd = bwd_docs[0]
    doc_before = shifted(docs_bwd[-1:], "seq", 1)[0]
    size, mine = (lax.axis_size("seq"), lax.axis_index("seq"))
    group = lax.axis_index("head")
    own_rows = proj_weight[0]
    slot_weight = jnp.concatenate(
        [own_rows] + [rotated(own_rows, "seq", k) for k in range(1, size)], axis=0
    )
    slot_value = jnp.dot(bwd_flat, slot_weight.T, preferred_element_type=jnp.float32)
    slot_value = slot_value.reshape(tokens, size, -1)[:, ::-1].reshape(tokens, -1)
    partial_value = roll_blocks(slot_value, mine + 1, size, 1)
    group_width = partial_value.shape[1] // 2
    mine_part = lax.dynamic_slice_in_dim(partial_value, group * group_width, group_width, axis=1)
    other_part = lax.dynamic_slice_in_dim(
        partial_value, (1 - group) * group_width, group_width, axis=1
    )
    mixer_bwd = (
        mine_part + swap_heads(other_part.astype(jnp.bfloat16)).astype(jnp.float32)
    ).astype(jnp.bfloat16)
    cotangent = bwd_grad[0].reshape(tokens, heads_here, head_width)

    def summary_bwd(values_in, mixer_in, weight_in, bias_in, rate_in):
        return span_summary(values_in, mixer_in, weight_in, bias_in, rate_in, docs_bwd, doc_before)

    summary_out, summary_pull = jax.vjp(
        summary_bwd, bwd_values, mixer_bwd, weight_heads, bias_heads, rate_heads
    )
    decay_bwd, state_bwd = summary_out
    state_shape = state_bwd.shape
    state_flat = state_bwd.reshape(heads_here, -1)

    out_ct = cotangent.astype(jnp.float32)

    def local_bwd(values_in, mixer_in, weight_in, bias_in, rate_in, skip_in):
        return span_local(values_in, mixer_in, weight_in, bias_in, rate_in, skip_in, docs_bwd)

    def local_pull(*primals):
        return jax.vjp(local_bwd, *primals[:-1])[1](primals[-1])


    def carry_bwd(values_in, mixer_in, weight_in, bias_in, rate_in, state_in):
        return span_carry(
            values_in, mixer_in, weight_in, bias_in, rate_in, docs_bwd, doc_before, state_in
        )

    def carried_only(state_in):
        return carry_bwd(bwd_values, mixer_bwd, weight_heads, bias_heads, rate_heads, state_in)

    state_grad = jax.vjp(carried_only, jnp.zeros(state_shape, jnp.float32))[1](out_ct)[0]
    state_grad = state_grad.reshape(heads_here, -1)
    incoming_flat, adjoint_flat, local_grads = both_scans(
        decay_bwd,
        state_flat,
        state_grad,
        "seq",
        local_pull,
        (bwd_values, mixer_bwd, weight_heads, bias_heads, rate_heads, skip_heads, out_ct),
    )
    incoming_bwd = incoming_flat.reshape(state_shape)
    carry_grads = jax.vjp(
        carry_bwd, bwd_values, mixer_bwd, weight_heads, bias_heads, rate_heads, incoming_bwd
    )[1](out_ct)
    out_grads = (
        (local_grads[0].astype(jnp.float32) + carry_grads[0].astype(jnp.float32)),
        (local_grads[1].astype(jnp.float32) + carry_grads[1].astype(jnp.float32)),
        local_grads[2] + carry_grads[2],
        local_grads[3] + carry_grads[3],
        local_grads[4] + carry_grads[4],
        local_grads[5],
    )
    decay_grad = jnp.sum(adjoint_flat * incoming_flat, axis=1)
    sum_grads = summary_pull((decay_grad, adjoint_flat.reshape(state_shape)))
    mixer_grad = (out_grads[1].astype(jnp.float32) + sum_grads[1].astype(jnp.float32)).astype(
        jnp.bfloat16
    )
    other_grad = swap_heads(mixer_grad)
    mixer_full = jnp.where(
        group == 0,
        jnp.concatenate([mixer_grad, other_grad], axis=1),
        jnp.concatenate([other_grad, mixer_grad], axis=1),
    )
    mixer_slots = roll_blocks(mixer_full, size - 1 - mine, size, 1)
    mixer_slots = mixer_slots.reshape(tokens, size, -1)[:, ::-1].reshape(tokens, -1)
    back_proj = jnp.dot(mixer_slots, slot_weight, preferred_element_type=jnp.float32)
    value_grad = (out_grads[0].astype(jnp.float32) + sum_grads[0].astype(jnp.float32)).reshape(
        tokens, channels_here
    ) + back_proj
    value_grad = value_grad.astype(jnp.bfloat16)
    prev_part = shifted(value_grad.reshape(1, tokens, channels_here), "section", -1)
    dest_grad = roll_blocks(mixer_full, size - mine, size, 1)
    row_parts = lax.dot_general(
        dest_grad, bwd_flat, (((0,), (0,)), ((), ())), preferred_element_type=jnp.float32
    ).reshape(size, -1, channels_here)
    small = jnp.concatenate(
        [
            (out_grads[2] + sum_grads[2]).reshape(channels_here),
            out_grads[3] + sum_grads[3],
            out_grads[4] + sum_grads[4],
            out_grads[5],
        ]
    )
    count = small.shape[0]
    block_rows = row_parts.shape[1]
    small_high = small.astype(jnp.bfloat16)
    small_low = (small - small_high.astype(jnp.float32)).astype(jnp.bfloat16)
    small_cols = -(-(2 * count) // (block_rows * 128)) * 128
    small_coded = jnp.concatenate([small_high, small_low])
    small_coded = jnp.pad(small_coded, (0, block_rows * small_cols - 2 * count))
    small_coded = small_coded.reshape(block_rows, small_cols)
    grad_rows = row_parts[0]
    small_slots = [small_coded]
    for k in range(1, size):
        message = jnp.concatenate([row_parts[k].astype(jnp.bfloat16), small_coded], axis=1)
        got = rotated(message, "seq", k)
        grad_rows = grad_rows + got[:, :channels_here].astype(jnp.float32)
        small_slots.append(got[:, channels_here:])
    small_slots = jnp.stack(small_slots[::-1])
    small_slots = roll_blocks(small_slots, mine + 1, size, 0).astype(jnp.float32)
    small_slots = small_slots.reshape(size, -1)
    small_parts = small_slots[:, :count] + small_slots[:, count : 2 * count]
    small_total = small_parts[0]
    for j in range(1, size):
        small_total = small_total + small_parts[j]
    small = small_total.reshape(-1)
    totals = (
        small[:channels_here],
        small[channels_here : channels_here + heads_here],
        small[channels_here + heads_here : channels_here + 2 * heads_here],
        small[channels_here + 2 * heads_here : channels_here + 3 * heads_here],
    )
    return (
        prev_part,
        grad_rows[None],
        totals[0][None],
        totals[1][None],
        totals[2][None],
        totals[3][None],
    )


def solution(mesh):
    in_specs = (
        P("section", "seq", "head"),
        P("section", "seq"),
        P("section", "seq", "head"),
        P("section", "seq", "head"),
        P("section", "head"),
        P("section", "head"),
        P("section", "head"),
        P("section", "head"),
    )
    out_specs = (
        P("section", "seq", "head"),
        P("section", "seq", "head"),
        P("section", "head"),
        P("section", "head"),
        P("section", "head"),
        P("section", "head"),
    )
    return jax.shard_map(shards, mesh=mesh, in_specs=in_specs, out_specs=out_specs, check_vma=False)
```

```python
import jax
import jax.numpy as jnp
from jax import lax
from jax.sharding import PartitionSpec as P

EXACT = lax.Precision.HIGHEST


def shifted(block, axis, distance):
    devices = range(lax.axis_size(axis))
    route = [(i - distance, i) for i in devices if i - distance in devices]
    return lax.ppermute(block, axis, route)


def rotated(block, axis, distance):
    size = lax.axis_size(axis)
    route = [(i, (i + distance) % size) for i in range(size)]
    return lax.ppermute(block, axis, route)


def roll_blocks(value, shift, parts, dim):
    doubled = jnp.concatenate([value, value], axis=dim)
    width = value.shape[dim] // parts
    start = ((parts - shift) % parts) * width
    return lax.dynamic_slice_in_dim(doubled, start, value.shape[dim], axis=dim)


def swap_heads(block):
    return lax.ppermute(block, "head", [(0, 1), (1, 0)])


def contract(spec, left, right):
    return jnp.einsum(spec, left, right, preferred_element_type=jnp.float32)


def local_setup(values, step_weight, step_bias, rate_log):
    tokens = values.shape[0]
    raw_step = (
        jnp.einsum("thp,hp->th", values.astype(jnp.float32), step_weight, precision=EXACT)
        + step_bias[None, :]
    )
    step_size = jax.nn.softplus(raw_step)
    decay_log = -jnp.exp(rate_log)[None, :] * step_size
    row_ids = lax.broadcasted_iota(jnp.int32, (tokens, tokens), 0)
    col_ids = lax.broadcasted_iota(jnp.int32, (tokens, tokens), 1)
    triangle = (row_ids >= col_ids).astype(jnp.float32)
    cumulative = jnp.dot(triangle, decay_log, precision=EXACT)
    return (step_size, cumulative, row_ids, col_ids)


def span_summary(values, mixer, step_weight, step_bias, rate_log, docs, doc_before):
    step_size, cumulative, row_ids, col_ids = local_setup(values, step_weight, step_bias, rate_log)
    final_log = cumulative[-1]
    tail_mask = (docs == docs[-1]).astype(jnp.float32)[:, None]
    tail_weight = (
        jnp.exp(jnp.where(tail_mask > 0, final_log[None, :] - cumulative, 0.0))
        * tail_mask
        * step_size
    )
    unbroken = (docs[-1] == doc_before).astype(jnp.float32)
    carry_decay = jnp.exp(final_log) * unbroken
    half_width = mixer.shape[1] // 2
    writers = mixer[:, :half_width]
    weighted = (tail_weight[:, :, None] * writers.astype(jnp.float32)[:, None, :]).astype(
        jnp.bfloat16
    )
    span_state = contract("thn,thp->hnp", weighted, values)
    return (carry_decay, span_state)


def span_local(values, mixer, step_weight, step_bias, rate_log, skip_gain, docs):
    step_size, cumulative, row_ids, col_ids = local_setup(values, step_weight, step_bias, rate_log)
    half_width = mixer.shape[1] // 2
    writers = mixer[:, :half_width]
    readers = mixer[:, half_width:]
    affinity = jnp.dot(readers, writers.T, preferred_element_type=jnp.float32)
    same_doc = ((docs[:, None] == docs[None, :]) & (row_ids >= col_ids)).astype(jnp.float32)
    heads_first = cumulative.T
    log_gap = heads_first[:, :, None] - heads_first[:, None, :]
    mixing = (
        jnp.exp(jnp.where(same_doc[None] > 0, log_gap, 0.0))
        * same_doc[None]
        * affinity[None]
        * step_size.T[:, None, :]
    )
    mixing = mixing.astype(jnp.bfloat16)
    local_part = contract("hts,shp->thp", mixing, values)
    return values.astype(jnp.float32) * (1.0 + skip_gain)[None, :, None] + local_part


def span_carry(values, mixer, step_weight, step_bias, rate_log, docs, doc_before, incoming):
    step_size, cumulative, row_ids, col_ids = local_setup(values, step_weight, step_bias, rate_log)
    half_width = mixer.shape[1] // 2
    readers = mixer[:, half_width:]
    unbroken = (docs == doc_before).astype(jnp.float32)
    carry_scale = jnp.exp(cumulative) * unbroken[:, None]
    carried = jnp.einsum("tn,hnp->thp", readers.astype(jnp.float32), incoming, precision=EXACT)
    return carry_scale[:, :, None] * carried


def scan_rounds(decay, state, axis, forward):
    size, mine = (lax.axis_size(axis), lax.axis_index(axis))
    far_decay, far_state = (decay, state)
    near_decay = jnp.ones_like(decay)
    near_state = jnp.zeros_like(state)
    distance = 1
    while distance < size:
        got_decay, got_state = shifted(
            (far_decay, far_state.astype(jnp.bfloat16)), axis, distance if forward else -distance
        )
        got_state = got_state.astype(jnp.float32)
        near_state = near_state + near_decay[:, None] * got_state
        near_decay = near_decay * got_decay
        if distance * 2 < size:
            far_state = far_state + far_decay[:, None] * got_state
            far_decay = far_decay * got_decay
        distance *= 2
    return near_state


def both_scans(decay, state, state_grad, axis, filler_fn, filler_args):
    size, mine = (lax.axis_size(axis), lax.axis_index(axis))
    if size & (size - 1):
        return (
            scan_rounds(decay, state, axis, True),
            scan_rounds(decay, state_grad, axis, False),
            filler_fn(*filler_args),
        )
    width = state.shape[1]
    total_decay = decay
    total_fwd, total_bwd = (state, state_grad)
    before = jnp.zeros_like(state)
    before_decay = jnp.ones_like(decay)
    after = jnp.zeros_like(state_grad)
    after_decay = jnp.ones_like(decay)
    distance = 1
    while distance < size:
        high = lax.convert_element_type(total_decay.astype(jnp.bfloat16), jnp.float32)
        low = total_decay - high
        pad = jnp.zeros((decay.shape[0], 126), jnp.float32)
        payload = jnp.concatenate(
            [total_fwd, total_bwd, high[:, None], low[:, None], pad], axis=1
        ).astype(jnp.bfloat16)
        upper = (mine // distance) % 2 == 1
        if distance == 1:
            payload, filler_args = lax.optimization_barrier((payload, filler_args))
        if distance * 2 < size:
            got = lax.ppermute(payload, axis, [(i, i ^ distance) for i in range(size)])
            got = got.astype(jnp.float32)
            got_fwd = got[:, :width]
            got_bwd = got[:, width : 2 * width]
        else:
            last = jnp.where(upper, total_bwd, total_fwd).astype(jnp.bfloat16)
            last = jnp.concatenate([last, payload[:, 2 * width :]], axis=1)
            got = lax.ppermute(last, axis, [(i, i ^ distance) for i in range(size)])
            got = got.astype(jnp.float32)
            got_fwd = got[:, :width]
            got_bwd = got_fwd
            got = jnp.concatenate([got[:, :width], got], axis=1)
        if distance == min(2, size // 2):
            got, filler = lax.optimization_barrier((got, filler_fn(*filler_args)))
        got_decay = got[:, 2 * width] + got[:, 2 * width + 1]
        before = jnp.where(upper, before + before_decay[:, None] * got_fwd, before)
        before_decay = jnp.where(upper, before_decay * got_decay, before_decay)
        after = jnp.where(upper, after, after + after_decay[:, None] * got_bwd)
        after_decay = jnp.where(upper, after_decay, after_decay * got_decay)
        if distance * 2 < size:
            total_fwd = jnp.where(
                upper,
                total_fwd + total_decay[:, None] * got_fwd,
                got_fwd + got_decay[:, None] * total_fwd,
            )
            total_bwd = jnp.where(
                upper,
                got_bwd + got_decay[:, None] * total_bwd,
                total_bwd + total_decay[:, None] * got_bwd,
            )
            total_decay = total_decay * got_decay
        distance *= 2
    return (before, after, filler)


def shards(bwd_input, bwd_docs, bwd_grad, proj_weight, step_weight, step_bias, rate_log, skip_gain):
    tokens = bwd_input.shape[1]
    channels_here = bwd_input.shape[2]
    heads_here = step_bias.shape[1]
    head_width = channels_here // heads_here
    bwd_flat = bwd_input[0]
    bwd_values = bwd_flat.reshape(tokens, heads_here, head_width)
    weight_heads = step_weight[0].reshape(heads_here, head_width)
    bias_heads = step_bias[0]
    rate_heads = rate_log[0]
    skip_heads = skip_gain[0]
    docs_bwd = bwd_docs[0]
    doc_before = shifted(docs_bwd[-1:], "seq", 1)[0]
    size, mine = (lax.axis_size("seq"), lax.axis_index("seq"))
    group = lax.axis_index("head")
    own_rows = proj_weight[0]
    slot_weight = jnp.concatenate(
        [own_rows] + [rotated(own_rows, "seq", k) for k in range(1, size)], axis=0
    )
    slot_value = jnp.dot(bwd_flat, slot_weight.T, preferred_element_type=jnp.float32)
    slot_value = slot_value.reshape(tokens, size, -1)[:, ::-1].reshape(tokens, -1)
    partial_value = roll_blocks(slot_value, mine + 1, size, 1)
    group_width = partial_value.shape[1] // 2
    mine_part = lax.dynamic_slice_in_dim(partial_value, group * group_width, group_width, axis=1)
    other_part = lax.dynamic_slice_in_dim(
        partial_value, (1 - group) * group_width, group_width, axis=1
    )
    mixer_bwd = (
        mine_part + swap_heads(other_part.astype(jnp.bfloat16)).astype(jnp.float32)
    ).astype(jnp.bfloat16)
    cotangent = bwd_grad[0].reshape(tokens, heads_here, head_width)

    def summary_bwd(values_in, mixer_in, weight_in, bias_in, rate_in):
        return span_summary(values_in, mixer_in, weight_in, bias_in, rate_in, docs_bwd, doc_before)

    summary_out, summary_pull = jax.vjp(
        summary_bwd, bwd_values, mixer_bwd, weight_heads, bias_heads, rate_heads
    )
    decay_bwd, state_bwd = summary_out
    state_shape = state_bwd.shape
    state_flat = state_bwd.reshape(heads_here, -1)

    out_ct = cotangent.astype(jnp.float32)

    def local_bwd(values_in, mixer_in, weight_in, bias_in, rate_in, skip_in):
        return span_local(values_in, mixer_in, weight_in, bias_in, rate_in, skip_in, docs_bwd)

    def local_pull(*primals):
        return jax.vjp(local_bwd, *primals[:-1])[1](primals[-1])


    def carry_bwd(values_in, mixer_in, weight_in, bias_in, rate_in, state_in):
        return span_carry(
            values_in, mixer_in, weight_in, bias_in, rate_in, docs_bwd, doc_before, state_in
        )

    def carried_only(state_in):
        return carry_bwd(bwd_values, mixer_bwd, weight_heads, bias_heads, rate_heads, state_in)

    state_grad = jax.vjp(carried_only, jnp.zeros(state_shape, jnp.float32))[1](out_ct)[0]
    state_grad = state_grad.reshape(heads_here, -1)
    incoming_flat, adjoint_flat, local_grads = both_scans(
        decay_bwd,
        state_flat,
        state_grad,
        "seq",
        local_pull,
        (bwd_values, mixer_bwd, weight_heads, bias_heads, rate_heads, skip_heads, out_ct),
    )
    incoming_bwd = incoming_flat.reshape(state_shape)
    carry_grads = jax.vjp(
        carry_bwd, bwd_values, mixer_bwd, weight_heads, bias_heads, rate_heads, incoming_bwd
    )[1](out_ct)
    out_grads = (
        (local_grads[0].astype(jnp.float32) + carry_grads[0].astype(jnp.float32)),
        (local_grads[1].astype(jnp.float32) + carry_grads[1].astype(jnp.float32)),
        local_grads[2] + carry_grads[2],
        local_grads[3] + carry_grads[3],
        local_grads[4] + carry_grads[4],
        local_grads[5],
    )
    decay_grad = jnp.sum(adjoint_flat * incoming_flat, axis=1)
    sum_grads = summary_pull((decay_grad, adjoint_flat.reshape(state_shape)))
    mixer_grad = (out_grads[1].astype(jnp.float32) + sum_grads[1].astype(jnp.float32)).astype(
        jnp.bfloat16
    )
    other_grad = swap_heads(mixer_grad)
    mixer_full = jnp.where(
        group == 0,
        jnp.concatenate([mixer_grad, other_grad], axis=1),
        jnp.concatenate([other_grad, mixer_grad], axis=1),
    )
    mixer_slots = roll_blocks(mixer_full, size - 1 - mine, size, 1)
    mixer_slots = mixer_slots.reshape(tokens, size, -1)[:, ::-1].reshape(tokens, -1)
    back_proj = jnp.dot(mixer_slots, slot_weight, preferred_element_type=jnp.float32)
    value_grad = (out_grads[0].astype(jnp.float32) + sum_grads[0].astype(jnp.float32)).reshape(
        tokens, channels_here
    ) + back_proj
    value_grad = value_grad.astype(jnp.bfloat16)
    prev_part = shifted(value_grad.reshape(1, tokens, channels_here), "section", -1)
    dest_grad = roll_blocks(mixer_full, size - mine, size, 1)
    row_parts = lax.dot_general(
        dest_grad, bwd_flat, (((0,), (0,)), ((), ())), preferred_element_type=jnp.float32
    ).reshape(size, -1, channels_here)
    small = jnp.concatenate(
        [
            (out_grads[2] + sum_grads[2]).reshape(channels_here),
            out_grads[3] + sum_grads[3],
            out_grads[4] + sum_grads[4],
            out_grads[5],
        ]
    )
    count = small.shape[0]
    block_rows = row_parts.shape[1]
    small_high = small.astype(jnp.bfloat16)
    small_low = (small - small_high.astype(jnp.float32)).astype(jnp.bfloat16)
    small_cols = -(-(2 * count) // (block_rows * 128)) * 128
    small_coded = jnp.concatenate([small_high, small_low])
    small_coded = jnp.pad(small_coded, (0, block_rows * small_cols - 2 * count))
    small_coded = small_coded.reshape(block_rows, small_cols)
    grad_rows = row_parts[0]
    small_slots = [small_coded]
    for k in range(1, size):
        message = jnp.concatenate([row_parts[k].astype(jnp.bfloat16), small_coded], axis=1)
        got = rotated(message, "seq", k)
        grad_rows = grad_rows + got[:, :channels_here].astype(jnp.float32)
        small_slots.append(got[:, channels_here:])
    small_slots = jnp.stack(small_slots[::-1])
    small_slots = roll_blocks(small_slots, mine + 1, size, 0).astype(jnp.float32)
    small_slots = small_slots.reshape(size, -1)
    small_parts = small_slots[:, :count] + small_slots[:, count : 2 * count]
    small_total = small_parts[0]
    for j in range(1, size):
        small_total = small_total + small_parts[j]
    small = small_total.reshape(-1)
    totals = (
        small[:channels_here],
        small[channels_here : channels_here + heads_here],
        small[channels_here + heads_here : channels_here + 2 * heads_here],
        small[channels_here + 2 * heads_here : channels_here + 3 * heads_here],
    )
    return (
        prev_part,
        grad_rows[None],
        totals[0][None],
        totals[1][None],
        totals[2][None],
        totals[3][None],
    )


def solution(mesh):
    in_specs = (
        P("section", "seq", "head"),
        P("section", "seq"),
        P("section", "seq", "head"),
        P("section", "seq", "head"),
        P("section", "head"),
        P("section", "head"),
        P("section", "head"),
        P("section", "head"),
    )
    out_specs = (
        P("section", "seq", "head"),
        P("section", "seq", "head"),
        P("section", "head"),
        P("section", "head"),
        P("section", "head"),
        P("section", "head"),
    )
    return jax.shard_map(shards, mesh=mesh, in_specs=in_specs, out_specs=out_specs, check_vma=False)
```

```python
import jax
import jax.numpy as jnp
from jax import lax
from jax.sharding import PartitionSpec as P

EXACT = lax.Precision.HIGHEST


def shifted(block, axis, distance):
    devices = range(lax.axis_size(axis))
    route = [(i - distance, i) for i in devices if i - distance in devices]
    return lax.ppermute(block, axis, route)


def rotated(block, axis, distance):
    size = lax.axis_size(axis)
    route = [(i, (i + distance) % size) for i in range(size)]
    return lax.ppermute(block, axis, route)


def roll_blocks(value, shift, parts, dim):
    doubled = jnp.concatenate([value, value], axis=dim)
    width = value.shape[dim] // parts
    start = ((parts - shift) % parts) * width
    return lax.dynamic_slice_in_dim(doubled, start, value.shape[dim], axis=dim)


def swap_heads(block):
    return lax.ppermute(block, "head", [(0, 1), (1, 0)])


def contract(spec, left, right):
    return jnp.einsum(spec, left, right, preferred_element_type=jnp.float32)


def local_setup(values, step_weight, step_bias, rate_log):
    tokens = values.shape[0]
    raw_step = (
        jnp.einsum("thp,hp->th", values.astype(jnp.float32), step_weight, precision=EXACT)
        + step_bias[None, :]
    )
    step_size = jax.nn.softplus(raw_step)
    decay_log = -jnp.exp(rate_log)[None, :] * step_size
    row_ids = lax.broadcasted_iota(jnp.int32, (tokens, tokens), 0)
    col_ids = lax.broadcasted_iota(jnp.int32, (tokens, tokens), 1)
    triangle = (row_ids >= col_ids).astype(jnp.float32)
    cumulative = jnp.dot(triangle, decay_log, precision=EXACT)
    return (step_size, cumulative, row_ids, col_ids)


def span_summary(values, mixer, step_weight, step_bias, rate_log, docs, doc_before):
    step_size, cumulative, row_ids, col_ids = local_setup(values, step_weight, step_bias, rate_log)
    final_log = cumulative[-1]
    tail_mask = (docs == docs[-1]).astype(jnp.float32)[:, None]
    tail_weight = (
        jnp.exp(jnp.where(tail_mask > 0, final_log[None, :] - cumulative, 0.0))
        * tail_mask
        * step_size
    )
    unbroken = (docs[-1] == doc_before).astype(jnp.float32)
    carry_decay = jnp.exp(final_log) * unbroken
    half_width = mixer.shape[1] // 2
    writers = mixer[:, :half_width]
    weighted = (tail_weight[:, :, None] * writers.astype(jnp.float32)[:, None, :]).astype(
        jnp.bfloat16
    )
    span_state = contract("thn,thp->hnp", weighted, values)
    return (carry_decay, span_state)


def span_local(values, mixer, step_weight, step_bias, rate_log, skip_gain, docs):
    step_size, cumulative, row_ids, col_ids = local_setup(values, step_weight, step_bias, rate_log)
    half_width = mixer.shape[1] // 2
    writers = mixer[:, :half_width]
    readers = mixer[:, half_width:]
    affinity = jnp.dot(readers, writers.T, preferred_element_type=jnp.float32)
    same_doc = ((docs[:, None] == docs[None, :]) & (row_ids >= col_ids)).astype(jnp.float32)
    heads_first = cumulative.T
    log_gap = heads_first[:, :, None] - heads_first[:, None, :]
    mixing = (
        jnp.exp(jnp.where(same_doc[None] > 0, log_gap, 0.0))
        * same_doc[None]
        * affinity[None]
        * step_size.T[:, None, :]
    )
    mixing = mixing.astype(jnp.bfloat16)
    local_part = contract("hts,shp->thp", mixing, values)
    return values.astype(jnp.float32) * (1.0 + skip_gain)[None, :, None] + local_part


def span_carry(values, mixer, step_weight, step_bias, rate_log, docs, doc_before, incoming):
    step_size, cumulative, row_ids, col_ids = local_setup(values, step_weight, step_bias, rate_log)
    half_width = mixer.shape[1] // 2
    readers = mixer[:, half_width:]
    unbroken = (docs == doc_before).astype(jnp.float32)
    carry_scale = jnp.exp(cumulative) * unbroken[:, None]
    carried = jnp.einsum("tn,hnp->thp", readers.astype(jnp.float32), incoming, precision=EXACT)
    return carry_scale[:, :, None] * carried


def scan_rounds(decay, state, axis, forward):
    size, mine = (lax.axis_size(axis), lax.axis_index(axis))
    far_decay, far_state = (decay, state)
    near_decay = jnp.ones_like(decay)
    near_state = jnp.zeros_like(state)
    distance = 1
    while distance < size:
        got_decay, got_state = shifted(
            (far_decay, far_state.astype(jnp.bfloat16)), axis, distance if forward else -distance
        )
        got_state = got_state.astype(jnp.float32)
        near_state = near_state + near_decay[:, None] * got_state
        near_decay = near_decay * got_decay
        if distance * 2 < size:
            far_state = far_state + far_decay[:, None] * got_state
            far_decay = far_decay * got_decay
        distance *= 2
    return near_state


def both_scans(decay, state, state_grad, axis, filler_fn, filler_args):
    size, mine = (lax.axis_size(axis), lax.axis_index(axis))
    if size & (size - 1):
        return (
            scan_rounds(decay, state, axis, True),
            scan_rounds(decay, state_grad, axis, False),
            filler_fn(*filler_args),
        )
    width = state.shape[1]
    total_decay = decay
    total_fwd, total_bwd = (state, state_grad)
    before = jnp.zeros_like(state)
    before_decay = jnp.ones_like(decay)
    after = jnp.zeros_like(state_grad)
    after_decay = jnp.ones_like(decay)
    distance = 1
    while distance < size:
        high = lax.convert_element_type(total_decay.astype(jnp.bfloat16), jnp.float32)
        low = total_decay - high
        pad = jnp.zeros((decay.shape[0], 126), jnp.float32)
        payload = jnp.concatenate(
            [total_fwd, total_bwd, high[:, None], low[:, None], pad], axis=1
        ).astype(jnp.bfloat16)
        upper = (mine // distance) % 2 == 1
        if distance == 1:
            payload, filler_args = lax.optimization_barrier((payload, filler_args))
        if distance * 2 < size:
            got = lax.ppermute(payload, axis, [(i, i ^ distance) for i in range(size)])
            at = 2 * width
        else:
            last = jnp.where(upper, total_bwd, total_fwd).astype(jnp.bfloat16)
            last = jnp.concatenate([last, payload[:, 2 * width :]], axis=1)
            got = lax.ppermute(last, axis, [(i, i ^ distance) for i in range(size)])
            at = width
        if distance == 1:
            got, filler = lax.optimization_barrier((got, filler_fn(*filler_args)))
        got_fwd = got[:, :width].astype(jnp.float32)
        got_bwd = got[:, at - width : at].astype(jnp.float32)
        got_decay = got[:, at].astype(jnp.float32) + got[:, at + 1].astype(jnp.float32)
        before = jnp.where(upper, before + before_decay[:, None] * got_fwd, before)
        before_decay = jnp.where(upper, before_decay * got_decay, before_decay)
        after = jnp.where(upper, after, after + after_decay[:, None] * got_bwd)
        after_decay = jnp.where(upper, after_decay, after_decay * got_decay)
        if distance * 2 < size:
            total_fwd = jnp.where(
                upper,
                total_fwd + total_decay[:, None] * got_fwd,
                got_fwd + got_decay[:, None] * total_fwd,
            )
            total_bwd = jnp.where(
                upper,
                got_bwd + got_decay[:, None] * total_bwd,
                total_bwd + total_decay[:, None] * got_bwd,
            )
            total_decay = total_decay * got_decay
        distance *= 2
    return (before, after, filler)


def shards(bwd_input, bwd_docs, bwd_grad, proj_weight, step_weight, step_bias, rate_log, skip_gain):
    tokens = bwd_input.shape[1]
    channels_here = bwd_input.shape[2]
    heads_here = step_bias.shape[1]
    head_width = channels_here // heads_here
    bwd_flat = bwd_input[0]
    bwd_values = bwd_flat.reshape(tokens, heads_here, head_width)
    weight_heads = step_weight[0].reshape(heads_here, head_width)
    bias_heads = step_bias[0]
    rate_heads = rate_log[0]
    skip_heads = skip_gain[0]
    docs_bwd = bwd_docs[0]
    doc_before = shifted(docs_bwd[-1:], "seq", 1)[0]
    size, mine = (lax.axis_size("seq"), lax.axis_index("seq"))
    group = lax.axis_index("head")
    own_rows = proj_weight[0]
    slot_weight = jnp.concatenate(
        [own_rows] + [rotated(own_rows, "seq", k) for k in range(1, size)], axis=0
    )
    slot_value = jnp.dot(bwd_flat, slot_weight.T, preferred_element_type=jnp.float32)
    slot_value = slot_value.reshape(tokens, size, -1)[:, ::-1].reshape(tokens, -1)
    partial_value = roll_blocks(slot_value, mine + 1, size, 1)
    group_width = partial_value.shape[1] // 2
    mine_part = lax.dynamic_slice_in_dim(partial_value, group * group_width, group_width, axis=1)
    other_part = lax.dynamic_slice_in_dim(
        partial_value, (1 - group) * group_width, group_width, axis=1
    )
    mixer_bwd = (
        mine_part + swap_heads(other_part.astype(jnp.bfloat16)).astype(jnp.float32)
    ).astype(jnp.bfloat16)
    cotangent = bwd_grad[0].reshape(tokens, heads_here, head_width)

    def summary_bwd(values_in, mixer_in, weight_in, bias_in, rate_in):
        return span_summary(values_in, mixer_in, weight_in, bias_in, rate_in, docs_bwd, doc_before)

    summary_out, summary_pull = jax.vjp(
        summary_bwd, bwd_values, mixer_bwd, weight_heads, bias_heads, rate_heads
    )
    decay_bwd, state_bwd = summary_out
    state_shape = state_bwd.shape
    state_flat = state_bwd.reshape(heads_here, -1)

    out_ct = cotangent.astype(jnp.float32)

    def local_bwd(values_in, mixer_in, weight_in, bias_in, rate_in, skip_in):
        return span_local(values_in, mixer_in, weight_in, bias_in, rate_in, skip_in, docs_bwd)

    def local_pull(*primals):
        return jax.vjp(local_bwd, *primals[:-1])[1](primals[-1])


    def carry_bwd(values_in, mixer_in, weight_in, bias_in, rate_in, state_in):
        return span_carry(
            values_in, mixer_in, weight_in, bias_in, rate_in, docs_bwd, doc_before, state_in
        )

    def carried_only(state_in):
        return carry_bwd(bwd_values, mixer_bwd, weight_heads, bias_heads, rate_heads, state_in)

    state_grad = jax.vjp(carried_only, jnp.zeros(state_shape, jnp.float32))[1](out_ct)[0]
    state_grad = state_grad.reshape(heads_here, -1)
    incoming_flat, adjoint_flat, local_grads = both_scans(
        decay_bwd,
        state_flat,
        state_grad,
        "seq",
        local_pull,
        (bwd_values, mixer_bwd, weight_heads, bias_heads, rate_heads, skip_heads, out_ct),
    )
    incoming_bwd = incoming_flat.reshape(state_shape)
    carry_grads = jax.vjp(
        carry_bwd, bwd_values, mixer_bwd, weight_heads, bias_heads, rate_heads, incoming_bwd
    )[1](out_ct)
    out_grads = (
        (local_grads[0].astype(jnp.float32) + carry_grads[0].astype(jnp.float32)),
        (local_grads[1].astype(jnp.float32) + carry_grads[1].astype(jnp.float32)),
        local_grads[2] + carry_grads[2],
        local_grads[3] + carry_grads[3],
        local_grads[4] + carry_grads[4],
        local_grads[5],
    )
    decay_grad = jnp.sum(adjoint_flat * incoming_flat, axis=1)
    sum_grads = summary_pull((decay_grad, adjoint_flat.reshape(state_shape)))
    mixer_grad = (out_grads[1].astype(jnp.float32) + sum_grads[1].astype(jnp.float32)).astype(
        jnp.bfloat16
    )
    other_grad = swap_heads(mixer_grad)
    mixer_full = jnp.where(
        group == 0,
        jnp.concatenate([mixer_grad, other_grad], axis=1),
        jnp.concatenate([other_grad, mixer_grad], axis=1),
    )
    mixer_slots = roll_blocks(mixer_full, size - 1 - mine, size, 1)
    mixer_slots = mixer_slots.reshape(tokens, size, -1)[:, ::-1].reshape(tokens, -1)
    back_proj = jnp.dot(mixer_slots, slot_weight, preferred_element_type=jnp.float32)
    value_grad = (out_grads[0].astype(jnp.float32) + sum_grads[0].astype(jnp.float32)).reshape(
        tokens, channels_here
    ) + back_proj
    value_grad = value_grad.astype(jnp.bfloat16)
    prev_part = shifted(value_grad.reshape(1, tokens, channels_here), "section", -1)
    dest_grad = roll_blocks(mixer_full, size - mine, size, 1)
    row_parts = lax.dot_general(
        dest_grad, bwd_flat, (((0,), (0,)), ((), ())), preferred_element_type=jnp.float32
    ).reshape(size, -1, channels_here)
    small = jnp.concatenate(
        [
            (out_grads[2] + sum_grads[2]).reshape(channels_here),
            out_grads[3] + sum_grads[3],
            out_grads[4] + sum_grads[4],
            out_grads[5],
        ]
    )
    count = small.shape[0]
    block_rows = row_parts.shape[1]
    small_high = small.astype(jnp.bfloat16)
    small_low = (small - small_high.astype(jnp.float32)).astype(jnp.bfloat16)
    small_cols = -(-(2 * count) // (block_rows * 128)) * 128
    small_coded = jnp.concatenate([small_high, small_low])
    small_coded = jnp.pad(small_coded, (0, block_rows * small_cols - 2 * count))
    small_coded = small_coded.reshape(block_rows, small_cols)
    grad_rows = row_parts[0]
    small_slots = [small_coded]
    for k in range(1, size):
        message = jnp.concatenate([row_parts[k].astype(jnp.bfloat16), small_coded], axis=1)
        got = rotated(message, "seq", k)
        grad_rows = grad_rows + got[:, :channels_here].astype(jnp.float32)
        small_slots.append(got[:, channels_here:])
    small_slots = jnp.stack(small_slots[::-1])
    small_slots = roll_blocks(small_slots, mine + 1, size, 0).astype(jnp.float32)
    small_slots = small_slots.reshape(size, -1)
    small_parts = small_slots[:, :count] + small_slots[:, count : 2 * count]
    small_total = small_parts[0]
    for j in range(1, size):
        small_total = small_total + small_parts[j]
    small = small_total.reshape(-1)
    totals = (
        small[:channels_here],
        small[channels_here : channels_here + heads_here],
        small[channels_here + heads_here : channels_here + 2 * heads_here],
        small[channels_here + 2 * heads_here : channels_here + 3 * heads_here],
    )
    return (
        prev_part,
        grad_rows[None],
        totals[0][None],
        totals[1][None],
        totals[2][None],
        totals[3][None],
    )


def solution(mesh):
    in_specs = (
        P("section", "seq", "head"),
        P("section", "seq"),
        P("section", "seq", "head"),
        P("section", "seq", "head"),
        P("section", "head"),
        P("section", "head"),
        P("section", "head"),
        P("section", "head"),
    )
    out_specs = (
        P("section", "seq", "head"),
        P("section", "seq", "head"),
        P("section", "head"),
        P("section", "head"),
        P("section", "head"),
        P("section", "head"),
    )
    return jax.shard_map(shards, mesh=mesh, in_specs=in_specs, out_specs=out_specs, check_vma=False)
```

```python
import jax
import jax.numpy as jnp
from jax import lax
from jax.sharding import PartitionSpec as P

EXACT = lax.Precision.HIGHEST


def shifted(block, axis, distance):
    devices = range(lax.axis_size(axis))
    route = [(i - distance, i) for i in devices if i - distance in devices]
    return lax.ppermute(block, axis, route)


def rotated(block, axis, distance):
    size = lax.axis_size(axis)
    route = [(i, (i + distance) % size) for i in range(size)]
    return lax.ppermute(block, axis, route)


def roll_blocks(value, shift, parts, dim):
    doubled = jnp.concatenate([value, value], axis=dim)
    width = value.shape[dim] // parts
    start = ((parts - shift) % parts) * width
    return lax.dynamic_slice_in_dim(doubled, start, value.shape[dim], axis=dim)


def swap_heads(block):
    return lax.ppermute(block, "head", [(0, 1), (1, 0)])


def contract(spec, left, right):
    return jnp.einsum(spec, left, right, preferred_element_type=jnp.float32)


def local_setup(values, step_weight, step_bias, rate_log):
    tokens = values.shape[0]
    raw_step = (
        jnp.einsum("thp,hp->th", values.astype(jnp.float32), step_weight, precision=EXACT)
        + step_bias[None, :]
    )
    step_size = jax.nn.softplus(raw_step)
    decay_log = -jnp.exp(rate_log)[None, :] * step_size
    row_ids = lax.broadcasted_iota(jnp.int32, (tokens, tokens), 0)
    col_ids = lax.broadcasted_iota(jnp.int32, (tokens, tokens), 1)
    triangle = (row_ids >= col_ids).astype(jnp.float32)
    cumulative = jnp.dot(triangle, decay_log, precision=EXACT)
    return (step_size, cumulative, row_ids, col_ids)


def span_summary(values, mixer, step_weight, step_bias, rate_log, docs, doc_before):
    step_size, cumulative, row_ids, col_ids = local_setup(values, step_weight, step_bias, rate_log)
    final_log = cumulative[-1]
    tail_mask = (docs == docs[-1]).astype(jnp.float32)[:, None]
    tail_weight = (
        jnp.exp(jnp.where(tail_mask > 0, final_log[None, :] - cumulative, 0.0))
        * tail_mask
        * step_size
    )
    unbroken = (docs[-1] == doc_before).astype(jnp.float32)
    carry_decay = jnp.exp(final_log) * unbroken
    half_width = mixer.shape[1] // 2
    writers = mixer[:, :half_width]
    weighted = (tail_weight[:, :, None] * writers.astype(jnp.float32)[:, None, :]).astype(
        jnp.bfloat16
    )
    span_state = contract("thn,thp->hnp", weighted, values)
    return (carry_decay, span_state)


def span_local(values, mixer, step_weight, step_bias, rate_log, skip_gain, docs):
    step_size, cumulative, row_ids, col_ids = local_setup(values, step_weight, step_bias, rate_log)
    half_width = mixer.shape[1] // 2
    writers = mixer[:, :half_width]
    readers = mixer[:, half_width:]
    affinity = jnp.dot(readers, writers.T, preferred_element_type=jnp.float32)
    same_doc = ((docs[:, None] == docs[None, :]) & (row_ids >= col_ids)).astype(jnp.float32)
    heads_first = cumulative.T
    log_gap = heads_first[:, :, None] - heads_first[:, None, :]
    mixing = (
        jnp.exp(jnp.where(same_doc[None] > 0, log_gap, 0.0))
        * same_doc[None]
        * affinity[None]
        * step_size.T[:, None, :]
    )
    mixing = mixing.astype(jnp.bfloat16)
    local_part = contract("hts,shp->thp", mixing, values)
    return values.astype(jnp.float32) * (1.0 + skip_gain)[None, :, None] + local_part


def span_carry(values, mixer, step_weight, step_bias, rate_log, docs, doc_before, incoming):
    step_size, cumulative, row_ids, col_ids = local_setup(values, step_weight, step_bias, rate_log)
    half_width = mixer.shape[1] // 2
    readers = mixer[:, half_width:]
    unbroken = (docs == doc_before).astype(jnp.float32)
    carry_scale = jnp.exp(cumulative) * unbroken[:, None]
    carried = jnp.einsum("tn,hnp->thp", readers.astype(jnp.float32), incoming, precision=EXACT)
    return carry_scale[:, :, None] * carried


def scan_rounds(decay, state, axis, forward):
    size, mine = (lax.axis_size(axis), lax.axis_index(axis))
    far_decay, far_state = (decay, state)
    near_decay = jnp.ones_like(decay)
    near_state = jnp.zeros_like(state)
    distance = 1
    while distance < size:
        got_decay, got_state = shifted(
            (far_decay, far_state.astype(jnp.bfloat16)), axis, distance if forward else -distance
        )
        got_state = got_state.astype(jnp.float32)
        near_state = near_state + near_decay[:, None] * got_state
        near_decay = near_decay * got_decay
        if distance * 2 < size:
            far_state = far_state + far_decay[:, None] * got_state
            far_decay = far_decay * got_decay
        distance *= 2
    return near_state


def both_scans(decay, state, state_grad, axis, filler_fn, filler_args):
    size, mine = (lax.axis_size(axis), lax.axis_index(axis))
    if size & (size - 1):
        return (
            scan_rounds(decay, state, axis, True),
            scan_rounds(decay, state_grad, axis, False),
            filler_fn(*filler_args),
        )
    width = state.shape[1]
    total_decay = decay
    total_fwd, total_bwd = (state, state_grad)
    before = jnp.zeros_like(state)
    before_decay = jnp.ones_like(decay)
    after = jnp.zeros_like(state_grad)
    after_decay = jnp.ones_like(decay)
    distance = 1
    while distance < size:
        high = lax.convert_element_type(total_decay.astype(jnp.bfloat16), jnp.float32)
        low = total_decay - high
        pad = jnp.zeros((decay.shape[0], 126), jnp.float32)
        payload = jnp.concatenate(
            [total_fwd, total_bwd, high[:, None], low[:, None], pad], axis=1
        ).astype(jnp.bfloat16)
        upper = (mine // distance) % 2 == 1
        if distance == 1:
            payload, filler_args = lax.optimization_barrier((payload, filler_args))
        if distance * 2 < size:
            got = lax.ppermute(payload, axis, [(i, i ^ distance) for i in range(size)])
            got = got.astype(jnp.float32)
            got_fwd = got[:, :width]
            got_bwd = got[:, width : 2 * width]
        else:
            last = jnp.where(upper, total_bwd, total_fwd).astype(jnp.bfloat16)
            last = jnp.concatenate([last, payload[:, 2 * width :]], axis=1)
            got = lax.ppermute(last, axis, [(i, i ^ distance) for i in range(size)])
            got = got.astype(jnp.float32)
            got_fwd = got[:, :width]
            got_bwd = got_fwd
        at = 2 * width if distance * 2 < size else width
        if distance == 1:
            got, filler = lax.optimization_barrier((got, filler_fn(*filler_args)))
        got_decay = got[:, at] + got[:, at + 1]
        before = jnp.where(upper, before + before_decay[:, None] * got_fwd, before)
        before_decay = jnp.where(upper, before_decay * got_decay, before_decay)
        after = jnp.where(upper, after, after + after_decay[:, None] * got_bwd)
        after_decay = jnp.where(upper, after_decay, after_decay * got_decay)
        if distance * 2 < size:
            total_fwd = jnp.where(
                upper,
                total_fwd + total_decay[:, None] * got_fwd,
                got_fwd + got_decay[:, None] * total_fwd,
            )
            total_bwd = jnp.where(
                upper,
                got_bwd + got_decay[:, None] * total_bwd,
                total_bwd + total_decay[:, None] * got_bwd,
            )
            total_decay = total_decay * got_decay
        distance *= 2
    return (before, after, filler)


def shards(bwd_input, bwd_docs, bwd_grad, proj_weight, step_weight, step_bias, rate_log, skip_gain):
    tokens = bwd_input.shape[1]
    channels_here = bwd_input.shape[2]
    heads_here = step_bias.shape[1]
    head_width = channels_here // heads_here
    bwd_flat = bwd_input[0]
    bwd_values = bwd_flat.reshape(tokens, heads_here, head_width)
    weight_heads = step_weight[0].reshape(heads_here, head_width)
    bias_heads = step_bias[0]
    rate_heads = rate_log[0]
    skip_heads = skip_gain[0]
    docs_bwd = bwd_docs[0]
    doc_before = shifted(docs_bwd[-1:], "seq", 1)[0]
    size, mine = (lax.axis_size("seq"), lax.axis_index("seq"))
    group = lax.axis_index("head")
    own_rows = proj_weight[0]
    slot_weight = jnp.concatenate(
        [own_rows] + [rotated(own_rows, "seq", k) for k in range(1, size)], axis=0
    )
    slot_value = jnp.dot(bwd_flat, slot_weight.T, preferred_element_type=jnp.float32)
    slot_value = slot_value.reshape(tokens, size, -1)[:, ::-1].reshape(tokens, -1)
    partial_value = roll_blocks(slot_value, mine + 1, size, 1)
    group_width = partial_value.shape[1] // 2
    mine_part = lax.dynamic_slice_in_dim(partial_value, group * group_width, group_width, axis=1)
    other_part = lax.dynamic_slice_in_dim(
        partial_value, (1 - group) * group_width, group_width, axis=1
    )
    mixer_bwd = (
        mine_part + swap_heads(other_part.astype(jnp.bfloat16)).astype(jnp.float32)
    ).astype(jnp.bfloat16)
    cotangent = bwd_grad[0].reshape(tokens, heads_here, head_width)

    def summary_bwd(values_in, mixer_in, weight_in, bias_in, rate_in):
        return span_summary(values_in, mixer_in, weight_in, bias_in, rate_in, docs_bwd, doc_before)

    summary_out, summary_pull = jax.vjp(
        summary_bwd, bwd_values, mixer_bwd, weight_heads, bias_heads, rate_heads
    )
    decay_bwd, state_bwd = summary_out
    state_shape = state_bwd.shape
    state_flat = state_bwd.reshape(heads_here, -1)

    out_ct = cotangent.astype(jnp.float32)

    def local_bwd(values_in, mixer_in, weight_in, bias_in, rate_in, skip_in):
        return span_local(values_in, mixer_in, weight_in, bias_in, rate_in, skip_in, docs_bwd)

    def local_pull(*primals):
        return jax.vjp(local_bwd, *primals[:-1])[1](primals[-1])


    def carry_bwd(values_in, mixer_in, weight_in, bias_in, rate_in, state_in):
        return span_carry(
            values_in, mixer_in, weight_in, bias_in, rate_in, docs_bwd, doc_before, state_in
        )

    def carried_only(state_in):
        return carry_bwd(bwd_values, mixer_bwd, weight_heads, bias_heads, rate_heads, state_in)

    state_grad = jax.vjp(carried_only, jnp.zeros(state_shape, jnp.float32))[1](out_ct)[0]
    state_grad = state_grad.reshape(heads_here, -1)
    incoming_flat, adjoint_flat, local_grads = both_scans(
        decay_bwd,
        state_flat,
        state_grad,
        "seq",
        local_pull,
        (bwd_values, mixer_bwd, weight_heads, bias_heads, rate_heads, skip_heads, out_ct),
    )
    incoming_bwd = incoming_flat.reshape(state_shape)
    carry_grads = jax.vjp(
        carry_bwd, bwd_values, mixer_bwd, weight_heads, bias_heads, rate_heads, incoming_bwd
    )[1](out_ct)
    out_grads = (
        (local_grads[0].astype(jnp.float32) + carry_grads[0].astype(jnp.float32)),
        (local_grads[1].astype(jnp.float32) + carry_grads[1].astype(jnp.float32)),
        local_grads[2] + carry_grads[2],
        local_grads[3] + carry_grads[3],
        local_grads[4] + carry_grads[4],
        local_grads[5],
    )
    decay_grad = jnp.sum(adjoint_flat * incoming_flat, axis=1)
    sum_grads = summary_pull((decay_grad, adjoint_flat.reshape(state_shape)))
    mixer_grad = (out_grads[1].astype(jnp.float32) + sum_grads[1].astype(jnp.float32)).astype(
        jnp.bfloat16
    )
    other_grad = swap_heads(mixer_grad)
    mixer_full = jnp.where(
        group == 0,
        jnp.concatenate([mixer_grad, other_grad], axis=1),
        jnp.concatenate([other_grad, mixer_grad], axis=1),
    )
    mixer_slots = roll_blocks(mixer_full, size - 1 - mine, size, 1)
    mixer_slots = mixer_slots.reshape(tokens, size, -1)[:, ::-1].reshape(tokens, -1)
    back_proj = jnp.dot(mixer_slots, slot_weight, preferred_element_type=jnp.float32)
    value_grad = (out_grads[0].astype(jnp.float32) + sum_grads[0].astype(jnp.float32)).reshape(
        tokens, channels_here
    ) + back_proj
    value_grad = value_grad.astype(jnp.bfloat16)
    prev_part = shifted(value_grad.reshape(1, tokens, channels_here), "section", -1)
    dest_grad = roll_blocks(mixer_full, size - mine, size, 1)
    row_parts = lax.dot_general(
        dest_grad, bwd_flat, (((0,), (0,)), ((), ())), preferred_element_type=jnp.float32
    ).reshape(size, -1, channels_here)
    small = jnp.concatenate(
        [
            (out_grads[2] + sum_grads[2]).reshape(channels_here),
            out_grads[3] + sum_grads[3],
            out_grads[4] + sum_grads[4],
            out_grads[5],
        ]
    )
    count = small.shape[0]
    block_rows = row_parts.shape[1]
    small_high = small.astype(jnp.bfloat16)
    small_low = (small - small_high.astype(jnp.float32)).astype(jnp.bfloat16)
    small_cols = -(-(2 * count) // (block_rows * 128)) * 128
    small_coded = jnp.concatenate([small_high, small_low])
    small_coded = jnp.pad(small_coded, (0, block_rows * small_cols - 2 * count))
    small_coded = small_coded.reshape(block_rows, small_cols)
    grad_rows = row_parts[0]
    small_slots = [small_coded]
    for k in range(1, size):
        message = jnp.concatenate([row_parts[k].astype(jnp.bfloat16), small_coded], axis=1)
        got = rotated(message, "seq", k)
        grad_rows = grad_rows + got[:, :channels_here].astype(jnp.float32)
        small_slots.append(got[:, channels_here:])
    small_slots = jnp.stack(small_slots[::-1])
    small_slots = roll_blocks(small_slots, mine + 1, size, 0).astype(jnp.float32)
    small_slots = small_slots.reshape(size, -1)
    small_parts = small_slots[:, :count] + small_slots[:, count : 2 * count]
    small_total = small_parts[0]
    for j in range(1, size):
        small_total = small_total + small_parts[j]
    small = small_total.reshape(-1)
    totals = (
        small[:channels_here],
        small[channels_here : channels_here + heads_here],
        small[channels_here + heads_here : channels_here + 2 * heads_here],
        small[channels_here + 2 * heads_here : channels_here + 3 * heads_here],
    )
    return (
        prev_part,
        grad_rows[None],
        totals[0][None],
        totals[1][None],
        totals[2][None],
        totals[3][None],
    )


def solution(mesh):
    in_specs = (
        P("section", "seq", "head"),
        P("section", "seq"),
        P("section", "seq", "head"),
        P("section", "seq", "head"),
        P("section", "head"),
        P("section", "head"),
        P("section", "head"),
        P("section", "head"),
    )
    out_specs = (
        P("section", "seq", "head"),
        P("section", "seq", "head"),
        P("section", "head"),
        P("section", "head"),
        P("section", "head"),
        P("section", "head"),
    )
    return jax.shard_map(shards, mesh=mesh, in_specs=in_specs, out_specs=out_specs, check_vma=False)
```

```python
import jax
import jax.numpy as jnp
from jax import lax
from jax.sharding import PartitionSpec as P

EXACT = lax.Precision.HIGHEST


def shifted(block, axis, distance):
    devices = range(lax.axis_size(axis))
    route = [(i - distance, i) for i in devices if i - distance in devices]
    return lax.ppermute(block, axis, route)


def rotated(block, axis, distance):
    size = lax.axis_size(axis)
    route = [(i, (i + distance) % size) for i in range(size)]
    return lax.ppermute(block, axis, route)


def roll_blocks(value, shift, parts, dim):
    doubled = jnp.concatenate([value, value], axis=dim)
    width = value.shape[dim] // parts
    start = ((parts - shift) % parts) * width
    return lax.dynamic_slice_in_dim(doubled, start, value.shape[dim], axis=dim)


def swap_heads(block):
    return lax.ppermute(block, "head", [(0, 1), (1, 0)])


def contract(spec, left, right):
    return jnp.einsum(spec, left, right, preferred_element_type=jnp.float32)


def local_setup(values, step_weight, step_bias, rate_log):
    tokens = values.shape[0]
    raw_step = (
        jnp.einsum("thp,hp->th", values.astype(jnp.float32), step_weight, precision=EXACT)
        + step_bias[None, :]
    )
    step_size = jax.nn.softplus(raw_step)
    decay_log = -jnp.exp(rate_log)[None, :] * step_size
    row_ids = lax.broadcasted_iota(jnp.int32, (tokens, tokens), 0)
    col_ids = lax.broadcasted_iota(jnp.int32, (tokens, tokens), 1)
    triangle = (row_ids >= col_ids).astype(jnp.float32)
    cumulative = jnp.dot(triangle, decay_log, precision=EXACT)
    return (step_size, cumulative, row_ids, col_ids)


def span_summary(values, mixer, step_weight, step_bias, rate_log, docs, doc_before):
    step_size, cumulative, row_ids, col_ids = local_setup(values, step_weight, step_bias, rate_log)
    final_log = cumulative[-1]
    tail_mask = (docs == docs[-1]).astype(jnp.float32)[:, None]
    tail_weight = (
        jnp.exp(jnp.where(tail_mask > 0, final_log[None, :] - cumulative, 0.0))
        * tail_mask
        * step_size
    )
    unbroken = (docs[-1] == doc_before).astype(jnp.float32)
    carry_decay = jnp.exp(final_log) * unbroken
    half_width = mixer.shape[1] // 2
    writers = mixer[:, :half_width]
    weighted = (tail_weight[:, :, None] * writers.astype(jnp.float32)[:, None, :]).astype(
        jnp.bfloat16
    )
    span_state = contract("thn,thp->hnp", weighted, values)
    return (carry_decay, span_state)


def span_local(values, mixer, step_weight, step_bias, rate_log, skip_gain, docs):
    step_size, cumulative, row_ids, col_ids = local_setup(values, step_weight, step_bias, rate_log)
    half_width = mixer.shape[1] // 2
    writers = mixer[:, :half_width]
    readers = mixer[:, half_width:]
    affinity = jnp.dot(readers, writers.T, preferred_element_type=jnp.float32)
    same_doc = ((docs[:, None] == docs[None, :]) & (row_ids >= col_ids)).astype(jnp.float32)
    heads_first = cumulative.T
    log_gap = heads_first[:, :, None] - heads_first[:, None, :]
    mixing = (
        jnp.exp(jnp.where(same_doc[None] > 0, log_gap, 0.0))
        * same_doc[None]
        * affinity[None]
        * step_size.T[:, None, :]
    )
    mixing = mixing.astype(jnp.bfloat16)
    local_part = contract("hts,shp->thp", mixing, values)
    return values.astype(jnp.float32) * (1.0 + skip_gain)[None, :, None] + local_part


def span_carry(values, mixer, step_weight, step_bias, rate_log, docs, doc_before, incoming):
    step_size, cumulative, row_ids, col_ids = local_setup(values, step_weight, step_bias, rate_log)
    half_width = mixer.shape[1] // 2
    readers = mixer[:, half_width:]
    unbroken = (docs == doc_before).astype(jnp.float32)
    carry_scale = jnp.exp(cumulative) * unbroken[:, None]
    carried = jnp.einsum(
        "tn,hnp->thp", readers, incoming.astype(jnp.bfloat16), preferred_element_type=jnp.float32
    )
    return carry_scale[:, :, None] * carried


def scan_rounds(decay, state, axis, forward):
    size, mine = (lax.axis_size(axis), lax.axis_index(axis))
    far_decay, far_state = (decay, state)
    near_decay = jnp.ones_like(decay)
    near_state = jnp.zeros_like(state)
    distance = 1
    while distance < size:
        got_decay, got_state = shifted(
            (far_decay, far_state.astype(jnp.bfloat16)), axis, distance if forward else -distance
        )
        got_state = got_state.astype(jnp.float32)
        near_state = near_state + near_decay[:, None] * got_state
        near_decay = near_decay * got_decay
        if distance * 2 < size:
            far_state = far_state + far_decay[:, None] * got_state
            far_decay = far_decay * got_decay
        distance *= 2
    return near_state


def both_scans(decay, state, state_grad, axis, filler_fn, filler_args):
    size, mine = (lax.axis_size(axis), lax.axis_index(axis))
    if size & (size - 1):
        return (
            scan_rounds(decay, state, axis, True),
            scan_rounds(decay, state_grad, axis, False),
            filler_fn(*filler_args),
        )
    width = state.shape[1]
    total_decay = decay
    total_fwd, total_bwd = (state, state_grad)
    before = jnp.zeros_like(state)
    before_decay = jnp.ones_like(decay)
    after = jnp.zeros_like(state_grad)
    after_decay = jnp.ones_like(decay)
    distance = 1
    while distance < size:
        high = lax.convert_element_type(total_decay.astype(jnp.bfloat16), jnp.float32)
        low = total_decay - high
        pad = jnp.zeros((decay.shape[0], 126), jnp.float32)
        payload = jnp.concatenate(
            [total_fwd, total_bwd, high[:, None], low[:, None], pad], axis=1
        ).astype(jnp.bfloat16)
        upper = (mine // distance) % 2 == 1
        if distance == 1:
            payload, filler_args = lax.optimization_barrier((payload, filler_args))
        if distance * 2 < size:
            got = lax.ppermute(payload, axis, [(i, i ^ distance) for i in range(size)])
            got = got.astype(jnp.float32)
            got_fwd = got[:, :width]
            got_bwd = got[:, width : 2 * width]
        else:
            last = jnp.where(upper, total_bwd, total_fwd).astype(jnp.bfloat16)
            last = jnp.concatenate([last, payload[:, 2 * width :]], axis=1)
            got = lax.ppermute(last, axis, [(i, i ^ distance) for i in range(size)])
            got = got.astype(jnp.float32)
            got_fwd = got[:, :width]
            got_bwd = got_fwd
            got = jnp.concatenate([got[:, :width], got], axis=1)
        if distance == 1:
            got, filler = lax.optimization_barrier((got, filler_fn(*filler_args)))
        got_decay = got[:, 2 * width] + got[:, 2 * width + 1]
        before = jnp.where(upper, before + before_decay[:, None] * got_fwd, before)
        before_decay = jnp.where(upper, before_decay * got_decay, before_decay)
        after = jnp.where(upper, after, after + after_decay[:, None] * got_bwd)
        after_decay = jnp.where(upper, after_decay, after_decay * got_decay)
        if distance * 2 < size:
            total_fwd = jnp.where(
                upper,
                total_fwd + total_decay[:, None] * got_fwd,
                got_fwd + got_decay[:, None] * total_fwd,
            )
            total_bwd = jnp.where(
                upper,
                got_bwd + got_decay[:, None] * total_bwd,
                total_bwd + total_decay[:, None] * got_bwd,
            )
            total_decay = total_decay * got_decay
        distance *= 2
    return (before, after, filler)


def shards(bwd_input, bwd_docs, bwd_grad, proj_weight, step_weight, step_bias, rate_log, skip_gain):
    tokens = bwd_input.shape[1]
    channels_here = bwd_input.shape[2]
    heads_here = step_bias.shape[1]
    head_width = channels_here // heads_here
    bwd_flat = bwd_input[0]
    bwd_values = bwd_flat.reshape(tokens, heads_here, head_width)
    weight_heads = step_weight[0].reshape(heads_here, head_width)
    bias_heads = step_bias[0]
    rate_heads = rate_log[0]
    skip_heads = skip_gain[0]
    docs_bwd = bwd_docs[0]
    doc_before = shifted(docs_bwd[-1:], "seq", 1)[0]
    size, mine = (lax.axis_size("seq"), lax.axis_index("seq"))
    group = lax.axis_index("head")
    own_rows = proj_weight[0]
    slot_weight = jnp.concatenate(
        [own_rows] + [rotated(own_rows, "seq", k) for k in range(1, size)], axis=0
    )
    slot_value = jnp.dot(bwd_flat, slot_weight.T, preferred_element_type=jnp.float32)
    slot_value = slot_value.reshape(tokens, size, -1)[:, ::-1].reshape(tokens, -1)
    partial_value = roll_blocks(slot_value, mine + 1, size, 1)
    group_width = partial_value.shape[1] // 2
    mine_part = lax.dynamic_slice_in_dim(partial_value, group * group_width, group_width, axis=1)
    other_part = lax.dynamic_slice_in_dim(
        partial_value, (1 - group) * group_width, group_width, axis=1
    )
    mixer_bwd = (
        mine_part + swap_heads(other_part.astype(jnp.bfloat16)).astype(jnp.float32)
    ).astype(jnp.bfloat16)
    cotangent = bwd_grad[0].reshape(tokens, heads_here, head_width)

    def summary_bwd(values_in, mixer_in, weight_in, bias_in, rate_in):
        return span_summary(values_in, mixer_in, weight_in, bias_in, rate_in, docs_bwd, doc_before)

    summary_out, summary_pull = jax.vjp(
        summary_bwd, bwd_values, mixer_bwd, weight_heads, bias_heads, rate_heads
    )
    decay_bwd, state_bwd = summary_out
    state_shape = state_bwd.shape
    state_flat = state_bwd.reshape(heads_here, -1)

    out_ct = cotangent.astype(jnp.float32)

    def local_bwd(values_in, mixer_in, weight_in, bias_in, rate_in, skip_in):
        return span_local(values_in, mixer_in, weight_in, bias_in, rate_in, skip_in, docs_bwd)

    def local_pull(*primals):
        return jax.vjp(local_bwd, *primals[:-1])[1](primals[-1])


    def carry_bwd(values_in, mixer_in, weight_in, bias_in, rate_in, state_in):
        return span_carry(
            values_in, mixer_in, weight_in, bias_in, rate_in, docs_bwd, doc_before, state_in
        )

    def carried_only(state_in):
        return carry_bwd(bwd_values, mixer_bwd, weight_heads, bias_heads, rate_heads, state_in)

    state_grad = jax.vjp(carried_only, jnp.zeros(state_shape, jnp.float32))[1](out_ct)[0]
    state_grad = state_grad.reshape(heads_here, -1)
    incoming_flat, adjoint_flat, local_grads = both_scans(
        decay_bwd,
        state_flat,
        state_grad,
        "seq",
        local_pull,
        (bwd_values, mixer_bwd, weight_heads, bias_heads, rate_heads, skip_heads, out_ct),
    )
    incoming_bwd = incoming_flat.reshape(state_shape)
    carry_grads = jax.vjp(
        carry_bwd, bwd_values, mixer_bwd, weight_heads, bias_heads, rate_heads, incoming_bwd
    )[1](out_ct)
    out_grads = (
        (local_grads[0].astype(jnp.float32) + carry_grads[0].astype(jnp.float32)),
        (local_grads[1].astype(jnp.float32) + carry_grads[1].astype(jnp.float32)),
        local_grads[2] + carry_grads[2],
        local_grads[3] + carry_grads[3],
        local_grads[4] + carry_grads[4],
        local_grads[5],
    )
    decay_grad = jnp.sum(adjoint_flat * incoming_flat, axis=1)
    sum_grads = summary_pull((decay_grad, adjoint_flat.reshape(state_shape)))
    mixer_grad = (out_grads[1].astype(jnp.float32) + sum_grads[1].astype(jnp.float32)).astype(
        jnp.bfloat16
    )
    other_grad = swap_heads(mixer_grad)
    mixer_full = jnp.where(
        group == 0,
        jnp.concatenate([mixer_grad, other_grad], axis=1),
        jnp.concatenate([other_grad, mixer_grad], axis=1),
    )
    mixer_slots = roll_blocks(mixer_full, size - 1 - mine, size, 1)
    mixer_slots = mixer_slots.reshape(tokens, size, -1)[:, ::-1].reshape(tokens, -1)
    back_proj = jnp.dot(mixer_slots, slot_weight, preferred_element_type=jnp.float32)
    value_grad = (out_grads[0].astype(jnp.float32) + sum_grads[0].astype(jnp.float32)).reshape(
        tokens, channels_here
    ) + back_proj
    value_grad = value_grad.astype(jnp.bfloat16)
    prev_part = shifted(value_grad.reshape(1, tokens, channels_here), "section", -1)
    dest_grad = roll_blocks(mixer_full, size - mine, size, 1)
    row_parts = lax.dot_general(
        dest_grad, bwd_flat, (((0,), (0,)), ((), ())), preferred_element_type=jnp.float32
    ).reshape(size, -1, channels_here)
    small = jnp.concatenate(
        [
            (out_grads[2] + sum_grads[2]).reshape(channels_here),
            out_grads[3] + sum_grads[3],
            out_grads[4] + sum_grads[4],
            out_grads[5],
        ]
    )
    count = small.shape[0]
    block_rows = row_parts.shape[1]
    small_high = small.astype(jnp.bfloat16)
    small_low = (small - small_high.astype(jnp.float32)).astype(jnp.bfloat16)
    small_cols = -(-(2 * count) // (block_rows * 128)) * 128
    small_coded = jnp.concatenate([small_high, small_low])
    small_coded = jnp.pad(small_coded, (0, block_rows * small_cols - 2 * count))
    small_coded = small_coded.reshape(block_rows, small_cols)
    grad_rows = row_parts[0]
    small_slots = [small_coded]
    for k in range(1, size):
        message = jnp.concatenate([row_parts[k].astype(jnp.bfloat16), small_coded], axis=1)
        got = rotated(message, "seq", k)
        grad_rows = grad_rows + got[:, :channels_here].astype(jnp.float32)
        small_slots.append(got[:, channels_here:])
    small_slots = jnp.stack(small_slots[::-1])
    small_slots = roll_blocks(small_slots, mine + 1, size, 0).astype(jnp.float32)
    small_slots = small_slots.reshape(size, -1)
    small_parts = small_slots[:, :count] + small_slots[:, count : 2 * count]
    small_total = small_parts[0]
    for j in range(1, size):
        small_total = small_total + small_parts[j]
    small = small_total.reshape(-1)
    totals = (
        small[:channels_here],
        small[channels_here : channels_here + heads_here],
        small[channels_here + heads_here : channels_here + 2 * heads_here],
        small[channels_here + 2 * heads_here : channels_here + 3 * heads_here],
    )
    return (
        prev_part,
        grad_rows[None],
        totals[0][None],
        totals[1][None],
        totals[2][None],
        totals[3][None],
    )


def solution(mesh):
    in_specs = (
        P("section", "seq", "head"),
        P("section", "seq"),
        P("section", "seq", "head"),
        P("section", "seq", "head"),
        P("section", "head"),
        P("section", "head"),
        P("section", "head"),
        P("section", "head"),
    )
    out_specs = (
        P("section", "seq", "head"),
        P("section", "seq", "head"),
        P("section", "head"),
        P("section", "head"),
        P("section", "head"),
        P("section", "head"),
    )
    return jax.shard_map(shards, mesh=mesh, in_specs=in_specs, out_specs=out_specs, check_vma=False)
```

```python
import jax
import jax.numpy as jnp
from jax import lax
from jax.sharding import PartitionSpec as P

EXACT = lax.Precision.HIGHEST


def shifted(block, axis, distance):
    devices = range(lax.axis_size(axis))
    route = [(i - distance, i) for i in devices if i - distance in devices]
    return lax.ppermute(block, axis, route)


def rotated(block, axis, distance):
    size = lax.axis_size(axis)
    route = [(i, (i + distance) % size) for i in range(size)]
    return lax.ppermute(block, axis, route)


def roll_blocks(value, shift, parts, dim):
    doubled = jnp.concatenate([value, value], axis=dim)
    width = value.shape[dim] // parts
    start = ((parts - shift) % parts) * width
    return lax.dynamic_slice_in_dim(doubled, start, value.shape[dim], axis=dim)


def swap_heads(block):
    return lax.ppermute(block, "head", [(0, 1), (1, 0)])


def contract(spec, left, right):
    return jnp.einsum(spec, left, right, preferred_element_type=jnp.float32)


def local_setup(values, step_weight, step_bias, rate_log):
    tokens = values.shape[0]
    raw_step = (
        jnp.einsum("thp,hp->th", values.astype(jnp.float32), step_weight, precision=EXACT)
        + step_bias[None, :]
    )
    step_size = jax.nn.softplus(raw_step)
    decay_log = -jnp.exp(rate_log)[None, :] * step_size
    row_ids = lax.broadcasted_iota(jnp.int32, (tokens, tokens), 0)
    col_ids = lax.broadcasted_iota(jnp.int32, (tokens, tokens), 1)
    triangle = (row_ids >= col_ids).astype(jnp.float32)
    cumulative = jnp.dot(triangle, decay_log, precision=EXACT)
    return (step_size, cumulative, row_ids, col_ids)


def span_summary(values, mixer, step_weight, step_bias, rate_log, docs, doc_before):
    step_size, cumulative, row_ids, col_ids = local_setup(values, step_weight, step_bias, rate_log)
    final_log = cumulative[-1]
    tail_mask = (docs == docs[-1]).astype(jnp.float32)[:, None]
    tail_weight = (
        jnp.exp(jnp.where(tail_mask > 0, final_log[None, :] - cumulative, 0.0))
        * tail_mask
        * step_size
    )
    unbroken = (docs[-1] == doc_before).astype(jnp.float32)
    carry_decay = jnp.exp(final_log) * unbroken
    half_width = mixer.shape[1] // 2
    writers = mixer[:, :half_width]
    weighted = (tail_weight[:, :, None] * writers.astype(jnp.float32)[:, None, :]).astype(
        jnp.bfloat16
    )
    span_state = contract("thn,thp->hnp", weighted, values)
    return (carry_decay, span_state)


def span_local(values, mixer, step_weight, step_bias, rate_log, skip_gain, docs):
    step_size, cumulative, row_ids, col_ids = local_setup(values, step_weight, step_bias, rate_log)
    half_width = mixer.shape[1] // 2
    writers = mixer[:, :half_width]
    readers = mixer[:, half_width:]
    affinity = jnp.dot(readers, writers.T, preferred_element_type=jnp.float32)
    same_doc = ((docs[:, None] == docs[None, :]) & (row_ids >= col_ids)).astype(jnp.float32)
    heads_first = cumulative.T
    log_gap = heads_first[:, :, None] - heads_first[:, None, :]
    mixing = (
        jnp.exp(jnp.where(same_doc[None] > 0, log_gap, 0.0))
        * same_doc[None]
        * affinity[None]
        * step_size.T[:, None, :]
    )
    mixing = mixing.astype(jnp.bfloat16)
    local_part = contract("hts,shp->thp", mixing, values)
    return values.astype(jnp.float32) * (1.0 + skip_gain)[None, :, None] + local_part


def span_carry(values, mixer, step_weight, step_bias, rate_log, docs, doc_before, incoming):
    step_size, cumulative, row_ids, col_ids = local_setup(values, step_weight, step_bias, rate_log)
    half_width = mixer.shape[1] // 2
    readers = mixer[:, half_width:]
    unbroken = (docs == doc_before).astype(jnp.float32)
    carry_scale = jnp.exp(cumulative) * unbroken[:, None]
    carried = jnp.einsum("tn,hnp->thp", readers.astype(jnp.float32), incoming, precision=EXACT)
    return carry_scale[:, :, None] * carried


def scan_rounds(decay, state, axis, forward):
    size, mine = (lax.axis_size(axis), lax.axis_index(axis))
    far_decay, far_state = (decay, state)
    near_decay = jnp.ones_like(decay)
    near_state = jnp.zeros_like(state)
    distance = 1
    while distance < size:
        got_decay, got_state = shifted(
            (far_decay, far_state.astype(jnp.bfloat16)), axis, distance if forward else -distance
        )
        got_state = got_state.astype(jnp.float32)
        near_state = near_state + near_decay[:, None] * got_state
        near_decay = near_decay * got_decay
        if distance * 2 < size:
            far_state = far_state + far_decay[:, None] * got_state
            far_decay = far_decay * got_decay
        distance *= 2
    return near_state


def both_scans(decay, state, state_grad, axis, filler_fn, filler_args):
    size, mine = (lax.axis_size(axis), lax.axis_index(axis))
    if size & (size - 1):
        return (
            scan_rounds(decay, state, axis, True),
            scan_rounds(decay, state_grad, axis, False),
            filler_fn(*filler_args),
        )
    width = state.shape[1]
    total_decay = decay
    total_fwd, total_bwd = (state, state_grad)
    before = jnp.zeros_like(state)
    before_decay = jnp.ones_like(decay)
    after = jnp.zeros_like(state_grad)
    after_decay = jnp.ones_like(decay)
    distance = 1
    while distance < size:
        high = lax.convert_element_type(total_decay.astype(jnp.bfloat16), jnp.float32)
        low = total_decay - high
        pad = jnp.zeros((decay.shape[0], 126), jnp.float32)
        payload = jnp.concatenate(
            [total_fwd, total_bwd, high[:, None], low[:, None], pad], axis=1
        ).astype(jnp.bfloat16)
        upper = (mine // distance) % 2 == 1
        if distance * 2 < size:
            got = lax.ppermute(payload, axis, [(i, i ^ distance) for i in range(size)])
            got = got.astype(jnp.float32)
            got_fwd = got[:, :width]
            got_bwd = got[:, width : 2 * width]
        else:
            last = jnp.where(upper, total_bwd, total_fwd).astype(jnp.bfloat16)
            last = jnp.concatenate([last, payload[:, 2 * width :]], axis=1)
            got = lax.ppermute(last, axis, [(i, i ^ distance) for i in range(size)])
            got = got.astype(jnp.float32)
            got_fwd = got[:, :width]
            got_bwd = got_fwd
            got = jnp.concatenate([got[:, :width], got], axis=1)
        if distance == 1:
            got, filler_args = lax.optimization_barrier((got, filler_args))
        if distance * 2 >= size:
            got, filler = lax.optimization_barrier((got, filler_fn(*filler_args)))
        got_decay = got[:, 2 * width] + got[:, 2 * width + 1]
        before = jnp.where(upper, before + before_decay[:, None] * got_fwd, before)
        before_decay = jnp.where(upper, before_decay * got_decay, before_decay)
        after = jnp.where(upper, after, after + after_decay[:, None] * got_bwd)
        after_decay = jnp.where(upper, after_decay, after_decay * got_decay)
        if distance * 2 < size:
            total_fwd = jnp.where(
                upper,
                total_fwd + total_decay[:, None] * got_fwd,
                got_fwd + got_decay[:, None] * total_fwd,
            )
            total_bwd = jnp.where(
                upper,
                got_bwd + got_decay[:, None] * total_bwd,
                total_bwd + total_decay[:, None] * got_bwd,
            )
            total_decay = total_decay * got_decay
        distance *= 2
    return (before, after, filler)


def shards(bwd_input, bwd_docs, bwd_grad, proj_weight, step_weight, step_bias, rate_log, skip_gain):
    tokens = bwd_input.shape[1]
    channels_here = bwd_input.shape[2]
    heads_here = step_bias.shape[1]
    head_width = channels_here // heads_here
    bwd_flat = bwd_input[0]
    bwd_values = bwd_flat.reshape(tokens, heads_here, head_width)
    weight_heads = step_weight[0].reshape(heads_here, head_width)
    bias_heads = step_bias[0]
    rate_heads = rate_log[0]
    skip_heads = skip_gain[0]
    docs_bwd = bwd_docs[0]
    doc_before = shifted(docs_bwd[-1:], "seq", 1)[0]
    size, mine = (lax.axis_size("seq"), lax.axis_index("seq"))
    group = lax.axis_index("head")
    own_rows = proj_weight[0]
    slot_weight = jnp.concatenate(
        [own_rows] + [rotated(own_rows, "seq", k) for k in range(1, size)], axis=0
    )
    slot_value = jnp.dot(bwd_flat, slot_weight.T, preferred_element_type=jnp.float32)
    slot_value = slot_value.reshape(tokens, size, -1)[:, ::-1].reshape(tokens, -1)
    partial_value = roll_blocks(slot_value, mine + 1, size, 1)
    group_width = partial_value.shape[1] // 2
    mine_part = lax.dynamic_slice_in_dim(partial_value, group * group_width, group_width, axis=1)
    other_part = lax.dynamic_slice_in_dim(
        partial_value, (1 - group) * group_width, group_width, axis=1
    )
    mixer_bwd = (
        mine_part + swap_heads(other_part.astype(jnp.bfloat16)).astype(jnp.float32)
    ).astype(jnp.bfloat16)
    cotangent = bwd_grad[0].reshape(tokens, heads_here, head_width)

    def summary_bwd(values_in, mixer_in, weight_in, bias_in, rate_in):
        return span_summary(values_in, mixer_in, weight_in, bias_in, rate_in, docs_bwd, doc_before)

    summary_out, summary_pull = jax.vjp(
        summary_bwd, bwd_values, mixer_bwd, weight_heads, bias_heads, rate_heads
    )
    decay_bwd, state_bwd = summary_out
    state_shape = state_bwd.shape
    state_flat = state_bwd.reshape(heads_here, -1)

    out_ct = cotangent.astype(jnp.float32)

    def local_bwd(values_in, mixer_in, weight_in, bias_in, rate_in, skip_in):
        return span_local(values_in, mixer_in, weight_in, bias_in, rate_in, skip_in, docs_bwd)

    def local_pull(*primals):
        return jax.vjp(local_bwd, *primals[:-1])[1](primals[-1])


    def carry_bwd(values_in, mixer_in, weight_in, bias_in, rate_in, state_in):
        return span_carry(
            values_in, mixer_in, weight_in, bias_in, rate_in, docs_bwd, doc_before, state_in
        )

    def carried_only(state_in):
        return carry_bwd(bwd_values, mixer_bwd, weight_heads, bias_heads, rate_heads, state_in)

    state_grad = jax.vjp(carried_only, jnp.zeros(state_shape, jnp.float32))[1](out_ct)[0]
    state_grad = state_grad.reshape(heads_here, -1)
    incoming_flat, adjoint_flat, local_grads = both_scans(
        decay_bwd,
        state_flat,
        state_grad,
        "seq",
        local_pull,
        (bwd_values, mixer_bwd, weight_heads, bias_heads, rate_heads, skip_heads, out_ct),
    )
    incoming_bwd = incoming_flat.reshape(state_shape)
    carry_grads = jax.vjp(
        carry_bwd, bwd_values, mixer_bwd, weight_heads, bias_heads, rate_heads, incoming_bwd
    )[1](out_ct)
    out_grads = (
        (local_grads[0].astype(jnp.float32) + carry_grads[0].astype(jnp.float32)),
        (local_grads[1].astype(jnp.float32) + carry_grads[1].astype(jnp.float32)),
        local_grads[2] + carry_grads[2],
        local_grads[3] + carry_grads[3],
        local_grads[4] + carry_grads[4],
        local_grads[5],
    )
    decay_grad = jnp.sum(adjoint_flat * incoming_flat, axis=1)
    sum_grads = summary_pull((decay_grad, adjoint_flat.reshape(state_shape)))
    mixer_grad = (out_grads[1].astype(jnp.float32) + sum_grads[1].astype(jnp.float32)).astype(
        jnp.bfloat16
    )
    other_grad = swap_heads(mixer_grad)
    mixer_full = jnp.where(
        group == 0,
        jnp.concatenate([mixer_grad, other_grad], axis=1),
        jnp.concatenate([other_grad, mixer_grad], axis=1),
    )
    mixer_slots = roll_blocks(mixer_full, size - 1 - mine, size, 1)
    mixer_slots = mixer_slots.reshape(tokens, size, -1)[:, ::-1].reshape(tokens, -1)
    back_proj = jnp.dot(mixer_slots, slot_weight, preferred_element_type=jnp.float32)
    value_grad = (out_grads[0].astype(jnp.float32) + sum_grads[0].astype(jnp.float32)).reshape(
        tokens, channels_here
    ) + back_proj
    value_grad = value_grad.astype(jnp.bfloat16)
    prev_part = shifted(value_grad.reshape(1, tokens, channels_here), "section", -1)
    dest_grad = roll_blocks(mixer_full, size - mine, size, 1)
    row_parts = lax.dot_general(
        dest_grad, bwd_flat, (((0,), (0,)), ((), ())), preferred_element_type=jnp.float32
    ).reshape(size, -1, channels_here)
    small = jnp.concatenate(
        [
            (out_grads[2] + sum_grads[2]).reshape(channels_here),
            out_grads[3] + sum_grads[3],
            out_grads[4] + sum_grads[4],
            out_grads[5],
        ]
    )
    count = small.shape[0]
    block_rows = row_parts.shape[1]
    small_high = small.astype(jnp.bfloat16)
    small_low = (small - small_high.astype(jnp.float32)).astype(jnp.bfloat16)
    small_cols = -(-(2 * count) // (block_rows * 128)) * 128
    small_coded = jnp.concatenate([small_high, small_low])
    small_coded = jnp.pad(small_coded, (0, block_rows * small_cols - 2 * count))
    small_coded = small_coded.reshape(block_rows, small_cols)
    grad_rows = row_parts[0]
    small_slots = [small_coded]
    for k in range(1, size):
        message = jnp.concatenate([row_parts[k].astype(jnp.bfloat16), small_coded], axis=1)
        got = rotated(message, "seq", k)
        grad_rows = grad_rows + got[:, :channels_here].astype(jnp.float32)
        small_slots.append(got[:, channels_here:])
    small_slots = jnp.stack(small_slots[::-1])
    small_slots = roll_blocks(small_slots, mine + 1, size, 0).astype(jnp.float32)
    small_slots = small_slots.reshape(size, -1)
    small_parts = small_slots[:, :count] + small_slots[:, count : 2 * count]
    small_total = small_parts[0]
    for j in range(1, size):
        small_total = small_total + small_parts[j]
    small = small_total.reshape(-1)
    totals = (
        small[:channels_here],
        small[channels_here : channels_here + heads_here],
        small[channels_here + heads_here : channels_here + 2 * heads_here],
        small[channels_here + 2 * heads_here : channels_here + 3 * heads_here],
    )
    return (
        prev_part,
        grad_rows[None],
        totals[0][None],
        totals[1][None],
        totals[2][None],
        totals[3][None],
    )


def solution(mesh):
    in_specs = (
        P("section", "seq", "head"),
        P("section", "seq"),
        P("section", "seq", "head"),
        P("section", "seq", "head"),
        P("section", "head"),
        P("section", "head"),
        P("section", "head"),
        P("section", "head"),
    )
    out_specs = (
        P("section", "seq", "head"),
        P("section", "seq", "head"),
        P("section", "head"),
        P("section", "head"),
        P("section", "head"),
        P("section", "head"),
    )
    return jax.shard_map(shards, mesh=mesh, in_specs=in_specs, out_specs=out_specs, check_vma=False)
```

```python
import jax
import jax.numpy as jnp
from jax import lax
from jax.sharding import PartitionSpec as P

EXACT = lax.Precision.HIGHEST


def shifted(block, axis, distance):
    devices = range(lax.axis_size(axis))
    route = [(i - distance, i) for i in devices if i - distance in devices]
    return lax.ppermute(block, axis, route)


def rotated(block, axis, distance):
    size = lax.axis_size(axis)
    route = [(i, (i + distance) % size) for i in range(size)]
    return lax.ppermute(block, axis, route)


def roll_blocks(value, shift, parts, dim):
    doubled = jnp.concatenate([value, value], axis=dim)
    width = value.shape[dim] // parts
    start = ((parts - shift) % parts) * width
    return lax.dynamic_slice_in_dim(doubled, start, value.shape[dim], axis=dim)


def swap_heads(block):
    return lax.ppermute(block, "head", [(0, 1), (1, 0)])


def contract(spec, left, right):
    return jnp.einsum(spec, left, right, preferred_element_type=jnp.float32)


def local_setup(values, step_weight, step_bias, rate_log):
    tokens = values.shape[0]
    raw_step = (
        jnp.einsum("thp,hp->th", values.astype(jnp.float32), step_weight, precision=EXACT)
        + step_bias[None, :]
    )
    step_size = jax.nn.softplus(raw_step)
    decay_log = -jnp.exp(rate_log)[None, :] * step_size
    row_ids = lax.broadcasted_iota(jnp.int32, (tokens, tokens), 0)
    col_ids = lax.broadcasted_iota(jnp.int32, (tokens, tokens), 1)
    triangle = (row_ids >= col_ids).astype(jnp.float32)
    cumulative = jnp.dot(triangle, decay_log, precision=EXACT)
    return (step_size, cumulative, row_ids, col_ids)


def span_summary(values, mixer, step_weight, step_bias, rate_log, docs, doc_before):
    step_size, cumulative, row_ids, col_ids = local_setup(values, step_weight, step_bias, rate_log)
    final_log = cumulative[-1]
    tail_mask = (docs == docs[-1]).astype(jnp.float32)[:, None]
    tail_weight = (
        jnp.exp(jnp.where(tail_mask > 0, final_log[None, :] - cumulative, 0.0))
        * tail_mask
        * step_size
    )
    unbroken = (docs[-1] == doc_before).astype(jnp.float32)
    carry_decay = jnp.exp(final_log) * unbroken
    half_width = mixer.shape[1] // 2
    writers = mixer[:, :half_width]
    weighted = (tail_weight[:, :, None] * writers.astype(jnp.float32)[:, None, :]).astype(
        jnp.bfloat16
    )
    span_state = contract("thn,thp->hnp", weighted, values)
    return (carry_decay, span_state)


def span_local(values, mixer, step_weight, step_bias, rate_log, skip_gain, docs):
    step_size, cumulative, row_ids, col_ids = local_setup(values, step_weight, step_bias, rate_log)
    half_width = mixer.shape[1] // 2
    writers = mixer[:, :half_width]
    readers = mixer[:, half_width:]
    affinity = jnp.dot(readers, writers.T, preferred_element_type=jnp.float32)
    same_doc = ((docs[:, None] == docs[None, :]) & (row_ids >= col_ids)).astype(jnp.float32)
    heads_first = cumulative.T
    log_gap = heads_first[:, :, None] - heads_first[:, None, :]
    mixing = (
        jnp.exp(jnp.where(same_doc[None] > 0, log_gap, 0.0))
        * same_doc[None]
        * affinity[None]
        * step_size.T[:, None, :]
    )
    mixing = mixing.astype(jnp.bfloat16)
    local_part = contract("hts,shp->thp", mixing, values)
    return values.astype(jnp.float32) * (1.0 + skip_gain)[None, :, None] + local_part


def span_carry(values, mixer, step_weight, step_bias, rate_log, docs, doc_before, incoming):
    step_size, cumulative, row_ids, col_ids = local_setup(values, step_weight, step_bias, rate_log)
    half_width = mixer.shape[1] // 2
    readers = mixer[:, half_width:]
    unbroken = (docs == doc_before).astype(jnp.float32)
    carry_scale = jnp.exp(cumulative) * unbroken[:, None]
    carried = jnp.einsum("tn,hnp->thp", readers.astype(jnp.float32), incoming, precision=EXACT)
    return carry_scale[:, :, None] * carried


def scan_rounds(decay, state, axis, forward):
    size, mine = (lax.axis_size(axis), lax.axis_index(axis))
    far_decay, far_state = (decay, state)
    near_decay = jnp.ones_like(decay)
    near_state = jnp.zeros_like(state)
    distance = 1
    while distance < size:
        got_decay, got_state = shifted(
            (far_decay, far_state.astype(jnp.bfloat16)), axis, distance if forward else -distance
        )
        got_state = got_state.astype(jnp.float32)
        near_state = near_state + near_decay[:, None] * got_state
        near_decay = near_decay * got_decay
        if distance * 2 < size:
            far_state = far_state + far_decay[:, None] * got_state
            far_decay = far_decay * got_decay
        distance *= 2
    return near_state


def both_scans(decay, state, state_grad, axis, filler_fn, filler_args):
    size, mine = (lax.axis_size(axis), lax.axis_index(axis))
    if size & (size - 1):
        return (
            scan_rounds(decay, state, axis, True),
            scan_rounds(decay, state_grad, axis, False),
            filler_fn(*filler_args),
        )
    width = state.shape[1]
    total_decay = decay
    total_fwd, total_bwd = (state, state_grad)
    before = jnp.zeros_like(state)
    before_decay = jnp.ones_like(decay)
    after = jnp.zeros_like(state_grad)
    after_decay = jnp.ones_like(decay)
    distance = 1
    while distance < size:
        high = lax.convert_element_type(total_decay.astype(jnp.bfloat16), jnp.float32)
        low = total_decay - high
        pad = jnp.zeros((decay.shape[0], 126), jnp.float32)
        payload = jnp.concatenate(
            [total_fwd, total_bwd, high[:, None], low[:, None], pad], axis=1
        ).astype(jnp.bfloat16)
        upper = (mine // distance) % 2 == 1
        if distance == 1:
            payload, filler_args = lax.optimization_barrier((payload, filler_args))
        if distance * 2 < size:
            got = lax.ppermute(payload, axis, [(i, i ^ distance) for i in range(size)])
            got = got.astype(jnp.float32)
            got_fwd = got[:, :width]
            got_bwd = got[:, width : 2 * width]
        else:
            last = jnp.where(upper, total_bwd, total_fwd).astype(jnp.bfloat16)
            last = jnp.concatenate([last, payload[:, 2 * width :]], axis=1)
            got = lax.ppermute(last, axis, [(i, i ^ distance) for i in range(size)])
            got = got.astype(jnp.float32)
            got_fwd = got[:, :width]
            got_bwd = got_fwd
            got = jnp.concatenate([got[:, :width], got], axis=1)
        if distance == 1:
            got, filler = lax.optimization_barrier((got, filler_fn(*filler_args)))
        got_decay = got[:, 2 * width] + got[:, 2 * width + 1]
        before = jnp.where(upper, before + before_decay[:, None] * got_fwd, before)
        before_decay = jnp.where(upper, before_decay * got_decay, before_decay)
        after = jnp.where(upper, after, after + after_decay[:, None] * got_bwd)
        after_decay = jnp.where(upper, after_decay, after_decay * got_decay)
        if distance * 2 < size:
            total_fwd = jnp.where(
                upper,
                total_fwd + total_decay[:, None] * got_fwd,
                got_fwd + got_decay[:, None] * total_fwd,
            )
            total_bwd = jnp.where(
                upper,
                got_bwd + got_decay[:, None] * total_bwd,
                total_bwd + total_decay[:, None] * got_bwd,
            )
            total_decay = total_decay * got_decay
        distance *= 2
    return (before, after, filler)


def shards(bwd_input, bwd_docs, bwd_grad, proj_weight, step_weight, step_bias, rate_log, skip_gain):
    tokens = bwd_input.shape[1]
    channels_here = bwd_input.shape[2]
    heads_here = step_bias.shape[1]
    head_width = channels_here // heads_here
    bwd_flat = bwd_input[0]
    bwd_values = bwd_flat.reshape(tokens, heads_here, head_width)
    weight_heads = step_weight[0].reshape(heads_here, head_width)
    bias_heads = step_bias[0]
    rate_heads = rate_log[0]
    skip_heads = skip_gain[0]
    docs_bwd = bwd_docs[0]
    doc_before = shifted(docs_bwd[-1:], "seq", 1)[0]
    size, mine = (lax.axis_size("seq"), lax.axis_index("seq"))
    group = lax.axis_index("head")
    own_rows = proj_weight[0]
    slot_weight = jnp.concatenate(
        [own_rows] + [rotated(own_rows, "seq", k) for k in range(1, size)], axis=0
    )
    slot_value = jnp.dot(bwd_flat, slot_weight.T, preferred_element_type=jnp.float32)
    slot_value = slot_value.reshape(tokens, size, -1)[:, ::-1].reshape(tokens, -1)
    partial_value = roll_blocks(slot_value, mine + 1, size, 1)
    group_width = partial_value.shape[1] // 2
    mine_part = lax.dynamic_slice_in_dim(partial_value, group * group_width, group_width, axis=1)
    other_part = lax.dynamic_slice_in_dim(
        partial_value, (1 - group) * group_width, group_width, axis=1
    )
    mixer_bwd = (
        mine_part + swap_heads(other_part.astype(jnp.bfloat16)).astype(jnp.float32)
    ).astype(jnp.bfloat16)
    cotangent = bwd_grad[0].reshape(tokens, heads_here, head_width)

    def summary_bwd(values_in, mixer_in, weight_in, bias_in, rate_in):
        return span_summary(values_in, mixer_in, weight_in, bias_in, rate_in, docs_bwd, doc_before)

    summary_out, summary_pull = jax.vjp(
        summary_bwd, bwd_values, mixer_bwd, weight_heads, bias_heads, rate_heads
    )
    decay_bwd, state_bwd = summary_out
    state_shape = state_bwd.shape
    state_flat = state_bwd.reshape(heads_here, -1)

    out_ct = cotangent.astype(jnp.float32)

    def local_bwd(values_in, mixer_in, weight_in, bias_in, rate_in, skip_in):
        return span_local(values_in, mixer_in, weight_in, bias_in, rate_in, skip_in, docs_bwd)

    def local_pull(*primals):
        return jax.vjp(local_bwd, *primals[:-1])[1](primals[-1])


    def carry_bwd(values_in, mixer_in, weight_in, bias_in, rate_in, state_in):
        return span_carry(
            values_in, mixer_in, weight_in, bias_in, rate_in, docs_bwd, doc_before, state_in
        )

    def carried_only(state_in):
        return carry_bwd(bwd_values, mixer_bwd, weight_heads, bias_heads, rate_heads, state_in)

    state_grad = jax.vjp(carried_only, jnp.zeros(state_shape, jnp.float32))[1](out_ct)[0]
    state_grad = state_grad.reshape(heads_here, -1)
    incoming_flat, adjoint_flat, local_grads = both_scans(
        decay_bwd,
        state_flat,
        state_grad,
        "seq",
        local_pull,
        (bwd_values, mixer_bwd, weight_heads, bias_heads, rate_heads, skip_heads, out_ct),
    )
    incoming_bwd = incoming_flat.reshape(state_shape)
    carry_grads = jax.vjp(
        carry_bwd, bwd_values, mixer_bwd, weight_heads, bias_heads, rate_heads, incoming_bwd
    )[1](out_ct)
    out_grads = (
        (local_grads[0].astype(jnp.float32) + carry_grads[0].astype(jnp.float32)),
        (local_grads[1].astype(jnp.float32) + carry_grads[1].astype(jnp.float32)),
        local_grads[2] + carry_grads[2],
        local_grads[3] + carry_grads[3],
        local_grads[4] + carry_grads[4],
        local_grads[5],
    )
    decay_grad = jnp.sum(adjoint_flat * incoming_flat, axis=1)
    sum_grads = summary_pull((decay_grad, adjoint_flat.reshape(state_shape)))
    mixer_grad = (out_grads[1].astype(jnp.float32) + sum_grads[1].astype(jnp.float32)).astype(
        jnp.bfloat16
    )
    other_grad = swap_heads(mixer_grad)
    mixer_full = jnp.where(
        group == 0,
        jnp.concatenate([mixer_grad, other_grad], axis=1),
        jnp.concatenate([other_grad, mixer_grad], axis=1),
    )
    mixer_slots = roll_blocks(mixer_full, size - 1 - mine, size, 1)
    mixer_slots = mixer_slots.reshape(tokens, size, -1)[:, ::-1].reshape(tokens, -1)
    back_proj = jnp.dot(mixer_slots, slot_weight, preferred_element_type=jnp.float32)
    value_grad = (out_grads[0].astype(jnp.float32) + sum_grads[0].astype(jnp.float32)).reshape(
        tokens, channels_here
    ) + back_proj
    value_grad = value_grad.astype(jnp.bfloat16)
    prev_part = shifted(value_grad.reshape(1, tokens, channels_here), "section", -1)
    dest_grad = roll_blocks(mixer_full, size - mine, size, 1)
    row_parts = lax.dot_general(
        dest_grad, bwd_flat, (((0,), (0,)), ((), ())), preferred_element_type=jnp.float32
    ).reshape(size, -1, channels_here)
    small = jnp.concatenate(
        [
            (out_grads[2] + sum_grads[2]).reshape(channels_here),
            out_grads[3] + sum_grads[3],
            out_grads[4] + sum_grads[4],
            out_grads[5],
        ]
    )
    count = small.shape[0]
    block_rows = row_parts.shape[1]
    small_high = small.astype(jnp.bfloat16)
    small_low = (small - small_high.astype(jnp.float32)).astype(jnp.bfloat16)
    small_cols = -(-(2 * count) // (block_rows * 128)) * 128
    small_coded = jnp.concatenate([small_high, small_low])
    small_coded = jnp.pad(small_coded, (0, block_rows * small_cols - 2 * count))
    small_coded = small_coded.reshape(block_rows, small_cols)
    grad_rows = row_parts[0]
    small_slots = [small_coded]
    for k in range(size - 1, 0, -1):
        message = jnp.concatenate([row_parts[k].astype(jnp.bfloat16), small_coded], axis=1)
        got = rotated(message, "seq", k)
        grad_rows = grad_rows + got[:, :channels_here].astype(jnp.float32)
        small_slots.append(got[:, channels_here:])
    small_slots = jnp.stack([small_slots[0]] + small_slots[1:][::-1])[::-1]
    small_slots = roll_blocks(small_slots, mine + 1, size, 0).astype(jnp.float32)
    small_slots = small_slots.reshape(size, -1)
    small_parts = small_slots[:, :count] + small_slots[:, count : 2 * count]
    small_total = small_parts[0]
    for j in range(1, size):
        small_total = small_total + small_parts[j]
    small = small_total.reshape(-1)
    totals = (
        small[:channels_here],
        small[channels_here : channels_here + heads_here],
        small[channels_here + heads_here : channels_here + 2 * heads_here],
        small[channels_here + 2 * heads_here : channels_here + 3 * heads_here],
    )
    return (
        prev_part,
        grad_rows[None],
        totals[0][None],
        totals[1][None],
        totals[2][None],
        totals[3][None],
    )


def solution(mesh):
    in_specs = (
        P("section", "seq", "head"),
        P("section", "seq"),
        P("section", "seq", "head"),
        P("section", "seq", "head"),
        P("section", "head"),
        P("section", "head"),
        P("section", "head"),
        P("section", "head"),
    )
    out_specs = (
        P("section", "seq", "head"),
        P("section", "seq", "head"),
        P("section", "head"),
        P("section", "head"),
        P("section", "head"),
        P("section", "head"),
    )
    return jax.shard_map(shards, mesh=mesh, in_specs=in_specs, out_specs=out_specs, check_vma=False)
```

```python
import jax
import jax.numpy as jnp
from jax import lax
from jax.sharding import PartitionSpec as P

EXACT = lax.Precision.HIGHEST


def shifted(block, axis, distance):
    devices = range(lax.axis_size(axis))
    route = [(i - distance, i) for i in devices if i - distance in devices]
    return lax.ppermute(block, axis, route)


def rotated(block, axis, distance):
    size = lax.axis_size(axis)
    route = [(i, (i + distance) % size) for i in range(size)]
    return lax.ppermute(block, axis, route)


def roll_blocks(value, shift, parts, dim):
    doubled = jnp.concatenate([value, value], axis=dim)
    width = value.shape[dim] // parts
    start = ((parts - shift) % parts) * width
    return lax.dynamic_slice_in_dim(doubled, start, value.shape[dim], axis=dim)


def swap_heads(block):
    return lax.ppermute(block, "head", [(0, 1), (1, 0)])


def contract(spec, left, right):
    return jnp.einsum(spec, left, right, preferred_element_type=jnp.float32)


def local_setup(values, step_weight, step_bias, rate_log):
    tokens = values.shape[0]
    raw_step = (
        jnp.einsum("thp,hp->th", values.astype(jnp.float32), step_weight, precision=EXACT)
        + step_bias[None, :]
    )
    step_size = jax.nn.softplus(raw_step)
    decay_log = -jnp.exp(rate_log)[None, :] * step_size
    row_ids = lax.broadcasted_iota(jnp.int32, (tokens, tokens), 0)
    col_ids = lax.broadcasted_iota(jnp.int32, (tokens, tokens), 1)
    triangle = (row_ids >= col_ids).astype(jnp.float32)
    cumulative = jnp.dot(triangle, decay_log, precision=EXACT)
    return (step_size, cumulative, row_ids, col_ids)


def span_summary(values, mixer, step_weight, step_bias, rate_log, docs, doc_before):
    step_size, cumulative, row_ids, col_ids = local_setup(values, step_weight, step_bias, rate_log)
    final_log = cumulative[-1]
    tail_mask = (docs == docs[-1]).astype(jnp.float32)[:, None]
    tail_weight = (
        jnp.exp(jnp.where(tail_mask > 0, final_log[None, :] - cumulative, 0.0))
        * tail_mask
        * step_size
    )
    unbroken = (docs[-1] == doc_before).astype(jnp.float32)
    carry_decay = jnp.exp(final_log) * unbroken
    half_width = mixer.shape[1] // 2
    writers = mixer[:, :half_width]
    weighted = (tail_weight[:, :, None] * writers.astype(jnp.float32)[:, None, :]).astype(
        jnp.bfloat16
    )
    span_state = contract("thn,thp->hnp", weighted, values)
    return (carry_decay, span_state)


def span_local(values, mixer, step_weight, step_bias, rate_log, skip_gain, docs):
    step_size, cumulative, row_ids, col_ids = local_setup(values, step_weight, step_bias, rate_log)
    half_width = mixer.shape[1] // 2
    writers = mixer[:, :half_width]
    readers = mixer[:, half_width:]
    affinity = jnp.dot(readers, writers.T, preferred_element_type=jnp.float32)
    same_doc = ((docs[:, None] == docs[None, :]) & (row_ids >= col_ids)).astype(jnp.float32)
    heads_first = cumulative.T
    log_gap = heads_first[:, :, None] - heads_first[:, None, :]
    mixing = (
        jnp.exp(jnp.where(same_doc[None] > 0, log_gap, 0.0))
        * same_doc[None]
        * affinity[None]
        * step_size.T[:, None, :]
    )
    mixing = mixing.astype(jnp.bfloat16)
    local_part = contract("hts,shp->thp", mixing, values)
    return values.astype(jnp.float32) * (1.0 + skip_gain)[None, :, None] + local_part


def span_carry(values, mixer, step_weight, step_bias, rate_log, docs, doc_before, incoming):
    step_size, cumulative, row_ids, col_ids = local_setup(values, step_weight, step_bias, rate_log)
    half_width = mixer.shape[1] // 2
    readers = mixer[:, half_width:]
    unbroken = (docs == doc_before).astype(jnp.float32)
    carry_scale = jnp.exp(cumulative) * unbroken[:, None]
    carried = jnp.einsum("tn,hnp->thp", readers.astype(jnp.float32), incoming, precision=EXACT)
    return carry_scale[:, :, None] * carried


def scan_rounds(decay, state, axis, forward):
    size, mine = (lax.axis_size(axis), lax.axis_index(axis))
    far_decay, far_state = (decay, state)
    near_decay = jnp.ones_like(decay)
    near_state = jnp.zeros_like(state)
    distance = 1
    while distance < size:
        got_decay, got_state = shifted(
            (far_decay, far_state.astype(jnp.bfloat16)), axis, distance if forward else -distance
        )
        got_state = got_state.astype(jnp.float32)
        near_state = near_state + near_decay[:, None] * got_state
        near_decay = near_decay * got_decay
        if distance * 2 < size:
            far_state = far_state + far_decay[:, None] * got_state
            far_decay = far_decay * got_decay
        distance *= 2
    return near_state


def both_scans(decay, state, state_grad, axis, filler_fn, filler_args):
    size, mine = (lax.axis_size(axis), lax.axis_index(axis))
    if size & (size - 1):
        return (
            scan_rounds(decay, state, axis, True),
            scan_rounds(decay, state_grad, axis, False),
            filler_fn(*filler_args),
        )
    width = state.shape[1]
    total_decay = decay
    total_fwd, total_bwd = (state, state_grad)
    before = jnp.zeros_like(state)
    before_decay = jnp.ones_like(decay)
    after = jnp.zeros_like(state_grad)
    after_decay = jnp.ones_like(decay)
    distance = 1
    while distance < size:
        high = lax.convert_element_type(total_decay.astype(jnp.bfloat16), jnp.float32)
        low = total_decay - high
        pad = jnp.zeros((decay.shape[0], 126), jnp.float32)
        payload = jnp.concatenate(
            [total_fwd, total_bwd, high[:, None], low[:, None], pad], axis=1
        ).astype(jnp.bfloat16)
        upper = (mine // distance) % 2 == 1
        if distance == 1:
            payload, filler_args = lax.optimization_barrier((payload, filler_args))
        if distance * 2 < size:
            got = lax.ppermute(payload, axis, [(i, i ^ distance) for i in range(size)])
            got = got.astype(jnp.float32)
            got_fwd = got[:, :width]
            got_bwd = got[:, width : 2 * width]
        else:
            last = jnp.where(upper, total_bwd, total_fwd).astype(jnp.bfloat16)
            last = jnp.concatenate([last, payload[:, 2 * width :]], axis=1)
            got = lax.ppermute(last, axis, [(i, i ^ distance) for i in range(size)])
            got = got.astype(jnp.float32)
            got_fwd = got[:, :width]
            got_bwd = got_fwd
            got = jnp.concatenate([got[:, :width], got], axis=1)
        if distance == 1:
            got, filler = lax.optimization_barrier((got, filler_fn(*filler_args)))
        got_decay = got[:, 2 * width] + got[:, 2 * width + 1]
        before = jnp.where(upper, before + before_decay[:, None] * got_fwd, before)
        before_decay = jnp.where(upper, before_decay * got_decay, before_decay)
        after = jnp.where(upper, after, after + after_decay[:, None] * got_bwd)
        after_decay = jnp.where(upper, after_decay, after_decay * got_decay)
        if distance * 2 < size:
            total_fwd = jnp.where(
                upper,
                total_fwd + total_decay[:, None] * got_fwd,
                got_fwd + got_decay[:, None] * total_fwd,
            )
            total_bwd = jnp.where(
                upper,
                got_bwd + got_decay[:, None] * total_bwd,
                total_bwd + total_decay[:, None] * got_bwd,
            )
            total_decay = total_decay * got_decay
        distance *= 2
    return (before, after, filler)


def shards(bwd_input, bwd_docs, bwd_grad, proj_weight, step_weight, step_bias, rate_log, skip_gain):
    tokens = bwd_input.shape[1]
    channels_here = bwd_input.shape[2]
    heads_here = step_bias.shape[1]
    head_width = channels_here // heads_here
    bwd_flat = bwd_input[0]
    bwd_values = bwd_flat.reshape(tokens, heads_here, head_width)
    weight_heads = step_weight[0].reshape(heads_here, head_width)
    bias_heads = step_bias[0]
    rate_heads = rate_log[0]
    skip_heads = skip_gain[0]
    docs_bwd = bwd_docs[0]
    doc_before = shifted(docs_bwd[-1:], "seq", 1)[0]
    size, mine = (lax.axis_size("seq"), lax.axis_index("seq"))
    group = lax.axis_index("head")
    own_rows = proj_weight[0]
    slot_weight = jnp.concatenate(
        [own_rows] + [rotated(own_rows, "seq", k) for k in range(1, size)], axis=0
    )
    slot_value = jnp.dot(bwd_flat, slot_weight.T, preferred_element_type=jnp.float32)
    slot_value = slot_value.reshape(tokens, size, -1)[:, ::-1].reshape(tokens, -1)
    partial_value = roll_blocks(slot_value, mine + 1, size, 1)
    group_width = partial_value.shape[1] // 2
    mine_part = lax.dynamic_slice_in_dim(partial_value, group * group_width, group_width, axis=1)
    other_part = lax.dynamic_slice_in_dim(
        partial_value, (1 - group) * group_width, group_width, axis=1
    )
    mixer_bwd = (
        mine_part + swap_heads(other_part.astype(jnp.bfloat16)).astype(jnp.float32)
    ).astype(jnp.bfloat16)
    cotangent = bwd_grad[0].reshape(tokens, heads_here, head_width)

    def summary_bwd(values_in, mixer_in, weight_in, bias_in, rate_in):
        return span_summary(values_in, mixer_in, weight_in, bias_in, rate_in, docs_bwd, doc_before)

    summary_out, summary_pull = jax.vjp(
        summary_bwd, bwd_values, mixer_bwd, weight_heads, bias_heads, rate_heads
    )
    decay_bwd, state_bwd = summary_out
    state_shape = state_bwd.shape
    state_flat = state_bwd.reshape(heads_here, -1)

    out_ct = cotangent.astype(jnp.float32)

    def local_bwd(values_in, mixer_in, weight_in, bias_in, rate_in, skip_in):
        return span_local(values_in, mixer_in, weight_in, bias_in, rate_in, skip_in, docs_bwd)

    def local_pull(*primals):
        return jax.vjp(local_bwd, *primals[:-1])[1](primals[-1])


    def carry_bwd(values_in, mixer_in, weight_in, bias_in, rate_in, state_in):
        return span_carry(
            values_in, mixer_in, weight_in, bias_in, rate_in, docs_bwd, doc_before, state_in
        )

    def carried_only(state_in):
        return carry_bwd(bwd_values, mixer_bwd, weight_heads, bias_heads, rate_heads, state_in)

    state_grad = jax.vjp(carried_only, jnp.zeros(state_shape, jnp.float32))[1](out_ct)[0]
    state_grad = state_grad.reshape(heads_here, -1)
    incoming_flat, adjoint_flat, local_grads = both_scans(
        decay_bwd,
        state_flat,
        state_grad,
        "seq",
        local_pull,
        (bwd_values, mixer_bwd, weight_heads, bias_heads, rate_heads, skip_heads, out_ct),
    )
    incoming_bwd = incoming_flat.reshape(state_shape)
    carry_grads = jax.vjp(
        carry_bwd, bwd_values, mixer_bwd, weight_heads, bias_heads, rate_heads, incoming_bwd
    )[1](out_ct)
    out_grads = (
        (local_grads[0].astype(jnp.float32) + carry_grads[0].astype(jnp.float32)),
        (local_grads[1].astype(jnp.float32) + carry_grads[1].astype(jnp.float32)),
        local_grads[2] + carry_grads[2],
        local_grads[3] + carry_grads[3],
        local_grads[4] + carry_grads[4],
        local_grads[5],
    )
    decay_grad = jnp.sum(adjoint_flat * incoming_flat, axis=1)
    sum_grads = summary_pull((decay_grad, adjoint_flat.reshape(state_shape)))
    mixer_grad = (out_grads[1].astype(jnp.float32) + sum_grads[1].astype(jnp.float32)).astype(
        jnp.bfloat16
    )
    other_grad = swap_heads(mixer_grad)
    mixer_full = jnp.where(
        group == 0,
        jnp.concatenate([mixer_grad, other_grad], axis=1),
        jnp.concatenate([other_grad, mixer_grad], axis=1),
    )
    mixer_slots = roll_blocks(mixer_full, size - 1 - mine, size, 1)
    mixer_slots = mixer_slots.reshape(tokens, size, -1)[:, ::-1].reshape(tokens, -1)
    back_proj = jnp.dot(mixer_slots, slot_weight, preferred_element_type=jnp.float32)
    value_grad = (out_grads[0].astype(jnp.float32) + sum_grads[0].astype(jnp.float32)).reshape(
        tokens, channels_here
    ) + back_proj
    value_grad = value_grad.astype(jnp.bfloat16)
    prev_part = shifted(value_grad.reshape(1, tokens, channels_here), "section", -1)
    dest_grad = roll_blocks(mixer_full, size - mine, size, 1)
    row_parts = lax.dot_general(
        dest_grad, bwd_flat, (((0,), (0,)), ((), ())), preferred_element_type=jnp.float32
    ).reshape(size, -1, channels_here)
    small = jnp.concatenate(
        [
            (out_grads[2] + sum_grads[2]).reshape(channels_here),
            out_grads[3] + sum_grads[3],
            out_grads[4] + sum_grads[4],
            out_grads[5],
        ]
    )
    count = small.shape[0]
    block_rows = row_parts.shape[1]
    small_high = small.astype(jnp.bfloat16)
    small_low = (small - small_high.astype(jnp.float32)).astype(jnp.bfloat16)
    small_cols = -(-(2 * count) // (block_rows * 128)) * 128
    small_coded = jnp.concatenate([small_high, small_low])
    small_coded = jnp.pad(small_coded, (0, block_rows * small_cols - 2 * count))
    small_coded = small_coded.reshape(block_rows, small_cols)
    grad_rows = row_parts[0]
    small_slots = [small_coded]
    messages = jnp.concatenate(
        [
            row_parts.astype(jnp.bfloat16),
            jnp.broadcast_to(small_coded[None], (size,) + small_coded.shape),
        ],
        axis=2,
    )
    for k in range(1, size):
        got = rotated(messages[k], "seq", k)
        grad_rows = grad_rows + got[:, :channels_here].astype(jnp.float32)
        small_slots.append(got[:, channels_here:])
    small_slots = jnp.stack(small_slots[::-1])
    small_slots = roll_blocks(small_slots, mine + 1, size, 0).astype(jnp.float32)
    small_slots = small_slots.reshape(size, -1)
    small_parts = small_slots[:, :count] + small_slots[:, count : 2 * count]
    small_total = small_parts[0]
    for j in range(1, size):
        small_total = small_total + small_parts[j]
    small = small_total.reshape(-1)
    totals = (
        small[:channels_here],
        small[channels_here : channels_here + heads_here],
        small[channels_here + heads_here : channels_here + 2 * heads_here],
        small[channels_here + 2 * heads_here : channels_here + 3 * heads_here],
    )
    return (
        prev_part,
        grad_rows[None],
        totals[0][None],
        totals[1][None],
        totals[2][None],
        totals[3][None],
    )


def solution(mesh):
    in_specs = (
        P("section", "seq", "head"),
        P("section", "seq"),
        P("section", "seq", "head"),
        P("section", "seq", "head"),
        P("section", "head"),
        P("section", "head"),
        P("section", "head"),
        P("section", "head"),
    )
    out_specs = (
        P("section", "seq", "head"),
        P("section", "seq", "head"),
        P("section", "head"),
        P("section", "head"),
        P("section", "head"),
        P("section", "head"),
    )
    return jax.shard_map(shards, mesh=mesh, in_specs=in_specs, out_specs=out_specs, check_vma=False)
```
